32 devices in a mesh: groups: 2 (over y), tm: 16 (over z, x, core).
Axes of the slice: x: 2, y: 2, z: 4, core: 2. Of those that a mesh axis runs over, the one named last changes fastest.
Arguments:
- ref_traj: float32 [8, 1024, 256], P('groups', 'tm'), parts along dimension 0, may hold values from -6 to 6
- cost_weights: float32 [8, 1024, 256], P('groups', 'tm'), parts along dimension 0, may hold values from 0.1 to 10
- x_init: float32 [8, 256], P('groups'), parts along dimension 0, may hold values from -6 to 6
- decay: float32 [256], replicated, as said below
- coupling: float32 [3, 64, 64], replicated, may hold values from -0.00018310547 to 0.00018310547
- links: int32 [3, 2], replicated, may hold values from 0 to 3, as said below
- input_map: float32 [256, 64], replicated, may hold values from -0.0007324219 to 0.0007324219
- ff_gain: float32 [64, 256], replicated, may hold values from -0.01171875 to 0.01171875
- lengths: int32 [8, 4], P('groups'), parts along dimension 0, may hold values from 1 to 512, 1024 in all within a row
Outputs:
- states: float32 [8, 1024, 256], P('groups', 'tm'), parts along dimension 0
- weight_grad: float32 [8, 1024, 256], P('groups', 'tm'), parts along dimension 0
- cost: float32 [8], P('groups'), parts along dimension 0
The draws below stay inside these ranges and needn't reach their ends.
There are 2 independent parts, one for each index of `groups`. The reference program is written for one: setup_inputs(seed, part) draws one part's arguments, and reference() takes and returns one part's arrays. A program takes and returns all parts, laid end to end along the dimension named above; an argument that names none is the same for every part. Nothing has to cross between parts.
Inputs may be any that keep to these rules, and one draw needn't show every extreme that they name: `links`: each pair names two different blocks, the row before the column, and no pair twice. The lengths of a scenario sum to 1024, and the longest is exactly 512. `decay`: every entry lies strictly between 0 and 1.
All inputs are finite; a program needn't handle non-finite values.
Results may differ from the reference program's by a relative error of at most 0.0003.
Values sent between devices are 32-bit elements; how exact they have to be, the bound alone decides.
No kernel may reach another device: no remote copies, remote signals or barrier semaphores. Data moves between devices by JAX's collectives and lax.ppermute only.
A program may use at most 64 MiB of HBM per device.

```python
import math
import jax
import jax.numpy as jnp
import numpy as np
from jax import lax

NS = 256
NC = 64
BW = 64
LINKS = 3
EPIS = 4
S = 4
TSTEPS = 1024


def draw_decay(key, part):
    key_slow, key_fast, key_pick = jax.random.split(key, 3)
    slow_rate = jnp.exp(jax.random.uniform(key_slow, (NS,), jnp.float32, jnp.log(0.5 / TSTEPS), jnp.log(2.3 / TSTEPS)))
    fast_rate = jnp.exp(jax.random.uniform(key_fast, (NS,), jnp.float32, jnp.log(1.0 / 50.0), jnp.log(1.0 / 30.0)))
    portion = 0.5
    chosen = jax.random.bernoulli(key_pick, portion, (NS,))
    return jnp.exp(-jnp.where(chosen, slow_rate, fast_rate)).astype(jnp.float32)


def draw_links(key, part):
    blocks = NS // BW
    cells = jnp.arange(blocks * blocks, dtype=jnp.int32)
    upper_row = cells // blocks
    upper_col = cells % blocks
    ranking = jax.random.permutation(key, blocks * blocks).astype(jnp.int32)
    scores = jnp.where(upper_row < upper_col, ranking, ranking + blocks * blocks)
    picked = jnp.argsort(scores)[:LINKS]
    return jnp.stack([upper_row[picked], upper_col[picked]], axis=1).astype(jnp.int32)


def block_scale(key, extent, pieces, least, largest):
    def one(dim, blocks):
        draws = jax.random.uniform(jax.random.fold_in(jax.random.fold_in(key, 6), dim), (blocks,), jnp.float32, least / len(pieces), largest / len(pieces))
        return jnp.repeat(jnp.exp(draws), extent[dim] // blocks).reshape((-1,) + (1,) * (len(extent) - dim - 1))

    gain = one(*pieces[0])
    for cut in pieces[1:]:
        gain = gain * one(*cut)
    return gain


def profile(count, total, bound, slope):
    portions = [(1 << 20) // math.isqrt(standing ** slope) + 1 for standing in range(2, count + 1)]
    spare, given = total - bound - (count - 1), [1] * (count - 1)
    while spare > 0:
        movable = [i for i in range(count - 1) if given[i] < bound]
        pool, budget = sum([portions[i] for i in movable]), spare
        for i in movable:
            extra = min(bound - given[i], max(1, budget * portions[i] // pool), spare)
            given[i] = given[i] + extra
            spare = spare - extra
    return np.array([bound] + given)


def ragged_sizes(rng, count, total, most, lean):
    if count == 2:
        one = jax.random.randint(rng, (), max(1, total - most), min(most, total - 1) + 1)
        return jnp.stack([one, total - one])
    sizes = jnp.asarray(profile(count, total, most, lean), jnp.int32)
    twos = (count - 1) // 2
    donor, taker = sizes[1:1 + 2 * twos:2], sizes[2:2 + 2 * twos:2]
    slack = jnp.minimum(donor - 1, most - taker)
    passed = jax.random.randint(jax.random.fold_in(rng, 1), (twos,), 0, 1 << 20) % (slack + 1)
    sizes = sizes.at[1:1 + 2 * twos:2].set(donor - passed).at[2:2 + 2 * twos:2].set(taker + passed)
    return sizes[jax.random.permutation(jax.random.fold_in(rng, 2), count)]


def centred(key, dims, spread, reach, cuts=(), kind=jnp.bfloat16):
    result = jax.random.normal(key, dims, jnp.float32) * spread
    if len(cuts) > 0:
        result = block_scale(key, dims, cuts, -0.22, 0.18) * result
    return jnp.clip(result, min=-reach, max=reach).astype(kind)


def setup_inputs(seed: int = 0, part: int = 0) -> dict:
    splits = jax.random.split(jax.random.key(seed), 10)
    part_splits = jax.random.split(jax.random.fold_in(splits[9], part), 10)
    return {
        "ref_traj": centred(part_splits[0], (S, TSTEPS, NS), 1.0, 6.0, ((1, 16),), jnp.float32),
        "cost_weights": jnp.clip(jnp.exp(math.log(10.0) - 4.6051702 * jax.random.uniform(part_splits[1], (S, TSTEPS, NS), jnp.float32) ** block_scale(part_splits[1], (S, TSTEPS, NS), ((1, 16),), -0.2, 0.2)), 0.1, 10.0),
        "x_init": centred(part_splits[2], (S, NS), 1.0, 6.0, (), jnp.float32),
        "decay": draw_decay(jax.random.fold_in(splits[9], 71), part),
        "coupling": centred(splits[4], (LINKS, BW, BW), (1024 * TSTEPS * TSTEPS) ** -0.5, 0.00018310547, (), jnp.float32),
        "links": draw_links(jax.random.fold_in(splits[9], 71), part),
        "input_map": centred(splits[6], (NS, NC), (NC * TSTEPS * TSTEPS) ** -0.5, 0.0007324219, (), jnp.float32),
        "ff_gain": centred(splits[7], (NC, NS), (NS * TSTEPS) ** -0.5, 0.01171875, (), jnp.float32),
        "lengths": jax.vmap(lambda own: ragged_sizes(own, EPIS, TSTEPS, TSTEPS // 2, 0))(jax.random.split(part_splits[8], S)).reshape((S, EPIS)).astype(jnp.int32),
    }


def build_dynamics(decay, coupling, links):
    size = decay.shape[0]
    width = coupling.shape[1]
    lanes = jnp.arange(size, dtype=jnp.int32)
    offsets = jnp.arange(width, dtype=jnp.int32)
    row_hot = (lanes[None, :, None] == (links[:, 0:1, None] * width + offsets[None, None, :])).astype(jnp.float32)
    col_hot = (lanes[None, :, None] == (links[:, 1:2, None] * width + offsets[None, None, :])).astype(jnp.float32)
    placed = jnp.einsum("lia,lab,ljb->ij", row_hot, coupling, col_hot, precision=lax.Precision.HIGHEST)
    return jnp.diag(decay) + placed


def run_chain(inputs, keeping, matrix, backward):
    def advance(carry, packed):
        driven, kept = packed
        nxt = kept[:, None] * jnp.dot(carry, matrix, precision=lax.Precision.HIGHEST) + driven
        return nxt, nxt

    start_value = jnp.zeros((inputs.shape[0], inputs.shape[2]), jnp.float32)
    finals, trail = lax.scan(advance, start_value, (jnp.swapaxes(inputs, 0, 1), jnp.swapaxes(keeping, 0, 1)), reverse=backward)
    return jnp.swapaxes(trail, 0, 1)


def reference(ref_traj, cost_weights, x_init, decay, coupling, links, input_map, ff_gain, lengths):
    dynamics = build_dynamics(decay, coupling, links)
    total = ref_traj.shape[1]
    ends_incl = jnp.cumsum(lengths, axis=1).astype(jnp.int32)
    starts = (ends_incl - lengths).astype(jnp.int32)
    steps_all = jnp.arange(total, dtype=jnp.int32)
    start_flag = jnp.any(steps_all[None, :, None] == starts[:, None, :], axis=-1).astype(jnp.float32)
    end_flag = jnp.any((steps_all[None, :, None] + 1) == ends_incl[:, None, :], axis=-1).astype(jnp.float32)
    high = lax.Precision.HIGHEST
    value_term = run_chain(cost_weights * ref_traj, 1.0 - end_flag, dynamics, True)
    controls = jnp.einsum("stn,cn->stc", value_term, ff_gain, precision=high)
    forcing = -jnp.einsum("stc,nc->stn", controls, input_map, precision=high)
    init_image = jnp.dot(x_init, dynamics.T, precision=high)
    driven = forcing + start_flag[:, :, None] * init_image[:, None, :]
    states = run_chain(driven, 1.0 - start_flag, dynamics.T, False)
    offset = states - ref_traj
    cost = jnp.sum(cost_weights * offset * offset, axis=(1, 2)) * (0.5 / total)
    adjoint = run_chain(cost_weights * offset, 1.0 - end_flag, dynamics, True)
    pulled = jnp.einsum("stn,nc->stc", adjoint, input_map, precision=high)
    source = -jnp.einsum("stc,cn->stn", pulled, ff_gain, precision=high)
    value_adjoint = run_chain(source, 1.0 - start_flag, dynamics.T, False)
    weight_grad = 0.5 * offset * offset + ref_traj * value_adjoint
    return (states, weight_grad, cost)
```

```python
import jax
import jax.numpy as jnp
from jax import lax
from jax.sharding import PartitionSpec as P


def build_dynamics(decay, coupling, links):
    size = decay.shape[0]
    width = coupling.shape[1]
    lanes = jnp.arange(size, dtype=jnp.int32)
    offsets = jnp.arange(width, dtype=jnp.int32)
    row_hot = (lanes[None, :, None] == links[:, 0:1, None] * width + offsets[None, None, :]).astype(
        jnp.float32
    )
    col_hot = (lanes[None, :, None] == links[:, 1:2, None] * width + offsets[None, None, :]).astype(
        jnp.float32
    )
    placed = jnp.einsum(
        "lia,lab,ljb->ij", row_hot, coupling, col_hot, precision=lax.Precision.HIGHEST
    )
    return jnp.diag(decay) + placed


def row_times(values, matrix):
    width = values.shape[-1]
    flat = jnp.dot(values.reshape(-1, width), matrix, precision=lax.Precision.HIGHEST)
    return flat.reshape(values.shape)


def run_chain(inputs, frame_starts, powers, backward, local_levels, device_levels, extra=None):
    scen_count, seg_steps, width = inputs.shape
    devices = lax.axis_size("tm")
    device = lax.axis_index("tm")
    if backward:
        driven = inputs[:, ::-1]
        frame_device = devices - 1 - device
    else:
        driven = inputs
        frame_device = device
    positions = frame_device * seg_steps + jnp.arange(seg_steps, dtype=jnp.int32)
    cut_here = jnp.any(positions[None, :, None] == frame_starts[:, None, :], axis=-1)
    values = driven
    flags = 1.0 - cut_here.astype(jnp.float32)
    for level in range(local_levels):
        stride = 2**level
        prior_values = jnp.pad(values[:, : seg_steps - stride], ((0, 0), (stride, 0), (0, 0)))
        prior_flags = jnp.pad(
            flags[:, : seg_steps - stride], ((0, 0), (stride, 0)), constant_values=1.0
        )
        values = values + flags[:, :, None] * row_times(prior_values, powers[level])
        flags = flags * prior_flags
    last_value = values[:, -1]
    if extra is None:
        all_values = lax.all_gather(last_value[None], "tm", axis=0, tiled=True)
        gathered_extra = None
    else:
        lanes = jnp.broadcast_to(extra[:, None], (scen_count, 128))
        packed = jnp.concatenate([last_value, lanes], axis=1)
        gathered = lax.all_gather(packed[None], "tm", axis=0, tiled=True)
        all_values = gathered[:, :, :width]
        gathered_extra = gathered[:, :, width]
    seg_lo = jnp.arange(devices, dtype=jnp.int32)[:, None, None] * seg_steps
    inside = (frame_starts[None] >= seg_lo) & (frame_starts[None] < seg_lo + seg_steps)
    all_flags = 1.0 - jnp.any(inside, axis=-1).astype(jnp.float32)
    if backward:
        all_values = all_values[::-1]
    roll_by = devices - frame_device
    all_values = jnp.roll(all_values, roll_by, axis=0)
    all_flags = jnp.roll(all_flags, roll_by, axis=0)
    keep = (jnp.arange(devices, dtype=jnp.int32) >= roll_by).astype(jnp.float32)
    all_values = all_values * keep[:, None, None]
    all_flags = all_flags * keep[:, None] + (1.0 - keep[:, None])
    for level in range(device_levels):
        half = all_values.shape[0] // 2
        paired_values = all_values.reshape(half, 2, scen_count, width)
        paired_flags = all_flags.reshape(half, 2, scen_count)
        moved = row_times(paired_values[:, 0], powers[local_levels + level])
        all_values = paired_flags[:, 1, :, None] * moved + paired_values[:, 1]
        all_flags = paired_flags[:, 0] * paired_flags[:, 1]
    entering = all_values[0]
    table = row_times(entering[:, None, :], powers[0])
    for level in range(local_levels):
        table = jnp.concatenate([table, row_times(table, powers[level])], axis=1)
    result = values + flags[:, :, None] * table
    if backward:
        result = result[:, ::-1]
    if extra is None:
        return result
    return result, gathered_extra


def per_device(ref_traj, cost_weights, x_init, decay, coupling, links, input_map, ff_gain, lengths):
    scen_count, seg_steps, width = ref_traj.shape
    devices = lax.axis_size("tm")
    device = lax.axis_index("tm")
    total = seg_steps * devices
    high = lax.Precision.HIGHEST
    dynamics = build_dynamics(decay, coupling, links)
    local_levels = seg_steps.bit_length() - 1
    device_levels = (devices - 1).bit_length()
    power_count = local_levels + max(device_levels, 1)
    squares = [dynamics]
    for level in range(power_count - 1):
        squares.append(jnp.dot(squares[-1], squares[-1], precision=high))
    forward_powers = [matrix.T for matrix in squares]
    ends_incl = jnp.cumsum(lengths, axis=1)
    starts = ends_incl - lengths
    mirrored = total - ends_incl
    value_term = run_chain(
        cost_weights * ref_traj, mirrored, squares, True, local_levels, device_levels
    )
    controls = jnp.einsum("stn,cn->stc", value_term, ff_gain, precision=high)
    forcing = -jnp.einsum("stc,nc->stn", controls, input_map, precision=high)
    positions = device * seg_steps + jnp.arange(seg_steps, dtype=jnp.int32)
    start_flag = jnp.any(positions[None, :, None] == starts[:, None, :], axis=-1).astype(
        jnp.float32
    )
    init_image = jnp.dot(x_init, dynamics.T, precision=high)
    driven = forcing + start_flag[:, :, None] * init_image[:, None, :]
    states = run_chain(driven, starts, forward_powers, False, local_levels, device_levels)
    offset = states - ref_traj
    local_cost = jnp.sum(cost_weights * offset * offset, axis=(1, 2)) * (0.5 / total)
    adjoint, all_costs = run_chain(
        cost_weights * offset, mirrored, squares, True, local_levels, device_levels, local_cost
    )
    cost = jnp.sum(all_costs, axis=0)
    pulled = jnp.einsum("stn,nc->stc", adjoint, input_map, precision=high)
    source = -jnp.einsum("stc,cn->stn", pulled, ff_gain, precision=high)
    value_adjoint = run_chain(source, starts, forward_powers, False, local_levels, device_levels)
    weight_grad = 0.5 * offset * offset + ref_traj * value_adjoint
    return (states, weight_grad, cost)


def solution(mesh):
    placed = (
        P("groups", "tm", None),
        P("groups", "tm", None),
        P("groups", None),
        P(),
        P(),
        P(),
        P(),
        P(),
        P("groups", None),
    )
    return jax.shard_map(
        per_device,
        mesh=mesh,
        in_specs=placed,
        out_specs=(P("groups", "tm", None), P("groups", "tm", None), P("groups")),
        check_vma=False,
    )
```

```python
import functools

import jax
import jax.numpy as jnp
from jax import lax
from jax.experimental import pallas as pl
from jax.experimental.pallas import tpu as pltpu
from jax.sharding import PartitionSpec as P

HIGH = lax.Precision.HIGHEST


def build_dynamics(decay, coupling, links):
    size = decay.shape[0]
    width = coupling.shape[1]
    lanes = jnp.arange(size, dtype=jnp.int32)
    offsets = jnp.arange(width, dtype=jnp.int32)
    row_hot = (lanes[None, :, None] == links[:, 0:1, None] * width + offsets[None, None, :]).astype(
        jnp.float32
    )
    col_hot = (lanes[None, :, None] == links[:, 1:2, None] * width + offsets[None, None, :]).astype(
        jnp.float32
    )
    placed = jnp.einsum(
        "lia,lab,ljb->ij", row_hot, coupling, col_hot, precision=lax.Precision.HIGHEST
    )
    return jnp.diag(decay) + placed


def row_times(values, matrix):
    width = values.shape[-1]
    flat = jnp.dot(values.reshape(-1, width), matrix, precision=lax.Precision.HIGHEST)
    return flat.reshape(values.shape)


def _dot(a, b):
    return jnp.dot(a, b, precision=HIGH, preferred_element_type=jnp.float32)


def _scan(v, cut, pw_ref, seg, backward, carry=None):
    rows, width = v.shape
    scen = rows // seg
    t = lax.broadcasted_iota(jnp.int32, (rows, width), 0) % seg
    flags = 1.0 - cut
    if carry is not None:
        pushed = _dot(carry, pw_ref[0])
        pushed = jnp.broadcast_to(pushed[:, None, :], (scen, seg, width)).reshape(rows, width)
        first = t == (seg - 1 if backward else 0)
        v = v + jnp.where(first, flags * pushed, 0.0)
    levels = pw_ref.shape[0]
    for level in range(levels):
        stride = 2**level
        if backward:
            prior_v = pltpu.roll(v, rows - stride, 0)
            prior_f = pltpu.roll(flags, rows - stride, 0)
            valid = t < seg - stride
        else:
            prior_v = pltpu.roll(v, stride, 0)
            prior_f = pltpu.roll(flags, stride, 0)
            valid = t >= stride
        prior_v = jnp.where(valid, prior_v, 0.0)
        prior_f = jnp.where(valid, prior_f, 1.0)
        v = v + flags * _dot(prior_v, pw_ref[level])
        flags = flags * prior_f
    return v


def _ends(v, seg, backward):
    rows, width = v.shape
    scen = rows // seg
    pick = lax.broadcasted_iota(jnp.int32, (scen, rows), 1)
    want = lax.broadcasted_iota(jnp.int32, (scen, rows), 0) * seg + (0 if backward else seg - 1)
    sel = (pick == want).astype(jnp.float32)
    return _dot(sel, v)


def _vmem(count):
    return [pl.BlockSpec(memory_space=pltpu.VMEM)] * count


def _call(kernel, outs, *args):
    return pl.pallas_call(
        kernel,
        out_shape=outs,
        in_specs=_vmem(len(args)),
        out_specs=tuple(_vmem(len(outs))),
    )(*args)


def k_first(seg, cw_ref, ref_ref, end_ref, pwb_ref, w1_ref, e1_ref):
    width = cw_ref.shape[1]
    cut = jnp.broadcast_to(end_ref[...], cw_ref.shape)
    w1 = cw_ref[...] * ref_ref[...]
    w1_ref[...] = w1
    e1_ref[...] = _ends(_scan(w1, cut, pwb_ref, seg, True), seg, True)


def k_states_in(seg, w1_ref, end_ref, start_ref, c1_ref, init_ref, gain_ref, imap_ref, pwb_ref,
                pwf_ref, d2_ref, e2_ref):
    shape = w1_ref.shape
    cut_e = jnp.broadcast_to(end_ref[...], shape)
    cut_s = jnp.broadcast_to(start_ref[...], shape)
    vt = _scan(w1_ref[...], cut_e, pwb_ref, seg, True, c1_ref[...])
    controls = lax.dot_general(
        vt, gain_ref[...], (((1,), (1,)), ((), ())), precision=HIGH,
        preferred_element_type=jnp.float32)
    forcing = -lax.dot_general(
        controls, imap_ref[...], (((1,), (1,)), ((), ())), precision=HIGH,
        preferred_element_type=jnp.float32)
    rows, width = shape
    scen = rows // seg
    init = jnp.broadcast_to(init_ref[...][:, None, :], (scen, seg, width)).reshape(rows, width)
    d2 = forcing + cut_s * init
    d2_ref[...] = d2
    e2_ref[...] = _ends(_scan(d2, cut_s, pwf_ref, seg, False), seg, False)


def k_adjoint_in(seg, scale, d2_ref, start_ref, end_ref, c2_ref, cw_ref, ref_ref, pwf_ref, pwb_ref,
                 x_ref, w3_ref, e3_ref, cost_ref):
    shape = d2_ref.shape
    rows, width = shape
    scen = rows // seg
    cut_s = jnp.broadcast_to(start_ref[...], shape)
    cut_e = jnp.broadcast_to(end_ref[...], shape)
    states = _scan(d2_ref[...], cut_s, pwf_ref, seg, False, c2_ref[...])
    x_ref[...] = states
    offset = states - ref_ref[...]
    cw = cw_ref[...]
    w3 = cw * offset
    w3_ref[...] = w3
    per_row = jnp.sum(w3 * offset, axis=1, keepdims=True)
    pick = lax.broadcasted_iota(jnp.int32, (scen, rows), 1) // seg
    want = lax.broadcasted_iota(jnp.int32, (scen, rows), 0)
    sel = (pick == want).astype(jnp.float32)
    per_scen = _dot(sel, jnp.broadcast_to(per_row, (rows, 128)))
    cost_ref[...] = per_scen * scale
    e3_ref[...] = _ends(_scan(w3, cut_e, pwb_ref, seg, True), seg, True)


def k_value_adjoint_in(seg, w3_ref, end_ref, start_ref, c3_ref, imap_ref, gain_ref, pwb_ref,
                       pwf_ref, s4_ref, e4_ref):
    shape = w3_ref.shape
    cut_e = jnp.broadcast_to(end_ref[...], shape)
    cut_s = jnp.broadcast_to(start_ref[...], shape)
    adjoint = _scan(w3_ref[...], cut_e, pwb_ref, seg, True, c3_ref[...])
    pulled = _dot(adjoint, imap_ref[...])
    source = -_dot(pulled, gain_ref[...])
    s4_ref[...] = source
    e4_ref[...] = _ends(_scan(source, cut_s, pwf_ref, seg, False), seg, False)


def k_last(seg, s4_ref, start_ref, c4_ref, x_ref, ref_ref, pwf_ref, g_ref):
    shape = s4_ref.shape
    cut_s = jnp.broadcast_to(start_ref[...], shape)
    va = _scan(s4_ref[...], cut_s, pwf_ref, seg, False, c4_ref[...])
    ref = ref_ref[...]
    offset = x_ref[...] - ref
    g_ref[...] = 0.5 * offset * offset + ref * va


def combine(last_value, frame_starts, powers, backward, seg_steps, local_levels, device_levels,
            extra=None):
    scen_count, width = last_value.shape
    devices = lax.axis_size("tm")
    device = lax.axis_index("tm")
    frame_device = devices - 1 - device if backward else device
    if extra is None:
        all_values = lax.all_gather(last_value[None], "tm", axis=0, tiled=True)
        gathered_extra = None
    else:
        lanes = jnp.broadcast_to(extra[:, None], (scen_count, 128))
        packed = jnp.concatenate([last_value, lanes], axis=1)
        gathered = lax.all_gather(packed[None], "tm", axis=0, tiled=True)
        all_values = gathered[:, :, :width]
        gathered_extra = gathered[:, :, width]
    seg_lo = jnp.arange(devices, dtype=jnp.int32)[:, None, None] * seg_steps
    inside = (frame_starts[None] >= seg_lo) & (frame_starts[None] < seg_lo + seg_steps)
    all_flags = 1.0 - jnp.any(inside, axis=-1).astype(jnp.float32)
    if backward:
        all_values = all_values[::-1]
    roll_by = devices - frame_device
    all_values = jnp.roll(all_values, roll_by, axis=0)
    all_flags = jnp.roll(all_flags, roll_by, axis=0)
    keep = (jnp.arange(devices, dtype=jnp.int32) >= roll_by).astype(jnp.float32)
    all_values = all_values * keep[:, None, None]
    all_flags = all_flags * keep[:, None] + (1.0 - keep[:, None])
    for level in range(device_levels):
        half = all_values.shape[0] // 2
        paired_values = all_values.reshape(half, 2, scen_count, width)
        paired_flags = all_flags.reshape(half, 2, scen_count)
        moved = row_times(paired_values[:, 0], powers[local_levels + level])
        all_values = paired_flags[:, 1, :, None] * moved + paired_values[:, 1]
        all_flags = paired_flags[:, 0] * paired_flags[:, 1]
    return all_values[0], gathered_extra


def per_device(ref_traj, cost_weights, x_init, decay, coupling, links, input_map, ff_gain, lengths):
    scen_count, seg_steps, width = ref_traj.shape
    rows = scen_count * seg_steps
    devices = lax.axis_size("tm")
    device = lax.axis_index("tm")
    total = seg_steps * devices
    dynamics = build_dynamics(decay, coupling, links)
    local_levels = seg_steps.bit_length() - 1
    device_levels = (devices - 1).bit_length()
    power_count = local_levels + max(device_levels, 1)
    squares = [dynamics]
    for level in range(power_count - 1):
        squares.append(jnp.dot(squares[-1], squares[-1], precision=HIGH))
    forward_powers = [matrix.T for matrix in squares]
    pwb = jnp.stack(squares[:local_levels])
    pwf = jnp.stack(forward_powers[:local_levels])
    ends_incl = jnp.cumsum(lengths, axis=1)
    starts = ends_incl - lengths
    mirrored = total - ends_incl
    positions = device * seg_steps + jnp.arange(seg_steps, dtype=jnp.int32)
    start_flag = jnp.any(positions[None, :, None] == starts[:, None, :], axis=-1)
    end_flag = jnp.any(positions[None, :, None] + 1 == ends_incl[:, None, :], axis=-1)
    start_col = start_flag.astype(jnp.float32).reshape(rows, 1)
    end_col = end_flag.astype(jnp.float32).reshape(rows, 1)
    init_image = jnp.dot(x_init, dynamics.T, precision=HIGH)
    cw = cost_weights.reshape(rows, width)
    ref = ref_traj.reshape(rows, width)
    f32 = jnp.float32
    full = jax.ShapeDtypeStruct((rows, width), f32)
    ends = jax.ShapeDtypeStruct((scen_count, width), f32)
    seg = seg_steps

    w1, e1 = _call(functools.partial(k_first, seg), (full, ends), cw, ref, end_col, pwb)
    c1, _ = combine(e1, mirrored, squares, True, seg, local_levels, device_levels)
    d2, e2 = _call(
        functools.partial(k_states_in, seg), (full, ends),
        w1, end_col, start_col, c1, init_image, ff_gain, input_map, pwb, pwf)
    c2, _ = combine(e2, starts, forward_powers, False, seg, local_levels, device_levels)
    cost_shape = jax.ShapeDtypeStruct((scen_count, 128), f32)
    states, w3, e3, cost_part = _call(
        functools.partial(k_adjoint_in, seg, 0.5 / total), (full, full, ends, cost_shape),
        d2, start_col, end_col, c2, cw, ref, pwf, pwb)
    c3, all_costs = combine(
        e3, mirrored, squares, True, seg, local_levels, device_levels, cost_part[:, 0])
    cost = jnp.sum(all_costs, axis=0)
    s4, e4 = _call(
        functools.partial(k_value_adjoint_in, seg), (full, ends),
        w3, end_col, start_col, c3, input_map, ff_gain, pwb, pwf)
    c4, _ = combine(e4, starts, forward_powers, False, seg, local_levels, device_levels)
    (grad,) = _call(
        functools.partial(k_last, seg), (full,), s4, start_col, c4, states, ref, pwf)
    shape3 = (scen_count, seg_steps, width)
    return (states.reshape(shape3), grad.reshape(shape3), cost)


def solution(mesh):
    placed = (
        P("groups", "tm", None),
        P("groups", "tm", None),
        P("groups", None),
        P(),
        P(),
        P(),
        P(),
        P(),
        P("groups", None),
    )
    return jax.shard_map(
        per_device,
        mesh=mesh,
        in_specs=placed,
        out_specs=(P("groups", "tm", None), P("groups", "tm", None), P("groups")),
        check_vma=False,
    )
```

```python
import functools

import jax
import jax.numpy as jnp
from jax import lax
from jax.experimental import pallas as pl
from jax.experimental.pallas import tpu as pltpu
from jax.sharding import PartitionSpec as P

HIGH = lax.Precision.HIGHEST


def build_dynamics(decay, coupling, links):
    size = decay.shape[0]
    width = coupling.shape[1]
    lanes = jnp.arange(size, dtype=jnp.int32)
    offsets = jnp.arange(width, dtype=jnp.int32)
    row_hot = (lanes[None, :, None] == links[:, 0:1, None] * width + offsets[None, None, :]).astype(
        jnp.float32
    )
    col_hot = (lanes[None, :, None] == links[:, 1:2, None] * width + offsets[None, None, :]).astype(
        jnp.float32
    )
    placed = jnp.einsum(
        "lia,lab,ljb->ij", row_hot, coupling, col_hot, precision=lax.Precision.HIGHEST
    )
    return jnp.diag(decay) + placed


def row_times(values, matrix):
    width = values.shape[-1]
    flat = jnp.dot(values.reshape(-1, width), matrix, precision=lax.Precision.HIGHEST)
    return flat.reshape(values.shape)


def _dot(a, b):
    return jnp.dot(a, b, precision=HIGH, preferred_element_type=jnp.float32)


def _dot_nt(a, b):
    return lax.dot_general(
        a, b, (((1,), (1,)), ((), ())), precision=HIGH, preferred_element_type=jnp.float32)


def k_powers(f_ref, out_ref):
    power = f_ref[...]
    out_ref[0] = power
    for level in range(1, out_ref.shape[0]):
        power = _dot(power, power)
        out_ref[level] = power


def _scan(v, cut, pw_ref, seg, backward, carry=None, levels=None):
    rows, width = v.shape
    scen = rows // seg
    t = lax.broadcasted_iota(jnp.int32, (rows, width), 0) % seg
    flags = 1.0 - cut
    if levels is None:
        levels = seg.bit_length() - 1
    step = _dot if backward else _dot_nt
    if carry is not None:
        pushed = step(carry, pw_ref[0])
        pushed = jnp.broadcast_to(pushed[:, None, :], (scen, seg, width)).reshape(rows, width)
        first = t == (seg - 1 if backward else 0)
        v = v + jnp.where(first, flags * pushed, 0.0)
    for level in range(levels):
        stride = 2**level
        if backward:
            prior_v = pltpu.roll(v, rows - stride, 0)
            prior_f = pltpu.roll(flags, rows - stride, 0)
            valid = t < seg - stride
        else:
            prior_v = pltpu.roll(v, stride, 0)
            prior_f = pltpu.roll(flags, stride, 0)
            valid = t >= stride
        prior_v = jnp.where(valid, prior_v, 0.0)
        prior_f = jnp.where(valid, prior_f, 1.0)
        v = v + flags * step(prior_v, pw_ref[level])
        flags = flags * prior_f
    return v


def _ends(v, seg, backward):
    rows, width = v.shape
    scen = rows // seg
    pick = lax.broadcasted_iota(jnp.int32, (scen, rows), 1)
    want = lax.broadcasted_iota(jnp.int32, (scen, rows), 0) * seg + (0 if backward else seg - 1)
    sel = (pick == want).astype(jnp.float32)
    return _dot(sel, v)


def _vmem(count):
    return [pl.BlockSpec(memory_space=pltpu.VMEM)] * count


def _call(kernel, outs, *args):
    return pl.pallas_call(
        kernel,
        out_shape=outs,
        in_specs=_vmem(len(args)),
        out_specs=tuple(_vmem(len(outs))),
    )(*args)


def k_first(seg, cw_ref, ref_ref, end_ref, pwb_ref, w1_ref, e1_ref):
    width = cw_ref.shape[1]
    cut = jnp.broadcast_to(end_ref[...], cw_ref.shape)
    w1 = cw_ref[...] * ref_ref[...]
    w1_ref[...] = w1
    e1_ref[...] = _ends(_scan(w1, cut, pwb_ref, seg, True), seg, True)


def k_states_in(seg, w1_ref, end_ref, start_ref, c1_ref, init_ref, gain_ref, imap_ref, pwb_ref,
                pwf_ref, d2_ref, e2_ref):
    shape = w1_ref.shape
    cut_e = jnp.broadcast_to(end_ref[...], shape)
    cut_s = jnp.broadcast_to(start_ref[...], shape)
    vt = _scan(w1_ref[...], cut_e, pwb_ref, seg, True, c1_ref[...])
    controls = lax.dot_general(
        vt, gain_ref[...], (((1,), (1,)), ((), ())), precision=HIGH,
        preferred_element_type=jnp.float32)
    forcing = -lax.dot_general(
        controls, imap_ref[...], (((1,), (1,)), ((), ())), precision=HIGH,
        preferred_element_type=jnp.float32)
    rows, width = shape
    scen = rows // seg
    init = jnp.broadcast_to(init_ref[...][:, None, :], (scen, seg, width)).reshape(rows, width)
    d2 = forcing + cut_s * init
    d2_ref[...] = d2
    e2_ref[...] = _ends(_scan(d2, cut_s, pwf_ref, seg, False), seg, False)


def k_adjoint_in(seg, scale, d2_ref, start_ref, end_ref, c2_ref, cw_ref, ref_ref, pwf_ref, pwb_ref,
                 x_ref, w3_ref, e3_ref, cost_ref):
    shape = d2_ref.shape
    rows, width = shape
    scen = rows // seg
    cut_s = jnp.broadcast_to(start_ref[...], shape)
    cut_e = jnp.broadcast_to(end_ref[...], shape)
    states = _scan(d2_ref[...], cut_s, pwf_ref, seg, False, c2_ref[...])
    x_ref[...] = states
    offset = states - ref_ref[...]
    cw = cw_ref[...]
    w3 = cw * offset
    w3_ref[...] = w3
    per_row = jnp.sum(w3 * offset, axis=1, keepdims=True)
    pick = lax.broadcasted_iota(jnp.int32, (scen, rows), 1) // seg
    want = lax.broadcasted_iota(jnp.int32, (scen, rows), 0)
    sel = (pick == want).astype(jnp.float32)
    per_scen = _dot(sel, jnp.broadcast_to(per_row, (rows, 128)))
    cost_ref[...] = per_scen * scale
    e3_ref[...] = _ends(_scan(w3, cut_e, pwb_ref, seg, True), seg, True)


def k_value_adjoint_in(seg, w3_ref, end_ref, start_ref, c3_ref, imap_ref, gain_ref, pwb_ref,
                       pwf_ref, s4_ref, e4_ref):
    shape = w3_ref.shape
    cut_e = jnp.broadcast_to(end_ref[...], shape)
    cut_s = jnp.broadcast_to(start_ref[...], shape)
    adjoint = _scan(w3_ref[...], cut_e, pwb_ref, seg, True, c3_ref[...])
    pulled = _dot(adjoint, imap_ref[...])
    source = -_dot(pulled, gain_ref[...])
    s4_ref[...] = source
    e4_ref[...] = _ends(_scan(source, cut_s, pwf_ref, seg, False), seg, False)


def k_last(seg, s4_ref, start_ref, c4_ref, x_ref, ref_ref, pwf_ref, g_ref):
    shape = s4_ref.shape
    cut_s = jnp.broadcast_to(start_ref[...], shape)
    va = _scan(s4_ref[...], cut_s, pwf_ref, seg, False, c4_ref[...])
    ref = ref_ref[...]
    offset = x_ref[...] - ref
    g_ref[...] = 0.5 * offset * offset + ref * va


def combine(last_value, frame_starts, powers, backward, seg_steps, local_levels, device_levels,
            extra=None):
    scen_count, width = last_value.shape
    devices = lax.axis_size("tm")
    device = lax.axis_index("tm")
    frame_device = devices - 1 - device if backward else device
    if extra is None:
        all_values = lax.all_gather(last_value[None], "tm", axis=0, tiled=True)
        gathered_extra = None
    else:
        lanes = jnp.broadcast_to(extra[:, None], (scen_count, 128))
        packed = jnp.concatenate([last_value, lanes], axis=1)
        gathered = lax.all_gather(packed[None], "tm", axis=0, tiled=True)
        all_values = gathered[:, :, :width]
        gathered_extra = gathered[:, :, width]
    seg_lo = jnp.arange(devices, dtype=jnp.int32)[:, None, None] * seg_steps
    inside = (frame_starts[None] >= seg_lo) & (frame_starts[None] < seg_lo + seg_steps)
    all_flags = 1.0 - jnp.any(inside, axis=-1).astype(jnp.float32)
    if backward:
        all_values = all_values[::-1]
    roll_by = devices - frame_device
    all_values = jnp.roll(all_values, roll_by, axis=0)
    all_flags = jnp.roll(all_flags, roll_by, axis=0)
    keep = (jnp.arange(devices, dtype=jnp.int32) >= roll_by).astype(jnp.float32)
    all_values = all_values * keep[:, None, None]
    all_flags = all_flags * keep[:, None] + (1.0 - keep[:, None])
    for level in range(device_levels):
        half = all_values.shape[0] // 2
        paired_values = all_values.reshape(half, 2, scen_count, width)
        paired_flags = all_flags.reshape(half, 2, scen_count)
        power = powers[local_levels + level]
        moved = row_times(paired_values[:, 0], power if backward else power.T)
        all_values = paired_flags[:, 1, :, None] * moved + paired_values[:, 1]
        all_flags = paired_flags[:, 0] * paired_flags[:, 1]
    return all_values[0], gathered_extra


def per_device(ref_traj, cost_weights, x_init, decay, coupling, links, input_map, ff_gain, lengths):
    scen_count, seg_steps, width = ref_traj.shape
    rows = scen_count * seg_steps
    devices = lax.axis_size("tm")
    device = lax.axis_index("tm")
    total = seg_steps * devices
    dynamics = build_dynamics(decay, coupling, links)
    local_levels = seg_steps.bit_length() - 1
    device_levels = (devices - 1).bit_length()
    power_count = local_levels + max(device_levels, 1)
    (squares,) = _call(
        k_powers, (jax.ShapeDtypeStruct((power_count, width, width), jnp.float32),), dynamics)
    forward_powers = squares
    pwb = squares
    pwf = squares
    ends_incl = jnp.cumsum(lengths, axis=1)
    starts = ends_incl - lengths
    mirrored = total - ends_incl
    positions = device * seg_steps + jnp.arange(seg_steps, dtype=jnp.int32)
    start_flag = jnp.any(positions[None, :, None] == starts[:, None, :], axis=-1)
    end_flag = jnp.any(positions[None, :, None] + 1 == ends_incl[:, None, :], axis=-1)
    start_col = start_flag.astype(jnp.float32).reshape(rows, 1)
    end_col = end_flag.astype(jnp.float32).reshape(rows, 1)
    init_image = jnp.dot(x_init, dynamics.T, precision=HIGH)
    cw = cost_weights.reshape(rows, width)
    ref = ref_traj.reshape(rows, width)
    f32 = jnp.float32
    full = jax.ShapeDtypeStruct((rows, width), f32)
    ends = jax.ShapeDtypeStruct((scen_count, width), f32)
    seg = seg_steps

    w1, e1 = _call(functools.partial(k_first, seg), (full, ends), cw, ref, end_col, pwb)
    c1, _ = combine(e1, mirrored, squares, True, seg, local_levels, device_levels)
    d2, e2 = _call(
        functools.partial(k_states_in, seg), (full, ends),
        w1, end_col, start_col, c1, init_image, ff_gain, input_map, pwb, pwf)
    c2, _ = combine(e2, starts, forward_powers, False, seg, local_levels, device_levels)
    cost_shape = jax.ShapeDtypeStruct((scen_count, 128), f32)
    states, w3, e3, cost_part = _call(
        functools.partial(k_adjoint_in, seg, 0.5 / total), (full, full, ends, cost_shape),
        d2, start_col, end_col, c2, cw, ref, pwf, pwb)
    c3, all_costs = combine(
        e3, mirrored, squares, True, seg, local_levels, device_levels, cost_part[:, 0])
    cost = jnp.sum(all_costs, axis=0)
    s4, e4 = _call(
        functools.partial(k_value_adjoint_in, seg), (full, ends),
        w3, end_col, start_col, c3, input_map, ff_gain, pwb, pwf)
    c4, _ = combine(e4, starts, forward_powers, False, seg, local_levels, device_levels)
    (grad,) = _call(
        functools.partial(k_last, seg), (full,), s4, start_col, c4, states, ref, pwf)
    shape3 = (scen_count, seg_steps, width)
    return (states.reshape(shape3), grad.reshape(shape3), cost)


def solution(mesh):
    placed = (
        P("groups", "tm", None),
        P("groups", "tm", None),
        P("groups", None),
        P(),
        P(),
        P(),
        P(),
        P(),
        P("groups", None),
    )
    return jax.shard_map(
        per_device,
        mesh=mesh,
        in_specs=placed,
        out_specs=(P("groups", "tm", None), P("groups", "tm", None), P("groups")),
        check_vma=False,
    )
```

```python
import functools

import jax
import jax.numpy as jnp
from jax import lax
from jax.experimental import pallas as pl
from jax.experimental.pallas import tpu as pltpu
from jax.sharding import PartitionSpec as P

HIGH = lax.Precision.HIGHEST


def build_dynamics(decay, coupling, links):
    size = decay.shape[0]
    width = coupling.shape[1]
    lanes = jnp.arange(size, dtype=jnp.int32)
    offsets = jnp.arange(width, dtype=jnp.int32)
    row_hot = (lanes[None, :, None] == links[:, 0:1, None] * width + offsets[None, None, :]).astype(
        jnp.float32
    )
    col_hot = (lanes[None, :, None] == links[:, 1:2, None] * width + offsets[None, None, :]).astype(
        jnp.float32
    )
    placed = jnp.einsum(
        "lia,lab,ljb->ij", row_hot, coupling, col_hot, precision=lax.Precision.HIGHEST
    )
    return jnp.diag(decay) + placed


def row_times(values, matrix):
    width = values.shape[-1]
    flat = jnp.dot(values.reshape(-1, width), matrix, precision=lax.Precision.HIGHEST)
    return flat.reshape(values.shape)


def _dot(a, b):
    return jnp.dot(a, b, precision=HIGH, preferred_element_type=jnp.float32)


def _dot_nt(a, b):
    return lax.dot_general(
        a, b, (((1,), (1,)), ((), ())), precision=HIGH, preferred_element_type=jnp.float32)


def k_powers(f_ref, out_ref):
    power = f_ref[...]
    out_ref[0] = power
    for level in range(1, out_ref.shape[0]):
        power = _dot(power, power)
        out_ref[level] = power


def _scan(v, cut, pw_ref, seg, backward, carry=None, levels=None):
    rows, width = v.shape
    scen = rows // seg
    t = lax.broadcasted_iota(jnp.int32, (rows, width), 0) % seg
    flags = 1.0 - cut
    if levels is None:
        levels = seg.bit_length() - 1
    step = _dot if backward else _dot_nt
    if carry is not None:
        pushed = step(carry, pw_ref[0])
        pushed = jnp.broadcast_to(pushed[:, None, :], (scen, seg, width)).reshape(rows, width)
        first = t == (seg - 1 if backward else 0)
        v = v + jnp.where(first, flags * pushed, 0.0)
    for level in range(levels):
        stride = 2**level
        if backward:
            prior_v = pltpu.roll(v, rows - stride, 0)
            prior_f = pltpu.roll(flags, rows - stride, 0)
            valid = t < seg - stride
        else:
            prior_v = pltpu.roll(v, stride, 0)
            prior_f = pltpu.roll(flags, stride, 0)
            valid = t >= stride
        prior_v = jnp.where(valid, prior_v, 0.0)
        prior_f = jnp.where(valid, prior_f, 1.0)
        v = v + flags * step(prior_v, pw_ref[level])
        flags = flags * prior_f
    return v


def _carry(g_ref, fl_ref, pw_ref, scen, backward):
    width = pw_ref.shape[1]
    g = g_ref[...][:, :width]
    rows = g.shape[0]
    devices = rows // scen
    local_levels = pw_ref.shape[0] - max((devices - 1).bit_length(), 1)
    r = lax.broadcasted_iota(jnp.int32, (rows, width), 0)
    flags = jnp.broadcast_to(fl_ref[...], (rows, width))
    step = _dot if backward else _dot_nt
    for level in range((devices - 1).bit_length()):
        stride = scen * 2**level
        if backward:
            prior_g = pltpu.roll(g, rows - stride, 0)
            prior_f = pltpu.roll(flags, rows - stride, 0)
            valid = r < rows - stride
        else:
            prior_g = pltpu.roll(g, stride, 0)
            prior_f = pltpu.roll(flags, stride, 0)
            valid = r >= stride
        prior_g = jnp.where(valid, prior_g, 0.0)
        prior_f = jnp.where(valid, prior_f, 1.0)
        g = g + flags * step(prior_g, pw_ref[local_levels + level])
        flags = flags * prior_f
    me = lax.axis_index("tm")
    target = me + 1 if backward else me - 1
    pick = lax.broadcasted_iota(jnp.int32, (scen, rows), 1)
    want = lax.broadcasted_iota(jnp.int32, (scen, rows), 0) + target * scen
    return _dot((pick == want).astype(jnp.float32), g)


def _ends(v, seg, backward):
    rows, width = v.shape
    scen = rows // seg
    pick = lax.broadcasted_iota(jnp.int32, (scen, rows), 1)
    want = lax.broadcasted_iota(jnp.int32, (scen, rows), 0) * seg + (0 if backward else seg - 1)
    sel = (pick == want).astype(jnp.float32)
    return _dot(sel, v)


def _vmem(count):
    return [pl.BlockSpec(memory_space=pltpu.VMEM)] * count


def _call(kernel, outs, *args):
    return pl.pallas_call(
        kernel,
        out_shape=outs,
        in_specs=_vmem(len(args)),
        out_specs=tuple(_vmem(len(outs))),
    )(*args)


def k_first(seg, cw_ref, ref_ref, end_ref, pwb_ref, w1_ref, e1_ref):
    width = cw_ref.shape[1]
    cut = jnp.broadcast_to(end_ref[...], cw_ref.shape)
    w1 = cw_ref[...] * ref_ref[...]
    w1_ref[...] = w1
    e1_ref[...] = _ends(_scan(w1, cut, pwb_ref, seg, True), seg, True)


def k_states_in(seg, w1_ref, end_ref, start_ref, c1_ref, fb_ref, init_ref, gain_ref, imap_ref, pwb_ref,
                pwf_ref, d2_ref, e2_ref):
    shape = w1_ref.shape
    cut_e = jnp.broadcast_to(end_ref[...], shape)
    cut_s = jnp.broadcast_to(start_ref[...], shape)
    c1 = _carry(c1_ref, fb_ref, pwb_ref, w1_ref.shape[0] // seg, True)
    vt = _scan(w1_ref[...], cut_e, pwb_ref, seg, True, c1)
    controls = lax.dot_general(
        vt, gain_ref[...], (((1,), (1,)), ((), ())), precision=HIGH,
        preferred_element_type=jnp.float32)
    forcing = -lax.dot_general(
        controls, imap_ref[...], (((1,), (1,)), ((), ())), precision=HIGH,
        preferred_element_type=jnp.float32)
    rows, width = shape
    scen = rows // seg
    init = jnp.broadcast_to(init_ref[...][:, None, :], (scen, seg, width)).reshape(rows, width)
    d2 = forcing + cut_s * init
    d2_ref[...] = d2
    e2_ref[...] = _ends(_scan(d2, cut_s, pwf_ref, seg, False), seg, False)


def k_adjoint_in(seg, scale, d2_ref, start_ref, end_ref, c2_ref, ff_ref, cw_ref, ref_ref, pwf_ref, pwb_ref,
                 x_ref, w3_ref, e3_ref, cost_ref):
    shape = d2_ref.shape
    rows, width = shape
    scen = rows // seg
    cut_s = jnp.broadcast_to(start_ref[...], shape)
    cut_e = jnp.broadcast_to(end_ref[...], shape)
    c2 = _carry(c2_ref, ff_ref, pwf_ref, scen, False)
    states = _scan(d2_ref[...], cut_s, pwf_ref, seg, False, c2)
    x_ref[...] = states
    offset = states - ref_ref[...]
    cw = cw_ref[...]
    w3 = cw * offset
    w3_ref[...] = w3
    per_row = jnp.sum(w3 * offset, axis=1, keepdims=True)
    pick = lax.broadcasted_iota(jnp.int32, (scen, rows), 1) // seg
    want = lax.broadcasted_iota(jnp.int32, (scen, rows), 0)
    sel = (pick == want).astype(jnp.float32)
    per_scen = _dot(sel, jnp.broadcast_to(per_row, (rows, 128)))
    cost_ref[...] = per_scen * scale
    e3_ref[...] = _ends(_scan(w3, cut_e, pwb_ref, seg, True), seg, True)


def k_value_adjoint_in(seg, w3_ref, end_ref, start_ref, c3_ref, fb_ref, imap_ref, gain_ref, pwb_ref,
                       pwf_ref, s4_ref, e4_ref):
    shape = w3_ref.shape
    cut_e = jnp.broadcast_to(end_ref[...], shape)
    cut_s = jnp.broadcast_to(start_ref[...], shape)
    c3 = _carry(c3_ref, fb_ref, pwb_ref, w3_ref.shape[0] // seg, True)
    adjoint = _scan(w3_ref[...], cut_e, pwb_ref, seg, True, c3)
    pulled = _dot(adjoint, imap_ref[...])
    source = -_dot(pulled, gain_ref[...])
    s4_ref[...] = source
    e4_ref[...] = _ends(_scan(source, cut_s, pwf_ref, seg, False), seg, False)


def k_last(seg, s4_ref, start_ref, c4_ref, ff_ref, x_ref, ref_ref, pwf_ref, g_ref):
    shape = s4_ref.shape
    cut_s = jnp.broadcast_to(start_ref[...], shape)
    c4 = _carry(c4_ref, ff_ref, pwf_ref, s4_ref.shape[0] // seg, False)
    va = _scan(s4_ref[...], cut_s, pwf_ref, seg, False, c4)
    ref = ref_ref[...]
    offset = x_ref[...] - ref
    g_ref[...] = 0.5 * offset * offset + ref * va


def combine(last_value, frame_starts, powers, backward, seg_steps, local_levels, device_levels,
            extra=None):
    scen_count, width = last_value.shape
    devices = lax.axis_size("tm")
    device = lax.axis_index("tm")
    frame_device = devices - 1 - device if backward else device
    if extra is None:
        all_values = lax.all_gather(last_value[None], "tm", axis=0, tiled=True)
        gathered_extra = None
    else:
        lanes = jnp.broadcast_to(extra[:, None], (scen_count, 128))
        packed = jnp.concatenate([last_value, lanes], axis=1)
        gathered = lax.all_gather(packed[None], "tm", axis=0, tiled=True)
        all_values = gathered[:, :, :width]
        gathered_extra = gathered[:, :, width]
    seg_lo = jnp.arange(devices, dtype=jnp.int32)[:, None, None] * seg_steps
    inside = (frame_starts[None] >= seg_lo) & (frame_starts[None] < seg_lo + seg_steps)
    all_flags = 1.0 - jnp.any(inside, axis=-1).astype(jnp.float32)
    if backward:
        all_values = all_values[::-1]
    roll_by = devices - frame_device
    all_values = jnp.roll(all_values, roll_by, axis=0)
    all_flags = jnp.roll(all_flags, roll_by, axis=0)
    keep = (jnp.arange(devices, dtype=jnp.int32) >= roll_by).astype(jnp.float32)
    all_values = all_values * keep[:, None, None]
    all_flags = all_flags * keep[:, None] + (1.0 - keep[:, None])
    for level in range(device_levels):
        half = all_values.shape[0] // 2
        paired_values = all_values.reshape(half, 2, scen_count, width)
        paired_flags = all_flags.reshape(half, 2, scen_count)
        power = powers[local_levels + level]
        moved = row_times(paired_values[:, 0], power if backward else power.T)
        all_values = paired_flags[:, 1, :, None] * moved + paired_values[:, 1]
        all_flags = paired_flags[:, 0] * paired_flags[:, 1]
    return all_values[0], gathered_extra


def per_device(ref_traj, cost_weights, x_init, decay, coupling, links, input_map, ff_gain, lengths):
    scen_count, seg_steps, width = ref_traj.shape
    rows = scen_count * seg_steps
    devices = lax.axis_size("tm")
    device = lax.axis_index("tm")
    total = seg_steps * devices
    dynamics = build_dynamics(decay, coupling, links)
    local_levels = seg_steps.bit_length() - 1
    device_levels = (devices - 1).bit_length()
    power_count = local_levels + max(device_levels, 1)
    (squares,) = _call(
        k_powers, (jax.ShapeDtypeStruct((power_count, width, width), jnp.float32),), dynamics)
    forward_powers = squares
    pwb = squares
    pwf = squares
    ends_incl = jnp.cumsum(lengths, axis=1)
    starts = ends_incl - lengths
    mirrored = total - ends_incl
    positions = device * seg_steps + jnp.arange(seg_steps, dtype=jnp.int32)
    start_flag = jnp.any(positions[None, :, None] == starts[:, None, :], axis=-1)
    end_flag = jnp.any(positions[None, :, None] + 1 == ends_incl[:, None, :], axis=-1)
    start_col = start_flag.astype(jnp.float32).reshape(rows, 1)
    end_col = end_flag.astype(jnp.float32).reshape(rows, 1)
    init_image = jnp.dot(x_init, dynamics.T, precision=HIGH)
    cw = cost_weights.reshape(rows, width)
    ref = ref_traj.reshape(rows, width)
    f32 = jnp.float32
    full = jax.ShapeDtypeStruct((rows, width), f32)
    ends = jax.ShapeDtypeStruct((scen_count, width), f32)
    seg = seg_steps

    seg_lo = jnp.arange(devices, dtype=jnp.int32)[:, None, None] * seg_steps
    in_fwd = (starts[None] >= seg_lo) & (starts[None] < seg_lo + seg_steps)
    in_bwd = (ends_incl[None] > seg_lo) & (ends_incl[None] <= seg_lo + seg_steps)
    flat = (devices * scen_count, 1)
    ff = 1.0 - jnp.any(in_fwd, axis=-1).astype(f32).reshape(flat)
    fb = 1.0 - jnp.any(in_bwd, axis=-1).astype(f32).reshape(flat)

    def gather(end_values):
        every = lax.all_gather(end_values[None], "tm", axis=0, tiled=True)
        return every.reshape(devices * scen_count, end_values.shape[1])

    w1, e1 = _call(functools.partial(k_first, seg), (full, ends), cw, ref, end_col, pwb)
    d2, e2 = _call(
        functools.partial(k_states_in, seg), (full, ends),
        w1, end_col, start_col, gather(e1), fb, init_image, ff_gain, input_map, pwb, pwf)
    cost_shape = jax.ShapeDtypeStruct((scen_count, 128), f32)
    states, w3, e3, cost_part = _call(
        functools.partial(k_adjoint_in, seg, 0.5 / total), (full, full, ends, cost_shape),
        d2, start_col, end_col, gather(e2), ff, cw, ref, pwf, pwb)
    g3 = gather(jnp.concatenate([e3, cost_part], axis=1))
    cost = jnp.sum(g3[:, width].reshape(devices, scen_count), axis=0)
    s4, e4 = _call(
        functools.partial(k_value_adjoint_in, seg), (full, ends),
        w3, end_col, start_col, g3, fb, input_map, ff_gain, pwb, pwf)
    (grad,) = _call(
        functools.partial(k_last, seg), (full,), s4, start_col, gather(e4), ff, states, ref, pwf)
    shape3 = (scen_count, seg_steps, width)
    return (states.reshape(shape3), grad.reshape(shape3), cost)


def solution(mesh):
    placed = (
        P("groups", "tm", None),
        P("groups", "tm", None),
        P("groups", None),
        P(),
        P(),
        P(),
        P(),
        P(),
        P("groups", None),
    )
    return jax.shard_map(
        per_device,
        mesh=mesh,
        in_specs=placed,
        out_specs=(P("groups", "tm", None), P("groups", "tm", None), P("groups")),
        check_vma=False,
    )
```

```python
import functools

import jax
import jax.numpy as jnp
from jax import lax
from jax.experimental import pallas as pl
from jax.experimental.pallas import tpu as pltpu
from jax.sharding import PartitionSpec as P

HIGH = lax.Precision.HIGHEST


def build_dynamics(decay, coupling, links):
    size = decay.shape[0]
    width = coupling.shape[1]
    lanes = jnp.arange(size, dtype=jnp.int32)
    offsets = jnp.arange(width, dtype=jnp.int32)
    row_hot = (lanes[None, :, None] == links[:, 0:1, None] * width + offsets[None, None, :]).astype(
        jnp.float32
    )
    col_hot = (lanes[None, :, None] == links[:, 1:2, None] * width + offsets[None, None, :]).astype(
        jnp.float32
    )
    placed = jnp.einsum(
        "lia,lab,ljb->ij", row_hot, coupling, col_hot, precision=lax.Precision.HIGHEST
    )
    return jnp.diag(decay) + placed


def row_times(values, matrix):
    width = values.shape[-1]
    flat = jnp.dot(values.reshape(-1, width), matrix, precision=lax.Precision.HIGHEST)
    return flat.reshape(values.shape)


def _dot(a, b):
    return jnp.dot(a, b, precision=HIGH, preferred_element_type=jnp.float32)


def _dot_nt(a, b):
    return lax.dot_general(
        a, b, (((1,), (1,)), ((), ())), precision=HIGH, preferred_element_type=jnp.float32)


def _split(x):
    hi = x.astype(jnp.bfloat16)
    lo = (x - hi.astype(jnp.float32)).astype(jnp.bfloat16)
    return hi, lo


def _mm(a, b, nt=False):
    dims = (((1,), (1 if nt else 0,)), ((), ()))
    a_hi, a_lo = _split(a)
    b_hi, b_lo = _split(b)
    part = functools.partial(lax.dot_general, dimension_numbers=dims,
                             preferred_element_type=jnp.float32)
    return part(a_lo, b_hi) + part(a_hi, b_lo) + part(a_hi, b_hi)


def k_powers(f_ref, out_ref):
    power = f_ref[...]
    out_ref[0] = power
    for level in range(1, out_ref.shape[0]):
        power = _dot(power, power)
        out_ref[level] = power


def _scan(v, cut, pw_ref, seg, backward, carry=None, levels=None):
    rows, width = v.shape
    scen = rows // seg
    t = lax.broadcasted_iota(jnp.int32, (rows, width), 0) % seg
    flags = 1.0 - cut
    if levels is None:
        levels = seg.bit_length() - 1
    step = functools.partial(_mm, nt=not backward)
    if carry is not None:
        pushed = step(carry, pw_ref[0])
        pushed = jnp.broadcast_to(pushed[:, None, :], (scen, seg, width)).reshape(rows, width)
        first = t == (seg - 1 if backward else 0)
        v = v + jnp.where(first, flags * pushed, 0.0)
    for level in range(levels):
        stride = 2**level
        if backward:
            prior_v = pltpu.roll(v, rows - stride, 0)
            prior_f = pltpu.roll(flags, rows - stride, 0)
            valid = t < seg - stride
        else:
            prior_v = pltpu.roll(v, stride, 0)
            prior_f = pltpu.roll(flags, stride, 0)
            valid = t >= stride
        prior_v = jnp.where(valid, prior_v, 0.0)
        prior_f = jnp.where(valid, prior_f, 1.0)
        v = v + flags * step(prior_v, pw_ref[level])
        flags = flags * prior_f
    return v


def _carry(g_ref, fl_ref, pw_ref, scen, backward):
    width = pw_ref.shape[1]
    g = g_ref[...][:, :width]
    rows = g.shape[0]
    devices = rows // scen
    local_levels = pw_ref.shape[0] - max((devices - 1).bit_length(), 1)
    r = lax.broadcasted_iota(jnp.int32, (rows, width), 0)
    flags = jnp.broadcast_to(fl_ref[...], (rows, width))
    step = functools.partial(_mm, nt=not backward)
    for level in range((devices - 1).bit_length()):
        stride = scen * 2**level
        if backward:
            prior_g = pltpu.roll(g, rows - stride, 0)
            prior_f = pltpu.roll(flags, rows - stride, 0)
            valid = r < rows - stride
        else:
            prior_g = pltpu.roll(g, stride, 0)
            prior_f = pltpu.roll(flags, stride, 0)
            valid = r >= stride
        prior_g = jnp.where(valid, prior_g, 0.0)
        prior_f = jnp.where(valid, prior_f, 1.0)
        g = g + flags * step(prior_g, pw_ref[local_levels + level])
        flags = flags * prior_f
    me = lax.axis_index("tm")
    target = me + 1 if backward else me - 1
    pick = lax.broadcasted_iota(jnp.int32, (scen, rows), 1)
    want = lax.broadcasted_iota(jnp.int32, (scen, rows), 0) + target * scen
    return _dot((pick == want).astype(jnp.float32), g)


def _ends(v, seg, backward):
    rows, width = v.shape
    scen = rows // seg
    pick = lax.broadcasted_iota(jnp.int32, (scen, rows), 1)
    want = lax.broadcasted_iota(jnp.int32, (scen, rows), 0) * seg + (0 if backward else seg - 1)
    sel = (pick == want).astype(jnp.float32)
    return _dot(sel, v)


def _vmem(count):
    return [pl.BlockSpec(memory_space=pltpu.VMEM)] * count


def _call(kernel, outs, *args):
    return pl.pallas_call(
        kernel,
        out_shape=outs,
        in_specs=_vmem(len(args)),
        out_specs=tuple(_vmem(len(outs))),
    )(*args)


def k_first(seg, cw_ref, ref_ref, end_ref, pwb_ref, w1_ref, e1_ref):
    width = cw_ref.shape[1]
    cut = jnp.broadcast_to(end_ref[...], cw_ref.shape)
    w1 = cw_ref[...] * ref_ref[...]
    w1_ref[...] = w1
    e1_ref[...] = _ends(_scan(w1, cut, pwb_ref, seg, True), seg, True)


def k_states_in(seg, w1_ref, end_ref, start_ref, c1_ref, fb_ref, init_ref, gain_ref, imap_ref, pwb_ref,
                pwf_ref, d2_ref, e2_ref):
    shape = w1_ref.shape
    cut_e = jnp.broadcast_to(end_ref[...], shape)
    cut_s = jnp.broadcast_to(start_ref[...], shape)
    c1 = _carry(c1_ref, fb_ref, pwb_ref, w1_ref.shape[0] // seg, True)
    vt = _scan(w1_ref[...], cut_e, pwb_ref, seg, True, c1)
    controls = _mm(vt, gain_ref[...], nt=True)
    forcing = -_mm(controls, imap_ref[...], nt=True)
    rows, width = shape
    scen = rows // seg
    init = jnp.broadcast_to(init_ref[...][:, None, :], (scen, seg, width)).reshape(rows, width)
    d2 = forcing + cut_s * init
    d2_ref[...] = d2
    e2_ref[...] = _ends(_scan(d2, cut_s, pwf_ref, seg, False), seg, False)


def k_adjoint_in(seg, scale, d2_ref, start_ref, end_ref, c2_ref, ff_ref, cw_ref, ref_ref, pwf_ref, pwb_ref,
                 x_ref, w3_ref, e3_ref, cost_ref):
    shape = d2_ref.shape
    rows, width = shape
    scen = rows // seg
    cut_s = jnp.broadcast_to(start_ref[...], shape)
    cut_e = jnp.broadcast_to(end_ref[...], shape)
    c2 = _carry(c2_ref, ff_ref, pwf_ref, scen, False)
    states = _scan(d2_ref[...], cut_s, pwf_ref, seg, False, c2)
    x_ref[...] = states
    offset = states - ref_ref[...]
    cw = cw_ref[...]
    w3 = cw * offset
    w3_ref[...] = w3
    per_row = jnp.sum(w3 * offset, axis=1, keepdims=True)
    pick = lax.broadcasted_iota(jnp.int32, (scen, rows), 1) // seg
    want = lax.broadcasted_iota(jnp.int32, (scen, rows), 0)
    sel = (pick == want).astype(jnp.float32)
    per_scen = _dot(sel, jnp.broadcast_to(per_row, (rows, 128)))
    cost_ref[...] = per_scen * scale
    e3_ref[...] = _ends(_scan(w3, cut_e, pwb_ref, seg, True), seg, True)


def k_value_adjoint_in(seg, w3_ref, end_ref, start_ref, c3_ref, fb_ref, imap_ref, gain_ref, pwb_ref,
                       pwf_ref, s4_ref, e4_ref):
    shape = w3_ref.shape
    cut_e = jnp.broadcast_to(end_ref[...], shape)
    cut_s = jnp.broadcast_to(start_ref[...], shape)
    c3 = _carry(c3_ref, fb_ref, pwb_ref, w3_ref.shape[0] // seg, True)
    adjoint = _scan(w3_ref[...], cut_e, pwb_ref, seg, True, c3)
    pulled = _mm(adjoint, imap_ref[...])
    source = -_mm(pulled, gain_ref[...])
    s4_ref[...] = source
    e4_ref[...] = _ends(_scan(source, cut_s, pwf_ref, seg, False), seg, False)


def k_last(seg, s4_ref, start_ref, c4_ref, ff_ref, x_ref, ref_ref, pwf_ref, g_ref):
    shape = s4_ref.shape
    cut_s = jnp.broadcast_to(start_ref[...], shape)
    c4 = _carry(c4_ref, ff_ref, pwf_ref, s4_ref.shape[0] // seg, False)
    va = _scan(s4_ref[...], cut_s, pwf_ref, seg, False, c4)
    ref = ref_ref[...]
    offset = x_ref[...] - ref
    g_ref[...] = 0.5 * offset * offset + ref * va


def combine(last_value, frame_starts, powers, backward, seg_steps, local_levels, device_levels,
            extra=None):
    scen_count, width = last_value.shape
    devices = lax.axis_size("tm")
    device = lax.axis_index("tm")
    frame_device = devices - 1 - device if backward else device
    if extra is None:
        all_values = lax.all_gather(last_value[None], "tm", axis=0, tiled=True)
        gathered_extra = None
    else:
        lanes = jnp.broadcast_to(extra[:, None], (scen_count, 128))
        packed = jnp.concatenate([last_value, lanes], axis=1)
        gathered = lax.all_gather(packed[None], "tm", axis=0, tiled=True)
        all_values = gathered[:, :, :width]
        gathered_extra = gathered[:, :, width]
    seg_lo = jnp.arange(devices, dtype=jnp.int32)[:, None, None] * seg_steps
    inside = (frame_starts[None] >= seg_lo) & (frame_starts[None] < seg_lo + seg_steps)
    all_flags = 1.0 - jnp.any(inside, axis=-1).astype(jnp.float32)
    if backward:
        all_values = all_values[::-1]
    roll_by = devices - frame_device
    all_values = jnp.roll(all_values, roll_by, axis=0)
    all_flags = jnp.roll(all_flags, roll_by, axis=0)
    keep = (jnp.arange(devices, dtype=jnp.int32) >= roll_by).astype(jnp.float32)
    all_values = all_values * keep[:, None, None]
    all_flags = all_flags * keep[:, None] + (1.0 - keep[:, None])
    for level in range(device_levels):
        half = all_values.shape[0] // 2
        paired_values = all_values.reshape(half, 2, scen_count, width)
        paired_flags = all_flags.reshape(half, 2, scen_count)
        power = powers[local_levels + level]
        moved = row_times(paired_values[:, 0], power if backward else power.T)
        all_values = paired_flags[:, 1, :, None] * moved + paired_values[:, 1]
        all_flags = paired_flags[:, 0] * paired_flags[:, 1]
    return all_values[0], gathered_extra


def per_device(ref_traj, cost_weights, x_init, decay, coupling, links, input_map, ff_gain, lengths):
    scen_count, seg_steps, width = ref_traj.shape
    rows = scen_count * seg_steps
    devices = lax.axis_size("tm")
    device = lax.axis_index("tm")
    total = seg_steps * devices
    dynamics = build_dynamics(decay, coupling, links)
    local_levels = seg_steps.bit_length() - 1
    device_levels = (devices - 1).bit_length()
    power_count = local_levels + max(device_levels, 1)
    (squares,) = _call(
        k_powers, (jax.ShapeDtypeStruct((power_count, width, width), jnp.float32),), dynamics)
    forward_powers = squares
    pwb = squares
    pwf = squares
    ends_incl = jnp.cumsum(lengths, axis=1)
    starts = ends_incl - lengths
    mirrored = total - ends_incl
    positions = device * seg_steps + jnp.arange(seg_steps, dtype=jnp.int32)
    start_flag = jnp.any(positions[None, :, None] == starts[:, None, :], axis=-1)
    end_flag = jnp.any(positions[None, :, None] + 1 == ends_incl[:, None, :], axis=-1)
    start_col = start_flag.astype(jnp.float32).reshape(rows, 1)
    end_col = end_flag.astype(jnp.float32).reshape(rows, 1)
    init_image = jnp.dot(x_init, dynamics.T, precision=HIGH)
    cw = cost_weights.reshape(rows, width)
    ref = ref_traj.reshape(rows, width)
    f32 = jnp.float32
    full = jax.ShapeDtypeStruct((rows, width), f32)
    ends = jax.ShapeDtypeStruct((scen_count, width), f32)
    seg = seg_steps

    seg_lo = jnp.arange(devices, dtype=jnp.int32)[:, None, None] * seg_steps
    in_fwd = (starts[None] >= seg_lo) & (starts[None] < seg_lo + seg_steps)
    in_bwd = (ends_incl[None] > seg_lo) & (ends_incl[None] <= seg_lo + seg_steps)
    flat = (devices * scen_count, 1)
    ff = 1.0 - jnp.any(in_fwd, axis=-1).astype(f32).reshape(flat)
    fb = 1.0 - jnp.any(in_bwd, axis=-1).astype(f32).reshape(flat)

    def gather(end_values):
        every = lax.all_gather(end_values[None], "tm", axis=0, tiled=True)
        return every.reshape(devices * scen_count, end_values.shape[1])

    w1, e1 = _call(functools.partial(k_first, seg), (full, ends), cw, ref, end_col, pwb)
    d2, e2 = _call(
        functools.partial(k_states_in, seg), (full, ends),
        w1, end_col, start_col, gather(e1), fb, init_image, ff_gain, input_map, pwb, pwf)
    cost_shape = jax.ShapeDtypeStruct((scen_count, 128), f32)
    states, w3, e3, cost_part = _call(
        functools.partial(k_adjoint_in, seg, 0.5 / total), (full, full, ends, cost_shape),
        d2, start_col, end_col, gather(e2), ff, cw, ref, pwf, pwb)
    g3 = gather(jnp.concatenate([e3, cost_part], axis=1))
    cost = jnp.sum(g3[:, width].reshape(devices, scen_count), axis=0)
    s4, e4 = _call(
        functools.partial(k_value_adjoint_in, seg), (full, ends),
        w3, end_col, start_col, g3, fb, input_map, ff_gain, pwb, pwf)
    (grad,) = _call(
        functools.partial(k_last, seg), (full,), s4, start_col, gather(e4), ff, states, ref, pwf)
    shape3 = (scen_count, seg_steps, width)
    return (states.reshape(shape3), grad.reshape(shape3), cost)


def solution(mesh):
    placed = (
        P("groups", "tm", None),
        P("groups", "tm", None),
        P("groups", None),
        P(),
        P(),
        P(),
        P(),
        P(),
        P("groups", None),
    )
    return jax.shard_map(
        per_device,
        mesh=mesh,
        in_specs=placed,
        out_specs=(P("groups", "tm", None), P("groups", "tm", None), P("groups")),
        check_vma=False,
    )
```

```python
import functools

import jax
import jax.numpy as jnp
from jax import lax
from jax.experimental import pallas as pl
from jax.experimental.pallas import tpu as pltpu
from jax.sharding import PartitionSpec as P

HIGH = lax.Precision.HIGHEST


def build_dynamics(decay, coupling, links):
    size = decay.shape[0]
    width = coupling.shape[1]
    lanes = jnp.arange(size, dtype=jnp.int32)
    offsets = jnp.arange(width, dtype=jnp.int32)
    row_hot = (lanes[None, :, None] == links[:, 0:1, None] * width + offsets[None, None, :]).astype(
        jnp.float32
    )
    col_hot = (lanes[None, :, None] == links[:, 1:2, None] * width + offsets[None, None, :]).astype(
        jnp.float32
    )
    placed = jnp.einsum(
        "lia,lab,ljb->ij", row_hot, coupling, col_hot, precision=lax.Precision.HIGHEST
    )
    return jnp.diag(decay) + placed


def row_times(values, matrix):
    width = values.shape[-1]
    flat = jnp.dot(values.reshape(-1, width), matrix, precision=lax.Precision.HIGHEST)
    return flat.reshape(values.shape)


def _dot(a, b):
    return jnp.dot(a, b, precision=HIGH, preferred_element_type=jnp.float32)


def _dot_nt(a, b):
    return lax.dot_general(
        a, b, (((1,), (1,)), ((), ())), precision=HIGH, preferred_element_type=jnp.float32)


def _split(x):
    hi = x.astype(jnp.bfloat16)
    lo = (x - hi.astype(jnp.float32)).astype(jnp.bfloat16)
    return hi, lo


def _mm(a, b, nt=False):
    dims = (((1,), (1 if nt else 0,)), ((), ()))
    a_hi, a_lo = _split(a)
    b_hi, b_lo = _split(b)
    part = functools.partial(lax.dot_general, dimension_numbers=dims,
                             preferred_element_type=jnp.float32)
    return part(a_lo, b_hi) + part(a_hi, b_lo) + part(a_hi, b_hi)


def k_powers(f_ref, out_ref):
    power = f_ref[...]
    out_ref[0] = power
    for level in range(1, out_ref.shape[0]):
        power = _dot(power, power)
        out_ref[level] = power


def _scan(v, cut, pw_ref, seg, backward, carry=None, levels=None):
    rows, width = v.shape
    scen = rows // seg
    t = lax.broadcasted_iota(jnp.int32, (rows, width), 0) % seg
    flags = 1.0 - cut
    if levels is None:
        levels = seg.bit_length() - 1
    step = functools.partial(_mm, nt=not backward)
    if carry is not None:
        pushed = step(carry, pw_ref[0])
        pushed = jnp.broadcast_to(pushed[:, None, :], (scen, seg, width)).reshape(rows, width)
        first = t == (seg - 1 if backward else 0)
        v = v + jnp.where(first, flags * pushed, 0.0)
    for level in range(levels):
        stride = 2**level
        if backward:
            prior_v = pltpu.roll(v, rows - stride, 0)
            prior_f = pltpu.roll(flags, rows - stride, 0)
            valid = t < seg - stride
        else:
            prior_v = pltpu.roll(v, stride, 0)
            prior_f = pltpu.roll(flags, stride, 0)
            valid = t >= stride
        prior_v = jnp.where(valid, prior_v, 0.0)
        prior_f = jnp.where(valid, prior_f, 1.0)
        v = v + flags * step(prior_v, pw_ref[level])
        flags = flags * prior_f
    return v


def _carry(g_ref, fl_ref, pw_ref, scen, backward):
    width = pw_ref.shape[1]
    g = g_ref[...][:, :width]
    rows = g.shape[0]
    devices = rows // scen
    local_levels = pw_ref.shape[0] - max((devices - 1).bit_length(), 1)
    r = lax.broadcasted_iota(jnp.int32, (rows, width), 0)
    flags = jnp.broadcast_to(fl_ref[...], (rows, width))
    step = functools.partial(_mm, nt=not backward)
    for level in range((devices - 1).bit_length()):
        stride = scen * 2**level
        if backward:
            prior_g = pltpu.roll(g, rows - stride, 0)
            prior_f = pltpu.roll(flags, rows - stride, 0)
            valid = r < rows - stride
        else:
            prior_g = pltpu.roll(g, stride, 0)
            prior_f = pltpu.roll(flags, stride, 0)
            valid = r >= stride
        prior_g = jnp.where(valid, prior_g, 0.0)
        prior_f = jnp.where(valid, prior_f, 1.0)
        g = g + flags * step(prior_g, pw_ref[local_levels + level])
        flags = flags * prior_f
    me = lax.axis_index("tm")
    target = me + 1 if backward else me - 1
    pick = lax.broadcasted_iota(jnp.int32, (scen, rows), 1)
    want = lax.broadcasted_iota(jnp.int32, (scen, rows), 0) + target * scen
    return _dot((pick == want).astype(jnp.float32), g)


def _ends(v, seg, backward):
    rows, width = v.shape
    scen = rows // seg
    pick = lax.broadcasted_iota(jnp.int32, (scen, rows), 1)
    want = lax.broadcasted_iota(jnp.int32, (scen, rows), 0) * seg + (0 if backward else seg - 1)
    sel = (pick == want).astype(jnp.float32)
    return _dot(sel, v)


def _vmem(count):
    return [pl.BlockSpec(memory_space=pltpu.VMEM)] * count


def _call(kernel, outs, *args):
    return pl.pallas_call(
        kernel,
        out_shape=outs,
        in_specs=_vmem(len(args)),
        out_specs=tuple(_vmem(len(outs))),
    )(*args)


def k_first(seg, cw_ref, ref_ref, end_ref, pwb_ref, w1_ref, e1_ref):
    width = cw_ref.shape[1]
    cut = jnp.broadcast_to(end_ref[...], cw_ref.shape)
    w1 = cw_ref[...] * ref_ref[...]
    w1_ref[...] = w1
    e1_ref[...] = _ends(_scan(w1, cut, pwb_ref, seg, True), seg, True)


def k_states_in(seg, w1_ref, end_ref, start_ref, c1_ref, fb_ref, init_ref, gain_ref, imap_ref, pwb_ref,
                pwf_ref, d2_ref, e2_ref):
    shape = w1_ref.shape
    cut_e = jnp.broadcast_to(end_ref[...], shape)
    cut_s = jnp.broadcast_to(start_ref[...], shape)
    c1 = _carry(c1_ref, fb_ref, pwb_ref, w1_ref.shape[0] // seg, True)
    vt = _scan(w1_ref[...], cut_e, pwb_ref, seg, True, c1)
    controls = _mm(vt, gain_ref[...], nt=True)
    forcing = -_mm(controls, imap_ref[...], nt=True)
    rows, width = shape
    scen = rows // seg
    init = jnp.broadcast_to(init_ref[...][:, None, :], (scen, seg, width)).reshape(rows, width)
    d2 = forcing + cut_s * init
    d2_ref[...] = d2
    e2_ref[...] = _ends(_scan(d2, cut_s, pwf_ref, seg, False), seg, False)


def k_adjoint_in(seg, scale, d2_ref, start_ref, end_ref, c2_ref, ff_ref, cw_ref, ref_ref, pwf_ref, pwb_ref,
                 x_ref, w3_ref, e3_ref, cost_ref):
    shape = d2_ref.shape
    rows, width = shape
    scen = rows // seg
    cut_s = jnp.broadcast_to(start_ref[...], shape)
    cut_e = jnp.broadcast_to(end_ref[...], shape)
    c2 = _carry(c2_ref, ff_ref, pwf_ref, scen, False)
    states = _scan(d2_ref[...], cut_s, pwf_ref, seg, False, c2)
    x_ref[...] = states
    offset = states - ref_ref[...]
    cw = cw_ref[...]
    w3 = cw * offset
    w3_ref[...] = w3
    per_row = jnp.sum(w3 * offset, axis=1, keepdims=True)
    pick = lax.broadcasted_iota(jnp.int32, (scen, rows), 1) // seg
    want = lax.broadcasted_iota(jnp.int32, (scen, rows), 0)
    sel = (pick == want).astype(jnp.float32)
    per_scen = _dot(sel, jnp.broadcast_to(per_row, (rows, 128)))
    cost_ref[...] = per_scen * scale
    e3_ref[...] = _ends(_scan(w3, cut_e, pwb_ref, seg, True), seg, True)


def k_value_adjoint_in(seg, w3_ref, end_ref, start_ref, c3_ref, fb_ref, imap_ref, gain_ref, pwb_ref,
                       pwf_ref, s4_ref, e4_ref):
    shape = w3_ref.shape
    cut_e = jnp.broadcast_to(end_ref[...], shape)
    cut_s = jnp.broadcast_to(start_ref[...], shape)
    c3 = _carry(c3_ref, fb_ref, pwb_ref, w3_ref.shape[0] // seg, True)
    adjoint = _scan(w3_ref[...], cut_e, pwb_ref, seg, True, c3)
    pulled = _mm(adjoint, imap_ref[...])
    source = -_mm(pulled, gain_ref[...])
    s4_ref[...] = source
    e4_ref[...] = _ends(_scan(source, cut_s, pwf_ref, seg, False), seg, False)


def k_last(seg, s4_ref, start_ref, c4_ref, ff_ref, x_ref, ref_ref, pwf_ref, g_ref):
    shape = s4_ref.shape
    cut_s = jnp.broadcast_to(start_ref[...], shape)
    c4 = _carry(c4_ref, ff_ref, pwf_ref, s4_ref.shape[0] // seg, False)
    va = _scan(s4_ref[...], cut_s, pwf_ref, seg, False, c4)
    ref = ref_ref[...]
    offset = x_ref[...] - ref
    g_ref[...] = 0.5 * offset * offset + ref * va


def combine(last_value, frame_starts, powers, backward, seg_steps, local_levels, device_levels,
            extra=None):
    scen_count, width = last_value.shape
    devices = lax.axis_size("tm")
    device = lax.axis_index("tm")
    frame_device = devices - 1 - device if backward else device
    if extra is None:
        all_values = lax.all_gather(last_value[None], "tm", axis=0, tiled=True)
        gathered_extra = None
    else:
        lanes = jnp.broadcast_to(extra[:, None], (scen_count, 128))
        packed = jnp.concatenate([last_value, lanes], axis=1)
        gathered = lax.all_gather(packed[None], "tm", axis=0, tiled=True)
        all_values = gathered[:, :, :width]
        gathered_extra = gathered[:, :, width]
    seg_lo = jnp.arange(devices, dtype=jnp.int32)[:, None, None] * seg_steps
    inside = (frame_starts[None] >= seg_lo) & (frame_starts[None] < seg_lo + seg_steps)
    all_flags = 1.0 - jnp.any(inside, axis=-1).astype(jnp.float32)
    if backward:
        all_values = all_values[::-1]
    roll_by = devices - frame_device
    all_values = jnp.roll(all_values, roll_by, axis=0)
    all_flags = jnp.roll(all_flags, roll_by, axis=0)
    keep = (jnp.arange(devices, dtype=jnp.int32) >= roll_by).astype(jnp.float32)
    all_values = all_values * keep[:, None, None]
    all_flags = all_flags * keep[:, None] + (1.0 - keep[:, None])
    for level in range(device_levels):
        half = all_values.shape[0] // 2
        paired_values = all_values.reshape(half, 2, scen_count, width)
        paired_flags = all_flags.reshape(half, 2, scen_count)
        power = powers[local_levels + level]
        moved = row_times(paired_values[:, 0], power if backward else power.T)
        all_values = paired_flags[:, 1, :, None] * moved + paired_values[:, 1]
        all_flags = paired_flags[:, 0] * paired_flags[:, 1]
    return all_values[0], gathered_extra


def per_device(ref_traj, cost_weights, x_init, decay, coupling, links, input_map, ff_gain, lengths):
    scen_count, seg_steps, width = ref_traj.shape
    rows = scen_count * seg_steps
    devices = lax.axis_size("tm")
    device = lax.axis_index("tm")
    total = seg_steps * devices
    dynamics = build_dynamics(decay, coupling, links)
    local_levels = seg_steps.bit_length() - 1
    device_levels = (devices - 1).bit_length()
    power_count = local_levels + max(device_levels, 1)
    (squares,) = _call(
        k_powers, (jax.ShapeDtypeStruct((power_count, width, width), jnp.float32),), dynamics)
    forward_powers = squares
    pwb = squares
    pwf = squares
    ends_incl = jnp.cumsum(lengths, axis=1)
    starts = ends_incl - lengths
    mirrored = total - ends_incl
    positions = device * seg_steps + jnp.arange(seg_steps, dtype=jnp.int32)
    start_flag = jnp.any(positions[None, :, None] == starts[:, None, :], axis=-1)
    end_flag = jnp.any(positions[None, :, None] + 1 == ends_incl[:, None, :], axis=-1)
    start_col = start_flag.astype(jnp.float32).reshape(rows, 1)
    end_col = end_flag.astype(jnp.float32).reshape(rows, 1)
    init_image = jnp.dot(x_init, dynamics.T, precision=HIGH)
    cw = cost_weights.reshape(rows, width)
    ref = ref_traj.reshape(rows, width)
    f32 = jnp.float32
    full = jax.ShapeDtypeStruct((rows, width), f32)
    ends = jax.ShapeDtypeStruct((scen_count, width), f32)
    seg = seg_steps

    seg_lo = jnp.arange(devices, dtype=jnp.int32)[:, None, None] * seg_steps
    in_fwd = (starts[None] >= seg_lo) & (starts[None] < seg_lo + seg_steps)
    in_bwd = (ends_incl[None] > seg_lo) & (ends_incl[None] <= seg_lo + seg_steps)
    flat = (devices * scen_count, 1)
    ff = 1.0 - jnp.any(in_fwd, axis=-1).astype(f32).reshape(flat)
    fb = 1.0 - jnp.any(in_bwd, axis=-1).astype(f32).reshape(flat)

    def gather(end_values):
        copies = jnp.broadcast_to(end_values[None], (devices,) + end_values.shape)
        every = lax.all_to_all(copies, "tm", 0, 0, tiled=True)
        return every.reshape(devices * scen_count, end_values.shape[1])

    w1, e1 = _call(functools.partial(k_first, seg), (full, ends), cw, ref, end_col, pwb)
    d2, e2 = _call(
        functools.partial(k_states_in, seg), (full, ends),
        w1, end_col, start_col, gather(e1), fb, init_image, ff_gain, input_map, pwb, pwf)
    cost_shape = jax.ShapeDtypeStruct((scen_count, 128), f32)
    states, w3, e3, cost_part = _call(
        functools.partial(k_adjoint_in, seg, 0.5 / total), (full, full, ends, cost_shape),
        d2, start_col, end_col, gather(e2), ff, cw, ref, pwf, pwb)
    g3 = gather(jnp.concatenate([e3, cost_part], axis=1))
    cost = jnp.sum(g3[:, width].reshape(devices, scen_count), axis=0)
    s4, e4 = _call(
        functools.partial(k_value_adjoint_in, seg), (full, ends),
        w3, end_col, start_col, g3, fb, input_map, ff_gain, pwb, pwf)
    (grad,) = _call(
        functools.partial(k_last, seg), (full,), s4, start_col, gather(e4), ff, states, ref, pwf)
    shape3 = (scen_count, seg_steps, width)
    return (states.reshape(shape3), grad.reshape(shape3), cost)


def solution(mesh):
    placed = (
        P("groups", "tm", None),
        P("groups", "tm", None),
        P("groups", None),
        P(),
        P(),
        P(),
        P(),
        P(),
        P("groups", None),
    )
    return jax.shard_map(
        per_device,
        mesh=mesh,
        in_specs=placed,
        out_specs=(P("groups", "tm", None), P("groups", "tm", None), P("groups")),
        check_vma=False,
    )
```

```python
import functools

import jax
import jax.numpy as jnp
from jax import lax
from jax.experimental import pallas as pl
from jax.experimental.pallas import tpu as pltpu
from jax.sharding import PartitionSpec as P

HIGH = lax.Precision.HIGHEST


def build_dynamics(decay, coupling, links):
    size = decay.shape[0]
    width = coupling.shape[1]
    lanes = jnp.arange(size, dtype=jnp.int32)
    offsets = jnp.arange(width, dtype=jnp.int32)
    row_hot = (lanes[None, :, None] == links[:, 0:1, None] * width + offsets[None, None, :]).astype(
        jnp.float32
    )
    col_hot = (lanes[None, :, None] == links[:, 1:2, None] * width + offsets[None, None, :]).astype(
        jnp.float32
    )
    placed = jnp.einsum(
        "lia,lab,ljb->ij", row_hot, coupling, col_hot, precision=lax.Precision.HIGHEST
    )
    return jnp.diag(decay) + placed


def row_times(values, matrix):
    width = values.shape[-1]
    flat = jnp.dot(values.reshape(-1, width), matrix, precision=lax.Precision.HIGHEST)
    return flat.reshape(values.shape)


def _dot(a, b):
    return jnp.dot(a, b, precision=HIGH, preferred_element_type=jnp.float32)


def _dot_nt(a, b):
    return lax.dot_general(
        a, b, (((1,), (1,)), ((), ())), precision=HIGH, preferred_element_type=jnp.float32)


def _split(x):
    hi = x.astype(jnp.bfloat16)
    lo = (x - hi.astype(jnp.float32)).astype(jnp.bfloat16)
    return hi, lo


def _mm(a, b, nt=False):
    dims = (((1,), (1 if nt else 0,)), ((), ()))
    a_hi, a_lo = _split(a)
    b_hi, b_lo = _split(b)
    part = functools.partial(lax.dot_general, dimension_numbers=dims,
                             preferred_element_type=jnp.float32)
    return part(a_lo, b_hi) + part(a_hi, b_lo) + part(a_hi, b_hi)


def k_powers(f_ref, out_ref):
    power = f_ref[...]
    out_ref[0] = power
    for level in range(1, out_ref.shape[0]):
        power = _dot(power, power)
        out_ref[level] = power


def _scan(v, cut, pw_ref, seg, backward, carry=None, levels=None):
    rows, width = v.shape
    scen = rows // seg
    t = lax.broadcasted_iota(jnp.int32, (rows, width), 0) % seg
    flags = 1.0 - cut
    if levels is None:
        levels = seg.bit_length() - 1
    step = functools.partial(_mm, nt=not backward)
    if carry is not None:
        pushed = step(carry, pw_ref[0])
        pushed = jnp.broadcast_to(pushed[:, None, :], (scen, seg, width)).reshape(rows, width)
        first = t == (seg - 1 if backward else 0)
        v = v + jnp.where(first, flags * pushed, 0.0)
    for level in range(levels):
        stride = 2**level
        if backward:
            prior_v = pltpu.roll(v, rows - stride, 0)
            prior_f = pltpu.roll(flags, rows - stride, 0)
            valid = t < seg - stride
        else:
            prior_v = pltpu.roll(v, stride, 0)
            prior_f = pltpu.roll(flags, stride, 0)
            valid = t >= stride
        prior_v = jnp.where(valid, prior_v, 0.0)
        prior_f = jnp.where(valid, prior_f, 1.0)
        v = v + flags * step(prior_v, pw_ref[level])
        flags = flags * prior_f
    return v


def _carry(g_ref, fl_ref, pw_ref, scen, backward):
    width = pw_ref.shape[1]
    g = g_ref[...][:, :width]
    rows = g.shape[0]
    devices = rows // scen
    local_levels = pw_ref.shape[0] - max((devices - 1).bit_length(), 1)
    r = lax.broadcasted_iota(jnp.int32, (rows, width), 0)
    flags = jnp.broadcast_to(fl_ref[...], (rows, width))
    step = functools.partial(_mm, nt=not backward)
    for level in range((devices - 1).bit_length()):
        stride = scen * 2**level
        if backward:
            prior_g = pltpu.roll(g, rows - stride, 0)
            prior_f = pltpu.roll(flags, rows - stride, 0)
            valid = r < rows - stride
        else:
            prior_g = pltpu.roll(g, stride, 0)
            prior_f = pltpu.roll(flags, stride, 0)
            valid = r >= stride
        prior_g = jnp.where(valid, prior_g, 0.0)
        prior_f = jnp.where(valid, prior_f, 1.0)
        g = g + flags * step(prior_g, pw_ref[local_levels + level])
        flags = flags * prior_f
    me = lax.axis_index("tm")
    target = me + 1 if backward else me - 1
    pick = lax.broadcasted_iota(jnp.int32, (scen, rows), 1)
    want = lax.broadcasted_iota(jnp.int32, (scen, rows), 0) + target * scen
    return _dot((pick == want).astype(jnp.float32), g)


def _ends(v, seg, backward, out_rows):
    rows, width = v.shape
    scen = rows // seg
    pick = lax.broadcasted_iota(jnp.int32, (out_rows, rows), 1)
    want = lax.broadcasted_iota(jnp.int32, (out_rows, rows), 0) % scen * seg
    want = want + (0 if backward else seg - 1)
    return _dot((pick == want).astype(jnp.float32), v)


def _vmem(count):
    return [pl.BlockSpec(memory_space=pltpu.VMEM)] * count


def _call(kernel, outs, *args):
    return pl.pallas_call(
        kernel,
        out_shape=outs,
        in_specs=_vmem(len(args)),
        out_specs=tuple(_vmem(len(outs))),
    )(*args)


def k_first(seg, cw_ref, ref_ref, end_ref, pwb_ref, w1_ref, e1_ref):
    width = cw_ref.shape[1]
    cut = jnp.broadcast_to(end_ref[...], cw_ref.shape)
    w1 = cw_ref[...] * ref_ref[...]
    w1_ref[...] = w1
    e1_ref[...] = _ends(_scan(w1, cut, pwb_ref, seg, True), seg, True, e1_ref.shape[0])


def k_states_in(seg, w1_ref, end_ref, start_ref, c1_ref, fb_ref, init_ref, gain_ref, imap_ref, pwb_ref,
                pwf_ref, d2_ref, e2_ref):
    shape = w1_ref.shape
    cut_e = jnp.broadcast_to(end_ref[...], shape)
    cut_s = jnp.broadcast_to(start_ref[...], shape)
    c1 = _carry(c1_ref, fb_ref, pwb_ref, w1_ref.shape[0] // seg, True)
    vt = _scan(w1_ref[...], cut_e, pwb_ref, seg, True, c1)
    controls = _mm(vt, gain_ref[...], nt=True)
    forcing = -_mm(controls, imap_ref[...], nt=True)
    rows, width = shape
    scen = rows // seg
    init = jnp.broadcast_to(init_ref[...][:, None, :], (scen, seg, width)).reshape(rows, width)
    d2 = forcing + cut_s * init
    d2_ref[...] = d2
    e2_ref[...] = _ends(_scan(d2, cut_s, pwf_ref, seg, False), seg, False, e2_ref.shape[0])


def k_adjoint_in(seg, scale, d2_ref, start_ref, end_ref, c2_ref, ff_ref, cw_ref, ref_ref, pwf_ref, pwb_ref,
                 x_ref, w3_ref, e3_ref):
    shape = d2_ref.shape
    rows, width = shape
    scen = rows // seg
    cut_s = jnp.broadcast_to(start_ref[...], shape)
    cut_e = jnp.broadcast_to(end_ref[...], shape)
    c2 = _carry(c2_ref, ff_ref, pwf_ref, scen, False)
    states = _scan(d2_ref[...], cut_s, pwf_ref, seg, False, c2)
    x_ref[...] = states
    offset = states - ref_ref[...]
    cw = cw_ref[...]
    w3 = cw * offset
    w3_ref[...] = w3
    per_row = jnp.sum(w3 * offset, axis=1, keepdims=True)
    out_rows = e3_ref.shape[0]
    pick = lax.broadcasted_iota(jnp.int32, (out_rows, rows), 1) // seg
    want = lax.broadcasted_iota(jnp.int32, (out_rows, rows), 0) % scen
    sel = (pick == want).astype(jnp.float32)
    per_scen = _dot(sel, jnp.broadcast_to(per_row, (rows, 128)))
    e3_ref[:, width:] = per_scen * scale
    e3_ref[:, :width] = _ends(_scan(w3, cut_e, pwb_ref, seg, True), seg, True, out_rows)


def k_value_adjoint_in(seg, w3_ref, end_ref, start_ref, c3_ref, fb_ref, imap_ref, gain_ref, pwb_ref,
                       pwf_ref, s4_ref, e4_ref):
    shape = w3_ref.shape
    cut_e = jnp.broadcast_to(end_ref[...], shape)
    cut_s = jnp.broadcast_to(start_ref[...], shape)
    c3 = _carry(c3_ref, fb_ref, pwb_ref, w3_ref.shape[0] // seg, True)
    adjoint = _scan(w3_ref[...], cut_e, pwb_ref, seg, True, c3)
    pulled = _mm(adjoint, imap_ref[...])
    source = -_mm(pulled, gain_ref[...])
    s4_ref[...] = source
    e4_ref[...] = _ends(_scan(source, cut_s, pwf_ref, seg, False), seg, False, e4_ref.shape[0])


def k_last(seg, s4_ref, start_ref, c4_ref, ff_ref, x_ref, ref_ref, pwf_ref, g_ref):
    shape = s4_ref.shape
    cut_s = jnp.broadcast_to(start_ref[...], shape)
    c4 = _carry(c4_ref, ff_ref, pwf_ref, s4_ref.shape[0] // seg, False)
    va = _scan(s4_ref[...], cut_s, pwf_ref, seg, False, c4)
    ref = ref_ref[...]
    offset = x_ref[...] - ref
    g_ref[...] = 0.5 * offset * offset + ref * va


def combine(last_value, frame_starts, powers, backward, seg_steps, local_levels, device_levels,
            extra=None):
    scen_count, width = last_value.shape
    devices = lax.axis_size("tm")
    device = lax.axis_index("tm")
    frame_device = devices - 1 - device if backward else device
    if extra is None:
        all_values = lax.all_gather(last_value[None], "tm", axis=0, tiled=True)
        gathered_extra = None
    else:
        lanes = jnp.broadcast_to(extra[:, None], (scen_count, 128))
        packed = jnp.concatenate([last_value, lanes], axis=1)
        gathered = lax.all_gather(packed[None], "tm", axis=0, tiled=True)
        all_values = gathered[:, :, :width]
        gathered_extra = gathered[:, :, width]
    seg_lo = jnp.arange(devices, dtype=jnp.int32)[:, None, None] * seg_steps
    inside = (frame_starts[None] >= seg_lo) & (frame_starts[None] < seg_lo + seg_steps)
    all_flags = 1.0 - jnp.any(inside, axis=-1).astype(jnp.float32)
    if backward:
        all_values = all_values[::-1]
    roll_by = devices - frame_device
    all_values = jnp.roll(all_values, roll_by, axis=0)
    all_flags = jnp.roll(all_flags, roll_by, axis=0)
    keep = (jnp.arange(devices, dtype=jnp.int32) >= roll_by).astype(jnp.float32)
    all_values = all_values * keep[:, None, None]
    all_flags = all_flags * keep[:, None] + (1.0 - keep[:, None])
    for level in range(device_levels):
        half = all_values.shape[0] // 2
        paired_values = all_values.reshape(half, 2, scen_count, width)
        paired_flags = all_flags.reshape(half, 2, scen_count)
        power = powers[local_levels + level]
        moved = row_times(paired_values[:, 0], power if backward else power.T)
        all_values = paired_flags[:, 1, :, None] * moved + paired_values[:, 1]
        all_flags = paired_flags[:, 0] * paired_flags[:, 1]
    return all_values[0], gathered_extra


def per_device(ref_traj, cost_weights, x_init, decay, coupling, links, input_map, ff_gain, lengths):
    scen_count, seg_steps, width = ref_traj.shape
    rows = scen_count * seg_steps
    devices = lax.axis_size("tm")
    device = lax.axis_index("tm")
    total = seg_steps * devices
    dynamics = build_dynamics(decay, coupling, links)
    local_levels = seg_steps.bit_length() - 1
    device_levels = (devices - 1).bit_length()
    power_count = local_levels + max(device_levels, 1)
    (squares,) = _call(
        k_powers, (jax.ShapeDtypeStruct((power_count, width, width), jnp.float32),), dynamics)
    forward_powers = squares
    pwb = squares
    pwf = squares
    ends_incl = jnp.cumsum(lengths, axis=1)
    starts = ends_incl - lengths
    mirrored = total - ends_incl
    positions = device * seg_steps + jnp.arange(seg_steps, dtype=jnp.int32)
    start_flag = jnp.any(positions[None, :, None] == starts[:, None, :], axis=-1)
    end_flag = jnp.any(positions[None, :, None] + 1 == ends_incl[:, None, :], axis=-1)
    start_col = start_flag.astype(jnp.float32).reshape(rows, 1)
    end_col = end_flag.astype(jnp.float32).reshape(rows, 1)
    init_image = jnp.dot(x_init, dynamics.T, precision=HIGH)
    cw = cost_weights.reshape(rows, width)
    ref = ref_traj.reshape(rows, width)
    f32 = jnp.float32
    full = jax.ShapeDtypeStruct((rows, width), f32)
    ends = jax.ShapeDtypeStruct((devices * scen_count, width), f32)
    seg = seg_steps

    seg_lo = jnp.arange(devices, dtype=jnp.int32)[:, None, None] * seg_steps
    in_fwd = (starts[None] >= seg_lo) & (starts[None] < seg_lo + seg_steps)
    in_bwd = (ends_incl[None] > seg_lo) & (ends_incl[None] <= seg_lo + seg_steps)
    flat = (devices * scen_count, 1)
    ff = 1.0 - jnp.any(in_fwd, axis=-1).astype(f32).reshape(flat)
    fb = 1.0 - jnp.any(in_bwd, axis=-1).astype(f32).reshape(flat)

    def gather(copies):
        return lax.all_to_all(copies, "tm", 0, 0, tiled=True)

    w1, e1 = _call(functools.partial(k_first, seg), (full, ends), cw, ref, end_col, pwb)
    d2, e2 = _call(
        functools.partial(k_states_in, seg), (full, ends),
        w1, end_col, start_col, gather(e1), fb, init_image, ff_gain, input_map, pwb, pwf)
    packed = jax.ShapeDtypeStruct((devices * scen_count, width + 128), f32)
    states, w3, e3 = _call(
        functools.partial(k_adjoint_in, seg, 0.5 / total), (full, full, packed),
        d2, start_col, end_col, gather(e2), ff, cw, ref, pwf, pwb)
    g3 = gather(e3)
    cost = jnp.sum(g3[:, width].reshape(devices, scen_count), axis=0)
    s4, e4 = _call(
        functools.partial(k_value_adjoint_in, seg), (full, ends),
        w3, end_col, start_col, g3, fb, input_map, ff_gain, pwb, pwf)
    (grad,) = _call(
        functools.partial(k_last, seg), (full,), s4, start_col, gather(e4), ff, states, ref, pwf)
    shape3 = (scen_count, seg_steps, width)
    return (states.reshape(shape3), grad.reshape(shape3), cost)


def solution(mesh):
    placed = (
        P("groups", "tm", None),
        P("groups", "tm", None),
        P("groups", None),
        P(),
        P(),
        P(),
        P(),
        P(),
        P("groups", None),
    )
    return jax.shard_map(
        per_device,
        mesh=mesh,
        in_specs=placed,
        out_specs=(P("groups", "tm", None), P("groups", "tm", None), P("groups")),
        check_vma=False,
    )
```

```python
import functools

import jax
import jax.numpy as jnp
from jax import lax
from jax.experimental import pallas as pl
from jax.experimental.pallas import tpu as pltpu
from jax.sharding import PartitionSpec as P

HIGH = lax.Precision.HIGHEST


def build_dynamics(decay, coupling, links):
    size = decay.shape[0]
    width = coupling.shape[1]
    lanes = jnp.arange(size, dtype=jnp.int32)
    offsets = jnp.arange(width, dtype=jnp.int32)
    row_hot = (lanes[None, :, None] == links[:, 0:1, None] * width + offsets[None, None, :]).astype(
        jnp.float32
    )
    col_hot = (lanes[None, :, None] == links[:, 1:2, None] * width + offsets[None, None, :]).astype(
        jnp.float32
    )
    placed = jnp.einsum(
        "lia,lab,ljb->ij", row_hot, coupling, col_hot, precision=lax.Precision.HIGHEST
    )
    return jnp.diag(decay) + placed


def row_times(values, matrix):
    width = values.shape[-1]
    flat = jnp.dot(values.reshape(-1, width), matrix, precision=lax.Precision.HIGHEST)
    return flat.reshape(values.shape)


def _dot(a, b):
    return jnp.dot(a, b, precision=HIGH, preferred_element_type=jnp.float32)


def _dot_nt(a, b):
    return lax.dot_general(
        a, b, (((1,), (1,)), ((), ())), precision=HIGH, preferred_element_type=jnp.float32)


def _split(x):
    hi = x.astype(jnp.bfloat16)
    lo = (x - hi.astype(jnp.float32)).astype(jnp.bfloat16)
    return hi, lo


def _mm(a, b, nt=False):
    dims = (((1,), (1 if nt else 0,)), ((), ()))
    a_hi, a_lo = _split(a)
    b_hi, b_lo = _split(b)
    part = functools.partial(lax.dot_general, dimension_numbers=dims,
                             preferred_element_type=jnp.float32)
    return part(a_lo, b_hi) + part(a_hi, b_lo) + part(a_hi, b_hi)


def k_powers(f_ref, out_ref):
    power = f_ref[...]
    out_ref[0] = power
    for level in range(1, out_ref.shape[0]):
        power = _dot(power, power)
        out_ref[level] = power


def _scan(v, cut, pw_ref, seg, backward, carry=None, levels=None):
    rows, width = v.shape
    scen = rows // seg
    t = lax.broadcasted_iota(jnp.int32, (rows, width), 0) % seg
    flags = 1.0 - cut
    if levels is None:
        levels = seg.bit_length() - 1
    step = functools.partial(_mm, nt=not backward)
    if carry is not None:
        pushed = step(carry, pw_ref[0])
        pushed = jnp.broadcast_to(pushed[:, None, :], (scen, seg, width)).reshape(rows, width)
        first = t == (seg - 1 if backward else 0)
        v = v + jnp.where(first, flags * pushed, 0.0)
    for level in range(levels):
        stride = 2**level
        if backward:
            prior_v = pltpu.roll(v, rows - stride, 0)
            prior_f = pltpu.roll(flags, rows - stride, 0)
            valid = t < seg - stride
        else:
            prior_v = pltpu.roll(v, stride, 0)
            prior_f = pltpu.roll(flags, stride, 0)
            valid = t >= stride
        prior_v = jnp.where(valid, prior_v, 0.0)
        prior_f = jnp.where(valid, prior_f, 1.0)
        v = v + flags * step(prior_v, pw_ref[level])
        flags = flags * prior_f
    return v


def _carry(g_ref, fl_ref, pw_ref, scen, backward):
    width = pw_ref.shape[1]
    g = g_ref[...][:, :width]
    rows = g.shape[0]
    devices = rows // scen
    local_levels = pw_ref.shape[0] - max((devices - 1).bit_length(), 1)
    r = lax.broadcasted_iota(jnp.int32, (rows, width), 0)
    flags = jnp.broadcast_to(fl_ref[...], (rows, width))
    step = functools.partial(_mm, nt=not backward)
    for level in range((devices - 1).bit_length()):
        stride = scen * 2**level
        if backward:
            prior_g = pltpu.roll(g, rows - stride, 0)
            prior_f = pltpu.roll(flags, rows - stride, 0)
            valid = r < rows - stride
        else:
            prior_g = pltpu.roll(g, stride, 0)
            prior_f = pltpu.roll(flags, stride, 0)
            valid = r >= stride
        prior_g = jnp.where(valid, prior_g, 0.0)
        prior_f = jnp.where(valid, prior_f, 1.0)
        g = g + flags * step(prior_g, pw_ref[local_levels + level])
        flags = flags * prior_f
    me = lax.axis_index("tm")
    target = me + 1 if backward else me - 1
    pick = lax.broadcasted_iota(jnp.int32, (scen, rows), 1)
    want = lax.broadcasted_iota(jnp.int32, (scen, rows), 0) + target * scen
    return _dot((pick == want).astype(jnp.float32), g)


def _ends(v, seg, backward, out_rows):
    rows, width = v.shape
    scen = rows // seg
    pick = lax.broadcasted_iota(jnp.int32, (scen, rows), 1)
    want = lax.broadcasted_iota(jnp.int32, (scen, rows), 0) * seg + (0 if backward else seg - 1)
    ends = _dot((pick == want).astype(jnp.float32), v)
    return jnp.broadcast_to(ends[None], (out_rows,) + ends.shape)


def _vmem(count):
    return [pl.BlockSpec(memory_space=pltpu.VMEM)] * count


def _call(kernel, outs, *args):
    return pl.pallas_call(
        kernel,
        out_shape=outs,
        in_specs=_vmem(len(args)),
        out_specs=tuple(_vmem(len(outs))),
    )(*args)


def k_first(seg, cw_ref, ref_ref, end_ref, pwb_ref, w1_ref, e1_ref):
    width = cw_ref.shape[1]
    cut = jnp.broadcast_to(end_ref[...], cw_ref.shape)
    w1 = cw_ref[...] * ref_ref[...]
    w1_ref[...] = w1
    e1_ref[...] = _ends(_scan(w1, cut, pwb_ref, seg, True), seg, True, e1_ref.shape[0])


def k_states_in(seg, w1_ref, end_ref, start_ref, c1_ref, fb_ref, init_ref, gain_ref, imap_ref, pwb_ref,
                pwf_ref, d2_ref, e2_ref):
    shape = w1_ref.shape
    cut_e = jnp.broadcast_to(end_ref[...], shape)
    cut_s = jnp.broadcast_to(start_ref[...], shape)
    c1 = _carry(c1_ref, fb_ref, pwb_ref, w1_ref.shape[0] // seg, True)
    vt = _scan(w1_ref[...], cut_e, pwb_ref, seg, True, c1)
    controls = _mm(vt, gain_ref[...], nt=True)
    forcing = -_mm(controls, imap_ref[...], nt=True)
    rows, width = shape
    scen = rows // seg
    init = jnp.broadcast_to(init_ref[...][:, None, :], (scen, seg, width)).reshape(rows, width)
    d2 = forcing + cut_s * init
    d2_ref[...] = d2
    e2_ref[...] = _ends(_scan(d2, cut_s, pwf_ref, seg, False), seg, False, e2_ref.shape[0])


def k_adjoint_in(seg, scale, d2_ref, start_ref, end_ref, c2_ref, ff_ref, cw_ref, ref_ref, pwf_ref, pwb_ref,
                 x_ref, w3_ref, e3_ref):
    shape = d2_ref.shape
    rows, width = shape
    scen = rows // seg
    cut_s = jnp.broadcast_to(start_ref[...], shape)
    cut_e = jnp.broadcast_to(end_ref[...], shape)
    c2 = _carry(c2_ref, ff_ref, pwf_ref, scen, False)
    states = _scan(d2_ref[...], cut_s, pwf_ref, seg, False, c2)
    x_ref[...] = states
    offset = states - ref_ref[...]
    cw = cw_ref[...]
    w3 = cw * offset
    w3_ref[...] = w3
    per_row = jnp.sum(w3 * offset, axis=1, keepdims=True)
    copies = e3_ref.shape[0]
    pick = lax.broadcasted_iota(jnp.int32, (scen, rows), 1) // seg
    want = lax.broadcasted_iota(jnp.int32, (scen, rows), 0)
    sel = (pick == want).astype(jnp.float32)
    per_scen = _dot(sel, jnp.broadcast_to(per_row, (rows, 128))) * scale
    e3_ref[:, :, width:] = jnp.broadcast_to(per_scen[None], (copies, scen, 128))
    e3_ref[:, :, :width] = _ends(_scan(w3, cut_e, pwb_ref, seg, True), seg, True, copies)


def k_value_adjoint_in(seg, w3_ref, end_ref, start_ref, c3_ref, fb_ref, imap_ref, gain_ref, pwb_ref,
                       pwf_ref, s4_ref, e4_ref):
    shape = w3_ref.shape
    cut_e = jnp.broadcast_to(end_ref[...], shape)
    cut_s = jnp.broadcast_to(start_ref[...], shape)
    c3 = _carry(c3_ref, fb_ref, pwb_ref, w3_ref.shape[0] // seg, True)
    adjoint = _scan(w3_ref[...], cut_e, pwb_ref, seg, True, c3)
    pulled = _mm(adjoint, imap_ref[...])
    source = -_mm(pulled, gain_ref[...])
    s4_ref[...] = source
    e4_ref[...] = _ends(_scan(source, cut_s, pwf_ref, seg, False), seg, False, e4_ref.shape[0])


def k_last(seg, s4_ref, start_ref, c4_ref, ff_ref, x_ref, ref_ref, pwf_ref, g_ref):
    shape = s4_ref.shape
    cut_s = jnp.broadcast_to(start_ref[...], shape)
    c4 = _carry(c4_ref, ff_ref, pwf_ref, s4_ref.shape[0] // seg, False)
    va = _scan(s4_ref[...], cut_s, pwf_ref, seg, False, c4)
    ref = ref_ref[...]
    offset = x_ref[...] - ref
    g_ref[...] = 0.5 * offset * offset + ref * va


def combine(last_value, frame_starts, powers, backward, seg_steps, local_levels, device_levels,
            extra=None):
    scen_count, width = last_value.shape
    devices = lax.axis_size("tm")
    device = lax.axis_index("tm")
    frame_device = devices - 1 - device if backward else device
    if extra is None:
        all_values = lax.all_gather(last_value[None], "tm", axis=0, tiled=True)
        gathered_extra = None
    else:
        lanes = jnp.broadcast_to(extra[:, None], (scen_count, 128))
        packed = jnp.concatenate([last_value, lanes], axis=1)
        gathered = lax.all_gather(packed[None], "tm", axis=0, tiled=True)
        all_values = gathered[:, :, :width]
        gathered_extra = gathered[:, :, width]
    seg_lo = jnp.arange(devices, dtype=jnp.int32)[:, None, None] * seg_steps
    inside = (frame_starts[None] >= seg_lo) & (frame_starts[None] < seg_lo + seg_steps)
    all_flags = 1.0 - jnp.any(inside, axis=-1).astype(jnp.float32)
    if backward:
        all_values = all_values[::-1]
    roll_by = devices - frame_device
    all_values = jnp.roll(all_values, roll_by, axis=0)
    all_flags = jnp.roll(all_flags, roll_by, axis=0)
    keep = (jnp.arange(devices, dtype=jnp.int32) >= roll_by).astype(jnp.float32)
    all_values = all_values * keep[:, None, None]
    all_flags = all_flags * keep[:, None] + (1.0 - keep[:, None])
    for level in range(device_levels):
        half = all_values.shape[0] // 2
        paired_values = all_values.reshape(half, 2, scen_count, width)
        paired_flags = all_flags.reshape(half, 2, scen_count)
        power = powers[local_levels + level]
        moved = row_times(paired_values[:, 0], power if backward else power.T)
        all_values = paired_flags[:, 1, :, None] * moved + paired_values[:, 1]
        all_flags = paired_flags[:, 0] * paired_flags[:, 1]
    return all_values[0], gathered_extra


def per_device(ref_traj, cost_weights, x_init, decay, coupling, links, input_map, ff_gain, lengths):
    scen_count, seg_steps, width = ref_traj.shape
    rows = scen_count * seg_steps
    devices = lax.axis_size("tm")
    device = lax.axis_index("tm")
    total = seg_steps * devices
    dynamics = build_dynamics(decay, coupling, links)
    local_levels = seg_steps.bit_length() - 1
    device_levels = (devices - 1).bit_length()
    power_count = local_levels + max(device_levels, 1)
    (squares,) = _call(
        k_powers, (jax.ShapeDtypeStruct((power_count, width, width), jnp.float32),), dynamics)
    forward_powers = squares
    pwb = squares
    pwf = squares
    ends_incl = jnp.cumsum(lengths, axis=1)
    starts = ends_incl - lengths
    mirrored = total - ends_incl
    positions = device * seg_steps + jnp.arange(seg_steps, dtype=jnp.int32)
    start_flag = jnp.any(positions[None, :, None] == starts[:, None, :], axis=-1)
    end_flag = jnp.any(positions[None, :, None] + 1 == ends_incl[:, None, :], axis=-1)
    start_col = start_flag.astype(jnp.float32).reshape(rows, 1)
    end_col = end_flag.astype(jnp.float32).reshape(rows, 1)
    init_image = jnp.dot(x_init, dynamics.T, precision=HIGH)
    cw = cost_weights.reshape(rows, width)
    ref = ref_traj.reshape(rows, width)
    f32 = jnp.float32
    full = jax.ShapeDtypeStruct((rows, width), f32)
    ends = jax.ShapeDtypeStruct((devices, scen_count, width), f32)
    seg = seg_steps

    seg_lo = jnp.arange(devices, dtype=jnp.int32)[:, None, None] * seg_steps
    in_fwd = (starts[None] >= seg_lo) & (starts[None] < seg_lo + seg_steps)
    in_bwd = (ends_incl[None] > seg_lo) & (ends_incl[None] <= seg_lo + seg_steps)
    flat = (devices * scen_count, 1)
    ff = 1.0 - jnp.any(in_fwd, axis=-1).astype(f32).reshape(flat)
    fb = 1.0 - jnp.any(in_bwd, axis=-1).astype(f32).reshape(flat)

    def gather(copies):
        every = lax.all_to_all(copies, "tm", 0, 0, tiled=True)
        return every.reshape(devices * scen_count, copies.shape[2])

    w1, e1 = _call(functools.partial(k_first, seg), (full, ends), cw, ref, end_col, pwb)
    d2, e2 = _call(
        functools.partial(k_states_in, seg), (full, ends),
        w1, end_col, start_col, gather(e1), fb, init_image, ff_gain, input_map, pwb, pwf)
    packed = jax.ShapeDtypeStruct((devices, scen_count, width + 128), f32)
    states, w3, e3 = _call(
        functools.partial(k_adjoint_in, seg, 0.5 / total), (full, full, packed),
        d2, start_col, end_col, gather(e2), ff, cw, ref, pwf, pwb)
    g3 = gather(e3)
    cost = jnp.sum(g3[:, width].reshape(devices, scen_count), axis=0)
    s4, e4 = _call(
        functools.partial(k_value_adjoint_in, seg), (full, ends),
        w3, end_col, start_col, g3, fb, input_map, ff_gain, pwb, pwf)
    (grad,) = _call(
        functools.partial(k_last, seg), (full,), s4, start_col, gather(e4), ff, states, ref, pwf)
    shape3 = (scen_count, seg_steps, width)
    return (states.reshape(shape3), grad.reshape(shape3), cost)


def solution(mesh):
    placed = (
        P("groups", "tm", None),
        P("groups", "tm", None),
        P("groups", None),
        P(),
        P(),
        P(),
        P(),
        P(),
        P("groups", None),
    )
    return jax.shard_map(
        per_device,
        mesh=mesh,
        in_specs=placed,
        out_specs=(P("groups", "tm", None), P("groups", "tm", None), P("groups")),
        check_vma=False,
    )
```

```python
import functools

import jax
import jax.numpy as jnp
from jax import lax
from jax.experimental import pallas as pl
from jax.experimental.pallas import tpu as pltpu
from jax.sharding import PartitionSpec as P

HIGH = lax.Precision.HIGHEST


def build_dynamics(decay, coupling, links):
    size = decay.shape[0]
    width = coupling.shape[1]
    lanes = jnp.arange(size, dtype=jnp.int32)
    offsets = jnp.arange(width, dtype=jnp.int32)
    row_hot = (lanes[None, :, None] == links[:, 0:1, None] * width + offsets[None, None, :]).astype(
        jnp.float32
    )
    col_hot = (lanes[None, :, None] == links[:, 1:2, None] * width + offsets[None, None, :]).astype(
        jnp.float32
    )
    placed = jnp.einsum(
        "lia,lab,ljb->ij", row_hot, coupling, col_hot, precision=lax.Precision.HIGHEST
    )
    return jnp.diag(decay) + placed


def row_times(values, matrix):
    width = values.shape[-1]
    flat = jnp.dot(values.reshape(-1, width), matrix, precision=lax.Precision.HIGHEST)
    return flat.reshape(values.shape)


def _dot(a, b):
    return jnp.dot(a, b, precision=HIGH, preferred_element_type=jnp.float32)


def _dot_nt(a, b):
    return lax.dot_general(
        a, b, (((1,), (1,)), ((), ())), precision=HIGH, preferred_element_type=jnp.float32)


def _split(x):
    hi = x.astype(jnp.bfloat16)
    lo = (x - hi.astype(jnp.float32)).astype(jnp.bfloat16)
    return hi, lo


def _mm(a, b, nt=False):
    dims = (((1,), (1 if nt else 0,)), ((), ()))
    a_hi, a_lo = _split(a)
    b_hi, b_lo = _split(b)
    part = functools.partial(lax.dot_general, dimension_numbers=dims,
                             preferred_element_type=jnp.float32)
    return part(a_lo, b_hi) + part(a_hi, b_lo) + part(a_hi, b_hi)


def k_powers(square_first, f_ref, out_ref):
    power = f_ref[...]
    if square_first:
        power = _dot(power, power)
    out_ref[0] = power
    for level in range(1, out_ref.shape[0]):
        power = _dot(power, power)
        out_ref[level] = power


def _scan(v, cut, pw_ref, seg, backward, carry=None, levels=None):
    rows, width = v.shape
    scen = rows // seg
    t = lax.broadcasted_iota(jnp.int32, (rows, width), 0) % seg
    flags = 1.0 - cut
    if levels is None:
        levels = seg.bit_length() - 1
    step = functools.partial(_mm, nt=not backward)
    if carry is not None:
        pushed = step(carry, pw_ref[0])
        pushed = jnp.broadcast_to(pushed[:, None, :], (scen, seg, width)).reshape(rows, width)
        first = t == (seg - 1 if backward else 0)
        v = v + jnp.where(first, flags * pushed, 0.0)
    for level in range(levels):
        stride = 2**level
        if backward:
            prior_v = pltpu.roll(v, rows - stride, 0)
            prior_f = pltpu.roll(flags, rows - stride, 0)
            valid = t < seg - stride
        else:
            prior_v = pltpu.roll(v, stride, 0)
            prior_f = pltpu.roll(flags, stride, 0)
            valid = t >= stride
        prior_v = jnp.where(valid, prior_v, 0.0)
        prior_f = jnp.where(valid, prior_f, 1.0)
        v = v + flags * step(prior_v, pw_ref[level])
        flags = flags * prior_f
    return v


def _carry(g_ref, fl_ref, pd_ref, backward):
    devices, scen = g_ref.shape[0], g_ref.shape[1]
    width = pd_ref.shape[1]
    g = jnp.concatenate([g_ref[:, s, :width] for s in range(scen)], axis=0)
    rows = g.shape[0]
    j = lax.broadcasted_iota(jnp.int32, (rows, width), 0) % devices
    flags = jnp.broadcast_to(fl_ref[...], (rows, width))
    step = functools.partial(_mm, nt=not backward)
    for level in range((devices - 1).bit_length()):
        stride = 2**level
        if backward:
            prior_g = pltpu.roll(g, rows - stride, 0)
            prior_f = pltpu.roll(flags, rows - stride, 0)
            valid = j < devices - stride
        else:
            prior_g = pltpu.roll(g, stride, 0)
            prior_f = pltpu.roll(flags, stride, 0)
            valid = j >= stride
        prior_g = jnp.where(valid, prior_g, 0.0)
        prior_f = jnp.where(valid, prior_f, 1.0)
        g = g + flags * step(prior_g, pd_ref[level])
        flags = flags * prior_f
    me = lax.axis_index("tm")
    target = me + 1 if backward else me - 1
    pick = lax.broadcasted_iota(jnp.int32, (scen, rows), 1)
    want = lax.broadcasted_iota(jnp.int32, (scen, rows), 0) * devices + target
    hit = (pick == want) & (target >= 0) & (target < devices)
    return _dot(hit.astype(jnp.float32), g)


def _ends(v, seg, backward, out_rows):
    rows, width = v.shape
    scen = rows // seg
    pick = lax.broadcasted_iota(jnp.int32, (scen, rows), 1)
    want = lax.broadcasted_iota(jnp.int32, (scen, rows), 0) * seg + (0 if backward else seg - 1)
    ends = _dot((pick == want).astype(jnp.float32), v)
    return jnp.broadcast_to(ends[None], (out_rows,) + ends.shape)


def _vmem(count):
    return [pl.BlockSpec(memory_space=pltpu.VMEM)] * count


def _call(kernel, outs, *args):
    return pl.pallas_call(
        kernel,
        out_shape=outs,
        in_specs=_vmem(len(args)),
        out_specs=tuple(_vmem(len(outs))),
    )(*args)


def k_first(seg, cw_ref, ref_ref, end_ref, pwb_ref, w1_ref, e1_ref):
    width = cw_ref.shape[1]
    cut = jnp.broadcast_to(end_ref[...], cw_ref.shape)
    w1 = cw_ref[...] * ref_ref[...]
    w1_ref[...] = w1
    e1_ref[...] = _ends(_scan(w1, cut, pwb_ref, seg, True), seg, True, e1_ref.shape[0])


def k_states_in(seg, w1_ref, end_ref, start_ref, c1_ref, fb_ref, init_ref, gain_ref, imap_ref, pwb_ref,
                pwf_ref, pd_ref, d2_ref, e2_ref):
    shape = w1_ref.shape
    cut_e = jnp.broadcast_to(end_ref[...], shape)
    cut_s = jnp.broadcast_to(start_ref[...], shape)
    c1 = _carry(c1_ref, fb_ref, pd_ref, True)
    vt = _scan(w1_ref[...], cut_e, pwb_ref, seg, True, c1)
    controls = _mm(vt, gain_ref[...], nt=True)
    forcing = -_mm(controls, imap_ref[...], nt=True)
    rows, width = shape
    scen = rows // seg
    init = jnp.broadcast_to(init_ref[...][:, None, :], (scen, seg, width)).reshape(rows, width)
    d2 = forcing + cut_s * init
    d2_ref[...] = d2
    e2_ref[...] = _ends(_scan(d2, cut_s, pwf_ref, seg, False), seg, False, e2_ref.shape[0])


def k_adjoint_in(seg, scale, d2_ref, start_ref, end_ref, c2_ref, ff_ref, cw_ref, ref_ref, pwf_ref, pwb_ref,
                 pd_ref, x_ref, w3_ref, e3_ref):
    shape = d2_ref.shape
    rows, width = shape
    scen = rows // seg
    cut_s = jnp.broadcast_to(start_ref[...], shape)
    cut_e = jnp.broadcast_to(end_ref[...], shape)
    c2 = _carry(c2_ref, ff_ref, pd_ref, False)
    states = _scan(d2_ref[...], cut_s, pwf_ref, seg, False, c2)
    x_ref[...] = states
    offset = states - ref_ref[...]
    cw = cw_ref[...]
    w3 = cw * offset
    w3_ref[...] = w3
    per_row = jnp.sum(w3 * offset, axis=1, keepdims=True)
    copies = e3_ref.shape[0]
    pick = lax.broadcasted_iota(jnp.int32, (scen, rows), 1) // seg
    want = lax.broadcasted_iota(jnp.int32, (scen, rows), 0)
    sel = (pick == want).astype(jnp.float32)
    per_scen = _dot(sel, jnp.broadcast_to(per_row, (rows, 128))) * scale
    e3_ref[:, :, width:] = jnp.broadcast_to(per_scen[None], (copies, scen, 128))
    e3_ref[:, :, :width] = _ends(_scan(w3, cut_e, pwb_ref, seg, True), seg, True, copies)


def k_value_adjoint_in(seg, w3_ref, end_ref, start_ref, c3_ref, fb_ref, imap_ref, gain_ref, pwb_ref,
                       pwf_ref, pd_ref, s4_ref, e4_ref):
    shape = w3_ref.shape
    cut_e = jnp.broadcast_to(end_ref[...], shape)
    cut_s = jnp.broadcast_to(start_ref[...], shape)
    c3 = _carry(c3_ref, fb_ref, pd_ref, True)
    adjoint = _scan(w3_ref[...], cut_e, pwb_ref, seg, True, c3)
    pulled = _mm(adjoint, imap_ref[...])
    source = -_mm(pulled, gain_ref[...])
    s4_ref[...] = source
    e4_ref[...] = _ends(_scan(source, cut_s, pwf_ref, seg, False), seg, False, e4_ref.shape[0])


def k_last(seg, s4_ref, start_ref, c4_ref, ff_ref, x_ref, ref_ref, pwf_ref, pd_ref, g_ref):
    shape = s4_ref.shape
    cut_s = jnp.broadcast_to(start_ref[...], shape)
    c4 = _carry(c4_ref, ff_ref, pd_ref, False)
    va = _scan(s4_ref[...], cut_s, pwf_ref, seg, False, c4)
    ref = ref_ref[...]
    offset = x_ref[...] - ref
    g_ref[...] = 0.5 * offset * offset + ref * va


def combine(last_value, frame_starts, powers, backward, seg_steps, local_levels, device_levels,
            extra=None):
    scen_count, width = last_value.shape
    devices = lax.axis_size("tm")
    device = lax.axis_index("tm")
    frame_device = devices - 1 - device if backward else device
    if extra is None:
        all_values = lax.all_gather(last_value[None], "tm", axis=0, tiled=True)
        gathered_extra = None
    else:
        lanes = jnp.broadcast_to(extra[:, None], (scen_count, 128))
        packed = jnp.concatenate([last_value, lanes], axis=1)
        gathered = lax.all_gather(packed[None], "tm", axis=0, tiled=True)
        all_values = gathered[:, :, :width]
        gathered_extra = gathered[:, :, width]
    seg_lo = jnp.arange(devices, dtype=jnp.int32)[:, None, None] * seg_steps
    inside = (frame_starts[None] >= seg_lo) & (frame_starts[None] < seg_lo + seg_steps)
    all_flags = 1.0 - jnp.any(inside, axis=-1).astype(jnp.float32)
    if backward:
        all_values = all_values[::-1]
    roll_by = devices - frame_device
    all_values = jnp.roll(all_values, roll_by, axis=0)
    all_flags = jnp.roll(all_flags, roll_by, axis=0)
    keep = (jnp.arange(devices, dtype=jnp.int32) >= roll_by).astype(jnp.float32)
    all_values = all_values * keep[:, None, None]
    all_flags = all_flags * keep[:, None] + (1.0 - keep[:, None])
    for level in range(device_levels):
        half = all_values.shape[0] // 2
        paired_values = all_values.reshape(half, 2, scen_count, width)
        paired_flags = all_flags.reshape(half, 2, scen_count)
        power = powers[local_levels + level]
        moved = row_times(paired_values[:, 0], power if backward else power.T)
        all_values = paired_flags[:, 1, :, None] * moved + paired_values[:, 1]
        all_flags = paired_flags[:, 0] * paired_flags[:, 1]
    return all_values[0], gathered_extra


def per_device(ref_traj, cost_weights, x_init, decay, coupling, links, input_map, ff_gain, lengths):
    scen_count, seg_steps, width = ref_traj.shape
    rows = scen_count * seg_steps
    devices = lax.axis_size("tm")
    device = lax.axis_index("tm")
    total = seg_steps * devices
    dynamics = build_dynamics(decay, coupling, links)
    local_levels = seg_steps.bit_length() - 1
    device_levels = (devices - 1).bit_length()
    power_count = local_levels + max(device_levels, 1)
    (squares,) = _call(
        functools.partial(k_powers, False),
        (jax.ShapeDtypeStruct((local_levels, width, width), jnp.float32),), dynamics)
    (dev_powers,) = _call(
        functools.partial(k_powers, True),
        (jax.ShapeDtypeStruct((max(device_levels, 1), width, width), jnp.float32),),
        squares[local_levels - 1])
    forward_powers = squares
    pwb = squares
    pwf = squares
    ends_incl = jnp.cumsum(lengths, axis=1)
    starts = ends_incl - lengths
    mirrored = total - ends_incl
    positions = device * seg_steps + jnp.arange(seg_steps, dtype=jnp.int32)
    start_flag = jnp.any(positions[None, :, None] == starts[:, None, :], axis=-1)
    end_flag = jnp.any(positions[None, :, None] + 1 == ends_incl[:, None, :], axis=-1)
    start_col = start_flag.astype(jnp.float32).reshape(rows, 1)
    end_col = end_flag.astype(jnp.float32).reshape(rows, 1)
    init_image = jnp.dot(x_init, dynamics.T, precision=HIGH)
    cw = cost_weights.reshape(rows, width)
    ref = ref_traj.reshape(rows, width)
    f32 = jnp.float32
    full = jax.ShapeDtypeStruct((rows, width), f32)
    ends = jax.ShapeDtypeStruct((devices, scen_count, width), f32)
    seg = seg_steps

    seg_lo = jnp.arange(devices, dtype=jnp.int32)[:, None, None] * seg_steps
    in_fwd = (starts[None] >= seg_lo) & (starts[None] < seg_lo + seg_steps)
    in_bwd = (ends_incl[None] > seg_lo) & (ends_incl[None] <= seg_lo + seg_steps)
    flat = (devices * scen_count, 1)
    ff = 1.0 - jnp.any(in_fwd, axis=-1).astype(f32).T.reshape(flat)
    fb = 1.0 - jnp.any(in_bwd, axis=-1).astype(f32).T.reshape(flat)

    def gather(copies):
        return lax.all_to_all(copies, "tm", 0, 0, tiled=True)

    w1, e1 = _call(functools.partial(k_first, seg), (full, ends), cw, ref, end_col, pwb)
    d2, e2 = _call(
        functools.partial(k_states_in, seg), (full, ends),
        w1, end_col, start_col, gather(e1), fb, init_image, ff_gain, input_map, pwb, pwf, dev_powers)
    packed = jax.ShapeDtypeStruct((devices, scen_count, width + 128), f32)
    states, w3, e3 = _call(
        functools.partial(k_adjoint_in, seg, 0.5 / total), (full, full, packed),
        d2, start_col, end_col, gather(e2), ff, cw, ref, pwf, pwb, dev_powers)
    g3 = gather(e3)
    cost = jnp.sum(g3[:, :, width], axis=0)
    s4, e4 = _call(
        functools.partial(k_value_adjoint_in, seg), (full, ends),
        w3, end_col, start_col, g3, fb, input_map, ff_gain, pwb, pwf, dev_powers)
    (grad,) = _call(
        functools.partial(k_last, seg), (full,), s4, start_col, gather(e4), ff, states, ref, pwf, dev_powers)
    shape3 = (scen_count, seg_steps, width)
    return (states.reshape(shape3), grad.reshape(shape3), cost)


def solution(mesh):
    placed = (
        P("groups", "tm", None),
        P("groups", "tm", None),
        P("groups", None),
        P(),
        P(),
        P(),
        P(),
        P(),
        P("groups", None),
    )
    return jax.shard_map(
        per_device,
        mesh=mesh,
        in_specs=placed,
        out_specs=(P("groups", "tm", None), P("groups", "tm", None), P("groups")),
        check_vma=False,
    )
```

```python
import functools

import jax
import jax.numpy as jnp
from jax import lax
from jax.experimental import pallas as pl
from jax.experimental.pallas import tpu as pltpu
from jax.sharding import PartitionSpec as P

HIGH = lax.Precision.HIGHEST


def build_dynamics(decay, coupling, links):
    size = decay.shape[0]
    width = coupling.shape[1]
    lanes = jnp.arange(size, dtype=jnp.int32)
    offsets = jnp.arange(width, dtype=jnp.int32)
    row_hot = (lanes[None, :, None] == links[:, 0:1, None] * width + offsets[None, None, :]).astype(
        jnp.float32
    )
    col_hot = (lanes[None, :, None] == links[:, 1:2, None] * width + offsets[None, None, :]).astype(
        jnp.float32
    )
    placed = jnp.einsum(
        "lia,lab,ljb->ij", row_hot, coupling, col_hot, precision=lax.Precision.HIGHEST
    )
    return jnp.diag(decay) + placed


def row_times(values, matrix):
    width = values.shape[-1]
    flat = jnp.dot(values.reshape(-1, width), matrix, precision=lax.Precision.HIGHEST)
    return flat.reshape(values.shape)


def _dot(a, b):
    return jnp.dot(a, b, precision=HIGH, preferred_element_type=jnp.float32)


def _dot_nt(a, b):
    return lax.dot_general(
        a, b, (((1,), (1,)), ((), ())), precision=HIGH, preferred_element_type=jnp.float32)


def _split(x):
    hi = x.astype(jnp.bfloat16)
    lo = (x - hi.astype(jnp.float32)).astype(jnp.bfloat16)
    return hi, lo


def _mm(a, b, nt=False):
    dims = (((1,), (1 if nt else 0,)), ((), ()))
    a_hi, a_lo = _split(a)
    b_hi, b_lo = _split(b)
    part = functools.partial(lax.dot_general, dimension_numbers=dims,
                             preferred_element_type=jnp.float32)
    return part(a_lo, b_hi) + part(a_hi, b_lo) + part(a_hi, b_hi)


def k_powers(decay_ref, coupling_ref, links_ref, out_ref):
    size = decay_ref.shape[1]
    width = coupling_ref.shape[1]
    r = lax.broadcasted_iota(jnp.int32, (size, size), 0)
    c = lax.broadcasted_iota(jnp.int32, (size, size), 1)
    power = jnp.where(r == c, jnp.broadcast_to(decay_ref[...], (size, size)), 0.0)
    lane = lax.broadcasted_iota(jnp.int32, (size, width), 0)
    off = lax.broadcasted_iota(jnp.int32, (size, width), 1)
    for link in range(coupling_ref.shape[0]):
        row_hot = (lane == links_ref[link, 0] * width + off).astype(jnp.float32)
        col_hot = (lane == links_ref[link, 1] * width + off).astype(jnp.float32)
        power = power + _dot_nt(_dot(row_hot, coupling_ref[link]), col_hot)
    out_ref[0] = power
    for level in range(1, out_ref.shape[0]):
        power = _dot(power, power)
        out_ref[level] = power


def _scan(v, cut, pw_ref, seg, backward, carry=None, levels=None):
    rows, width = v.shape
    scen = rows // seg
    t = lax.broadcasted_iota(jnp.int32, (rows, width), 0) % seg
    flags = 1.0 - cut
    if levels is None:
        levels = seg.bit_length() - 1
    step = functools.partial(_mm, nt=not backward)
    if carry is not None:
        pushed = step(carry, pw_ref[0])
        pushed = jnp.broadcast_to(pushed[:, None, :], (scen, seg, width)).reshape(rows, width)
        first = t == (seg - 1 if backward else 0)
        v = v + jnp.where(first, flags * pushed, 0.0)
    for level in range(levels):
        stride = 2**level
        if backward:
            prior_v = pltpu.roll(v, rows - stride, 0)
            prior_f = pltpu.roll(flags, rows - stride, 0)
            valid = t < seg - stride
        else:
            prior_v = pltpu.roll(v, stride, 0)
            prior_f = pltpu.roll(flags, stride, 0)
            valid = t >= stride
        prior_v = jnp.where(valid, prior_v, 0.0)
        prior_f = jnp.where(valid, prior_f, 1.0)
        v = v + flags * step(prior_v, pw_ref[level])
        flags = flags * prior_f
    return v


def _carry(g_ref, len_ref, pw_ref, scen, backward, seg):
    width = pw_ref.shape[1]
    g = g_ref[...][:, :width]
    rows = g.shape[0]
    devices = rows // scen
    local_levels = pw_ref.shape[0] - max((devices - 1).bit_length(), 1)
    r = lax.broadcasted_iota(jnp.int32, (rows, width), 0)
    flags = jnp.broadcast_to(_seg_flags(len_ref, devices, seg, not backward), (rows, width))
    step = functools.partial(_mm, nt=not backward)
    for level in range((devices - 1).bit_length()):
        stride = scen * 2**level
        if backward:
            prior_g = pltpu.roll(g, rows - stride, 0)
            prior_f = pltpu.roll(flags, rows - stride, 0)
            valid = r < rows - stride
        else:
            prior_g = pltpu.roll(g, stride, 0)
            prior_f = pltpu.roll(flags, stride, 0)
            valid = r >= stride
        prior_g = jnp.where(valid, prior_g, 0.0)
        prior_f = jnp.where(valid, prior_f, 1.0)
        g = g + flags * step(prior_g, pw_ref[local_levels + level])
        flags = flags * prior_f
    me = lax.axis_index("tm")
    target = me + 1 if backward else me - 1
    pick = lax.broadcasted_iota(jnp.int32, (scen, rows), 1)
    want = lax.broadcasted_iota(jnp.int32, (scen, rows), 0) + target * scen
    return _dot((pick == want).astype(jnp.float32), g)


def _ends(v, seg, backward, out_rows):
    rows, width = v.shape
    scen = rows // seg
    pick = lax.broadcasted_iota(jnp.int32, (scen, rows), 1)
    want = lax.broadcasted_iota(jnp.int32, (scen, rows), 0) * seg + (0 if backward else seg - 1)
    ends = _dot((pick == want).astype(jnp.float32), v)
    return jnp.broadcast_to(ends[None], (out_rows,) + ends.shape)


def _cut_rows(len_ref, shape, seg, start):
    rows, width = shape
    scen, episodes = len_ref.shape
    r = lax.broadcasted_iota(jnp.int32, (rows, 1), 0)
    which = r // seg
    pos = lax.axis_index("tm") * seg + r % seg
    hit = jnp.zeros((rows, 1), jnp.bool_)
    for s in range(scen):
        edge = 0
        for k in range(episodes):
            first = edge
            edge = edge + len_ref[s, k]
            hit = hit | ((which == s) & (pos == first if start else pos + 1 == edge))
    return jnp.broadcast_to(hit.astype(jnp.float32), shape)


def _seg_flags(len_ref, devices, seg, start):
    scen, episodes = len_ref.shape
    rows = devices * scen
    r = lax.broadcasted_iota(jnp.int32, (rows, 1), 0)
    which = r % scen
    lo = r // scen * seg
    hit = jnp.zeros((rows, 1), jnp.bool_)
    for s in range(scen):
        edge = 0
        for k in range(episodes):
            first = edge
            edge = edge + len_ref[s, k]
            if start:
                inside = (first >= lo) & (first < lo + seg)
            else:
                inside = (edge > lo) & (edge <= lo + seg)
            hit = hit | ((which == s) & inside)
    return 1.0 - hit.astype(jnp.float32)


def _vmem(count):
    return [pl.BlockSpec(memory_space=pltpu.VMEM)] * count


def _call(kernel, outs, *args, smem=()):
    specs = _vmem(len(args))
    for index in smem:
        specs[index] = pl.BlockSpec(memory_space=pltpu.SMEM)
    return pl.pallas_call(
        kernel,
        out_shape=outs,
        in_specs=specs,
        out_specs=tuple(_vmem(len(outs))),
    )(*args)


def k_first(seg, cw_ref, ref_ref, len_ref, pwb_ref, w1_ref, e1_ref):
    cut = _cut_rows(len_ref, cw_ref.shape, seg, False)
    w1 = cw_ref[...] * ref_ref[...]
    w1_ref[...] = w1
    e1_ref[...] = _ends(_scan(w1, cut, pwb_ref, seg, True), seg, True, e1_ref.shape[0])


def k_states_in(seg, w1_ref, len_ref, c1_ref, xi_ref, gain_ref, imap_ref, pwb_ref,
                pwf_ref, d2_ref, e2_ref):
    shape = w1_ref.shape
    cut_e = _cut_rows(len_ref, shape, seg, False)
    cut_s = _cut_rows(len_ref, shape, seg, True)
    c1 = _carry(c1_ref, len_ref, pwb_ref, w1_ref.shape[0] // seg, True, seg)
    vt = _scan(w1_ref[...], cut_e, pwb_ref, seg, True, c1)
    controls = _mm(vt, gain_ref[...], nt=True)
    forcing = -_mm(controls, imap_ref[...], nt=True)
    rows, width = shape
    scen = rows // seg
    image = _dot_nt(xi_ref[...], pwf_ref[0])
    init = jnp.broadcast_to(image[:, None, :], (scen, seg, width)).reshape(rows, width)
    d2 = forcing + cut_s * init
    d2_ref[...] = d2
    e2_ref[...] = _ends(_scan(d2, cut_s, pwf_ref, seg, False), seg, False, e2_ref.shape[0])


def k_adjoint_in(seg, scale, d2_ref, len_ref, c2_ref, cw_ref, ref_ref, pwf_ref, pwb_ref,
                 x_ref, w3_ref, e3_ref):
    shape = d2_ref.shape
    rows, width = shape
    scen = rows // seg
    cut_s = _cut_rows(len_ref, shape, seg, True)
    cut_e = _cut_rows(len_ref, shape, seg, False)
    c2 = _carry(c2_ref, len_ref, pwf_ref, scen, False, seg)
    states = _scan(d2_ref[...], cut_s, pwf_ref, seg, False, c2)
    x_ref[...] = states
    offset = states - ref_ref[...]
    cw = cw_ref[...]
    w3 = cw * offset
    w3_ref[...] = w3
    per_row = jnp.sum(w3 * offset, axis=1, keepdims=True)
    copies = e3_ref.shape[0]
    pick = lax.broadcasted_iota(jnp.int32, (scen, rows), 1) // seg
    want = lax.broadcasted_iota(jnp.int32, (scen, rows), 0)
    sel = (pick == want).astype(jnp.float32)
    per_scen = _dot(sel, jnp.broadcast_to(per_row, (rows, 128))) * scale
    e3_ref[:, :, width:] = jnp.broadcast_to(per_scen[None], (copies, scen, 128))
    e3_ref[:, :, :width] = _ends(_scan(w3, cut_e, pwb_ref, seg, True), seg, True, copies)


def k_value_adjoint_in(seg, w3_ref, len_ref, c3_ref, imap_ref, gain_ref, pwb_ref,
                       pwf_ref, s4_ref, e4_ref):
    shape = w3_ref.shape
    cut_e = _cut_rows(len_ref, shape, seg, False)
    cut_s = _cut_rows(len_ref, shape, seg, True)
    c3 = _carry(c3_ref, len_ref, pwb_ref, w3_ref.shape[0] // seg, True, seg)
    adjoint = _scan(w3_ref[...], cut_e, pwb_ref, seg, True, c3)
    pulled = _mm(adjoint, imap_ref[...])
    source = -_mm(pulled, gain_ref[...])
    s4_ref[...] = source
    e4_ref[...] = _ends(_scan(source, cut_s, pwf_ref, seg, False), seg, False, e4_ref.shape[0])


def k_last(seg, s4_ref, len_ref, c4_ref, x_ref, ref_ref, pwf_ref, g_ref):
    shape = s4_ref.shape
    cut_s = _cut_rows(len_ref, shape, seg, True)
    c4 = _carry(c4_ref, len_ref, pwf_ref, s4_ref.shape[0] // seg, False, seg)
    va = _scan(s4_ref[...], cut_s, pwf_ref, seg, False, c4)
    ref = ref_ref[...]
    offset = x_ref[...] - ref
    g_ref[...] = 0.5 * offset * offset + ref * va


def per_device(ref_traj, cost_weights, x_init, decay, coupling, links, input_map, ff_gain, lengths):
    scen_count, seg_steps, width = ref_traj.shape
    rows = scen_count * seg_steps
    devices = lax.axis_size("tm")
    device = lax.axis_index("tm")
    total = seg_steps * devices
    local_levels = seg_steps.bit_length() - 1
    device_levels = (devices - 1).bit_length()
    power_count = local_levels + max(device_levels, 1)
    (squares,) = _call(
        k_powers, (jax.ShapeDtypeStruct((power_count, width, width), jnp.float32),),
        decay.reshape(1, width), coupling, links, smem=(2,))
    forward_powers = squares
    pwb = squares
    pwf = squares
    cw = cost_weights.reshape(rows, width)
    ref = ref_traj.reshape(rows, width)
    f32 = jnp.float32
    full = jax.ShapeDtypeStruct((rows, width), f32)
    ends = jax.ShapeDtypeStruct((devices, scen_count, width), f32)
    seg = seg_steps

    def gather(copies):
        every = lax.all_to_all(copies, "tm", 0, 0, tiled=True)
        return every.reshape(devices * scen_count, copies.shape[2])

    w1, e1 = _call(functools.partial(k_first, seg), (full, ends), cw, ref, lengths, pwb, smem=(2,))
    d2, e2 = _call(
        functools.partial(k_states_in, seg), (full, ends),
        w1, lengths, gather(e1), x_init, ff_gain, input_map, pwb, pwf, smem=(1,))
    packed = jax.ShapeDtypeStruct((devices, scen_count, width + 128), f32)
    states, w3, e3 = _call(
        functools.partial(k_adjoint_in, seg, 0.5 / total), (full, full, packed),
        d2, lengths, gather(e2), cw, ref, pwf, pwb, smem=(1,))
    g3 = gather(e3)
    cost = jnp.sum(g3[:, width].reshape(devices, scen_count), axis=0)
    s4, e4 = _call(
        functools.partial(k_value_adjoint_in, seg), (full, ends),
        w3, lengths, g3, input_map, ff_gain, pwb, pwf, smem=(1,))
    (grad,) = _call(
        functools.partial(k_last, seg), (full,), s4, lengths, gather(e4), states, ref, pwf,
        smem=(1,))
    shape3 = (scen_count, seg_steps, width)
    return (states.reshape(shape3), grad.reshape(shape3), cost)


def solution(mesh):
    placed = (
        P("groups", "tm", None),
        P("groups", "tm", None),
        P("groups", None),
        P(),
        P(),
        P(),
        P(),
        P(),
        P("groups", None),
    )
    return jax.shard_map(
        per_device,
        mesh=mesh,
        in_specs=placed,
        out_specs=(P("groups", "tm", None), P("groups", "tm", None), P("groups")),
        check_vma=False,
    )
```

```python
import functools

import jax
import jax.numpy as jnp
from jax import lax
from jax.experimental import pallas as pl
from jax.experimental.pallas import tpu as pltpu
from jax.sharding import PartitionSpec as P

HIGH = lax.Precision.HIGHEST


def build_dynamics(decay, coupling, links):
    size = decay.shape[0]
    width = coupling.shape[1]
    lanes = jnp.arange(size, dtype=jnp.int32)
    offsets = jnp.arange(width, dtype=jnp.int32)
    row_hot = (lanes[None, :, None] == links[:, 0:1, None] * width + offsets[None, None, :]).astype(
        jnp.float32
    )
    col_hot = (lanes[None, :, None] == links[:, 1:2, None] * width + offsets[None, None, :]).astype(
        jnp.float32
    )
    placed = jnp.einsum(
        "lia,lab,ljb->ij", row_hot, coupling, col_hot, precision=lax.Precision.HIGHEST
    )
    return jnp.diag(decay) + placed


def row_times(values, matrix):
    width = values.shape[-1]
    flat = jnp.dot(values.reshape(-1, width), matrix, precision=lax.Precision.HIGHEST)
    return flat.reshape(values.shape)


def _dot(a, b):
    return jnp.dot(a, b, precision=HIGH, preferred_element_type=jnp.float32)


def _dot_nt(a, b):
    return lax.dot_general(
        a, b, (((1,), (1,)), ((), ())), precision=HIGH, preferred_element_type=jnp.float32)


def _split(x):
    hi = x.astype(jnp.bfloat16)
    lo = (x - hi.astype(jnp.float32)).astype(jnp.bfloat16)
    return hi, lo


def _mm(a, b, nt=False):
    dims = (((1,), (1 if nt else 0,)), ((), ()))
    a_hi, a_lo = _split(a)
    b_hi, b_lo = _split(b)
    part = functools.partial(lax.dot_general, dimension_numbers=dims,
                             preferred_element_type=jnp.float32)
    return part(a_lo, b_hi) + part(a_hi, b_lo) + part(a_hi, b_hi)


def _build(decay_ref, coupling_ref, links_ref):
    size = decay_ref.shape[1]
    width = coupling_ref.shape[1]
    r = lax.broadcasted_iota(jnp.int32, (size, size), 0)
    c = lax.broadcasted_iota(jnp.int32, (size, size), 1)
    power = jnp.where(r == c, jnp.broadcast_to(decay_ref[...], (size, size)), 0.0)
    lane = lax.broadcasted_iota(jnp.int32, (size, width), 0)
    off = lax.broadcasted_iota(jnp.int32, (size, width), 1)
    for link in range(coupling_ref.shape[0]):
        row_hot = (lane == links_ref[0, link] * width + off).astype(jnp.float32)
        col_hot = (lane == links_ref[1, link] * width + off).astype(jnp.float32)
        power = power + _dot_nt(_dot(row_hot, coupling_ref[link]), col_hot)
    return power


def _scan(v, cut, pw_ref, seg, backward, carry=None, levels=None):
    rows, width = v.shape
    scen = rows // seg
    t = lax.broadcasted_iota(jnp.int32, (rows, width), 0) % seg
    flags = 1.0 - cut
    if levels is None:
        levels = seg.bit_length() - 1
    step = functools.partial(_mm, nt=not backward)
    if carry is not None:
        pushed = step(carry, pw_ref[0])
        pushed = jnp.broadcast_to(pushed[:, None, :], (scen, seg, width)).reshape(rows, width)
        first = t == (seg - 1 if backward else 0)
        v = v + jnp.where(first, flags * pushed, 0.0)
    for level in range(levels):
        stride = 2**level
        if backward:
            prior_v = pltpu.roll(v, rows - stride, 0)
            prior_f = pltpu.roll(flags, rows - stride, 0)
            valid = t < seg - stride
        else:
            prior_v = pltpu.roll(v, stride, 0)
            prior_f = pltpu.roll(flags, stride, 0)
            valid = t >= stride
        prior_v = jnp.where(valid, prior_v, 0.0)
        prior_f = jnp.where(valid, prior_f, 1.0)
        v = v + flags * step(prior_v, pw_ref[level])
        flags = flags * prior_f
    return v


def _carry(g_ref, len_ref, pw_ref, scen, backward, seg):
    width = pw_ref.shape[1]
    g = g_ref[...][:, :width]
    rows = g.shape[0]
    devices = rows // scen
    local_levels = pw_ref.shape[0] - max((devices - 1).bit_length(), 1)
    r = lax.broadcasted_iota(jnp.int32, (rows, width), 0)
    flags = jnp.broadcast_to(_seg_flags(len_ref, devices, seg, not backward), (rows, width))
    step = functools.partial(_mm, nt=not backward)
    for level in range((devices - 1).bit_length()):
        stride = scen * 2**level
        if backward:
            prior_g = pltpu.roll(g, rows - stride, 0)
            prior_f = pltpu.roll(flags, rows - stride, 0)
            valid = r < rows - stride
        else:
            prior_g = pltpu.roll(g, stride, 0)
            prior_f = pltpu.roll(flags, stride, 0)
            valid = r >= stride
        prior_g = jnp.where(valid, prior_g, 0.0)
        prior_f = jnp.where(valid, prior_f, 1.0)
        g = g + flags * step(prior_g, pw_ref[local_levels + level])
        flags = flags * prior_f
    me = lax.axis_index("tm")
    target = me + 1 if backward else me - 1
    pick = lax.broadcasted_iota(jnp.int32, (scen, rows), 1)
    want = lax.broadcasted_iota(jnp.int32, (scen, rows), 0) + target * scen
    return _dot((pick == want).astype(jnp.float32), g)


def _ends(v, seg, backward, out_rows):
    rows, width = v.shape
    scen = rows // seg
    pick = lax.broadcasted_iota(jnp.int32, (scen, rows), 1)
    want = lax.broadcasted_iota(jnp.int32, (scen, rows), 0) * seg + (0 if backward else seg - 1)
    ends = _dot((pick == want).astype(jnp.float32), v)
    return jnp.broadcast_to(ends[None], (out_rows,) + ends.shape)


def _cut_rows(len_ref, shape, seg, start):
    rows, width = shape
    scen, episodes = len_ref.shape
    r = lax.broadcasted_iota(jnp.int32, (rows, 1), 0)
    which = r // seg
    pos = lax.axis_index("tm") * seg + r % seg
    hit = jnp.zeros((rows, 1), jnp.bool_)
    for s in range(scen):
        edge = 0
        for k in range(episodes):
            first = edge
            edge = edge + len_ref[s, k]
            hit = hit | ((which == s) & (pos == first if start else pos + 1 == edge))
    return jnp.broadcast_to(hit.astype(jnp.float32), shape)


def _seg_flags(len_ref, devices, seg, start):
    scen, episodes = len_ref.shape
    rows = devices * scen
    r = lax.broadcasted_iota(jnp.int32, (rows, 1), 0)
    which = r % scen
    lo = r // scen * seg
    hit = jnp.zeros((rows, 1), jnp.bool_)
    for s in range(scen):
        edge = 0
        for k in range(episodes):
            first = edge
            edge = edge + len_ref[s, k]
            if start:
                inside = (first >= lo) & (first < lo + seg)
            else:
                inside = (edge > lo) & (edge <= lo + seg)
            hit = hit | ((which == s) & inside)
    return 1.0 - hit.astype(jnp.float32)


def _vmem(count):
    return [pl.BlockSpec(memory_space=pltpu.VMEM)] * count


def _call(kernel, outs, *args, smem=()):
    specs = _vmem(len(args))
    for index in smem:
        specs[index] = pl.BlockSpec(memory_space=pltpu.SMEM)
    return pl.pallas_call(
        kernel,
        out_shape=outs,
        in_specs=specs,
        out_specs=tuple(_vmem(len(outs))),
    )(*args)


def k_first(seg, decay_ref, coupling_ref, links_ref, cw_ref, ref_ref, len_ref, pwb_ref, w1_ref,
            e1_ref):
    local_levels = seg.bit_length() - 1
    power = _build(decay_ref, coupling_ref, links_ref)
    pwb_ref[0] = power
    for level in range(1, pwb_ref.shape[0]):
        if level == local_levels:
            cut = _cut_rows(len_ref, cw_ref.shape, seg, False)
            w1 = cw_ref[...] * ref_ref[...]
            w1_ref[...] = w1
            e1_ref[...] = _ends(_scan(w1, cut, pwb_ref, seg, True), seg, True, e1_ref.shape[0])
        power = _dot(power, power)
        pwb_ref[level] = power


def k_states_in(seg, w1_ref, len_ref, c1_ref, xi_ref, gain_ref, imap_ref, pwb_ref,
                pwf_ref, d2_ref, e2_ref):
    shape = w1_ref.shape
    cut_e = _cut_rows(len_ref, shape, seg, False)
    cut_s = _cut_rows(len_ref, shape, seg, True)
    c1 = _carry(c1_ref, len_ref, pwb_ref, w1_ref.shape[0] // seg, True, seg)
    vt = _scan(w1_ref[...], cut_e, pwb_ref, seg, True, c1)
    controls = _mm(vt, gain_ref[...], nt=True)
    forcing = -_mm(controls, imap_ref[...], nt=True)
    rows, width = shape
    scen = rows // seg
    image = _dot_nt(xi_ref[...], pwf_ref[0])
    init = jnp.broadcast_to(image[:, None, :], (scen, seg, width)).reshape(rows, width)
    d2 = forcing + cut_s * init
    d2_ref[...] = d2
    e2_ref[...] = _ends(_scan(d2, cut_s, pwf_ref, seg, False), seg, False, e2_ref.shape[0])


def k_adjoint_in(seg, scale, d2_ref, len_ref, c2_ref, cw_ref, ref_ref, pwf_ref, pwb_ref,
                 x_ref, w3_ref, e3_ref):
    shape = d2_ref.shape
    rows, width = shape
    scen = rows // seg
    cut_s = _cut_rows(len_ref, shape, seg, True)
    cut_e = _cut_rows(len_ref, shape, seg, False)
    c2 = _carry(c2_ref, len_ref, pwf_ref, scen, False, seg)
    states = _scan(d2_ref[...], cut_s, pwf_ref, seg, False, c2)
    x_ref[...] = states
    offset = states - ref_ref[...]
    cw = cw_ref[...]
    w3 = cw * offset
    w3_ref[...] = w3
    per_row = jnp.sum(w3 * offset, axis=1, keepdims=True)
    copies = e3_ref.shape[0]
    pick = lax.broadcasted_iota(jnp.int32, (scen, rows), 1) // seg
    want = lax.broadcasted_iota(jnp.int32, (scen, rows), 0)
    sel = (pick == want).astype(jnp.float32)
    per_scen = _dot(sel, jnp.broadcast_to(per_row, (rows, 128))) * scale
    e3_ref[:, :, width:] = jnp.broadcast_to(per_scen[None], (copies, scen, 128))
    e3_ref[:, :, :width] = _ends(_scan(w3, cut_e, pwb_ref, seg, True), seg, True, copies)


def k_value_adjoint_in(seg, w3_ref, len_ref, c3_ref, imap_ref, gain_ref, pwb_ref,
                       pwf_ref, s4_ref, e4_ref):
    shape = w3_ref.shape
    cut_e = _cut_rows(len_ref, shape, seg, False)
    cut_s = _cut_rows(len_ref, shape, seg, True)
    c3 = _carry(c3_ref, len_ref, pwb_ref, w3_ref.shape[0] // seg, True, seg)
    adjoint = _scan(w3_ref[...], cut_e, pwb_ref, seg, True, c3)
    pulled = _mm(adjoint, imap_ref[...])
    source = -_mm(pulled, gain_ref[...])
    s4_ref[...] = source
    e4_ref[...] = _ends(_scan(source, cut_s, pwf_ref, seg, False), seg, False, e4_ref.shape[0])


def k_last(seg, s4_ref, len_ref, c4_ref, x_ref, ref_ref, pwf_ref, g_ref):
    shape = s4_ref.shape
    cut_s = _cut_rows(len_ref, shape, seg, True)
    c4 = _carry(c4_ref, len_ref, pwf_ref, s4_ref.shape[0] // seg, False, seg)
    va = _scan(s4_ref[...], cut_s, pwf_ref, seg, False, c4)
    ref = ref_ref[...]
    offset = x_ref[...] - ref
    g_ref[...] = 0.5 * offset * offset + ref * va


def per_device(ref_traj, cost_weights, x_init, decay, coupling, links, input_map, ff_gain, lengths):
    scen_count, seg_steps, width = ref_traj.shape
    rows = scen_count * seg_steps
    devices = lax.axis_size("tm")
    device = lax.axis_index("tm")
    total = seg_steps * devices
    local_levels = seg_steps.bit_length() - 1
    device_levels = (devices - 1).bit_length()
    power_count = local_levels + max(device_levels, 1)
    cw = cost_weights.reshape(rows, width)
    ref = ref_traj.reshape(rows, width)
    f32 = jnp.float32
    full = jax.ShapeDtypeStruct((rows, width), f32)
    ends = jax.ShapeDtypeStruct((devices, scen_count, width), f32)
    seg = seg_steps

    def gather(copies):
        every = lax.all_to_all(copies, "tm", 0, 0, tiled=True)
        return every.reshape(devices * scen_count, copies.shape[2])

    powers = jax.ShapeDtypeStruct((power_count, width, width), f32)
    pwb, w1, e1 = _call(
        functools.partial(k_first, seg), (powers, full, ends),
        decay.reshape(1, width), coupling, links.T, cw, ref, lengths, smem=(2, 5))
    pwf = pwb
    d2, e2 = _call(
        functools.partial(k_states_in, seg), (full, ends),
        w1, lengths, gather(e1), x_init, ff_gain, input_map, pwb, pwf, smem=(1,))
    packed = jax.ShapeDtypeStruct((devices, scen_count, width + 128), f32)
    states, w3, e3 = _call(
        functools.partial(k_adjoint_in, seg, 0.5 / total), (full, full, packed),
        d2, lengths, gather(e2), cw, ref, pwf, pwb, smem=(1,))
    g3 = gather(e3)
    cost = jnp.sum(g3[:, width].reshape(devices, scen_count), axis=0)
    s4, e4 = _call(
        functools.partial(k_value_adjoint_in, seg), (full, ends),
        w3, lengths, g3, input_map, ff_gain, pwb, pwf, smem=(1,))
    (grad,) = _call(
        functools.partial(k_last, seg), (full,), s4, lengths, gather(e4), states, ref, pwf,
        smem=(1,))
    shape3 = (scen_count, seg_steps, width)
    return (states.reshape(shape3), grad.reshape(shape3), cost)


def solution(mesh):
    placed = (
        P("groups", "tm", None),
        P("groups", "tm", None),
        P("groups", None),
        P(),
        P(),
        P(),
        P(),
        P(),
        P("groups", None),
    )
    return jax.shard_map(
        per_device,
        mesh=mesh,
        in_specs=placed,
        out_specs=(P("groups", "tm", None), P("groups", "tm", None), P("groups")),
        check_vma=False,
    )
```

```python
import functools

import jax
import jax.numpy as jnp
from jax import lax
from jax.experimental import pallas as pl
from jax.experimental.pallas import tpu as pltpu
from jax.sharding import PartitionSpec as P

HIGH = lax.Precision.HIGHEST


def build_dynamics(decay, coupling, links):
    size = decay.shape[0]
    width = coupling.shape[1]
    lanes = jnp.arange(size, dtype=jnp.int32)
    offsets = jnp.arange(width, dtype=jnp.int32)
    row_hot = (lanes[None, :, None] == links[:, 0:1, None] * width + offsets[None, None, :]).astype(
        jnp.float32
    )
    col_hot = (lanes[None, :, None] == links[:, 1:2, None] * width + offsets[None, None, :]).astype(
        jnp.float32
    )
    placed = jnp.einsum(
        "lia,lab,ljb->ij", row_hot, coupling, col_hot, precision=lax.Precision.HIGHEST
    )
    return jnp.diag(decay) + placed


def row_times(values, matrix):
    width = values.shape[-1]
    flat = jnp.dot(values.reshape(-1, width), matrix, precision=lax.Precision.HIGHEST)
    return flat.reshape(values.shape)


def _dot(a, b):
    return jnp.dot(a, b, precision=HIGH, preferred_element_type=jnp.float32)


def _dot_nt(a, b):
    return lax.dot_general(
        a, b, (((1,), (1,)), ((), ())), precision=HIGH, preferred_element_type=jnp.float32)


def _split(x):
    hi = x.astype(jnp.bfloat16)
    lo = (x - hi.astype(jnp.float32)).astype(jnp.bfloat16)
    return hi, lo


def _mm(a, b, nt=False):
    dims = (((1,), (1 if nt else 0,)), ((), ()))
    a_hi, a_lo = _split(a)
    b_hi, b_lo = _split(b)
    part = functools.partial(lax.dot_general, dimension_numbers=dims,
                             preferred_element_type=jnp.float32)
    rows = a.shape[0]
    both = part(jnp.concatenate([a_hi, a_lo], axis=0), b_hi)
    return both[:rows] + both[rows:] + part(a_hi, b_lo)


def _build(decay_ref, coupling_ref, links_ref):
    size = decay_ref.shape[1]
    width = coupling_ref.shape[1]
    r = lax.broadcasted_iota(jnp.int32, (size, size), 0)
    c = lax.broadcasted_iota(jnp.int32, (size, size), 1)
    power = jnp.where(r == c, jnp.broadcast_to(decay_ref[...], (size, size)), 0.0)
    lane = lax.broadcasted_iota(jnp.int32, (size, width), 0)
    off = lax.broadcasted_iota(jnp.int32, (size, width), 1)
    for link in range(coupling_ref.shape[0]):
        row_hot = (lane == links_ref[0, link] * width + off).astype(jnp.float32)
        col_hot = (lane == links_ref[1, link] * width + off).astype(jnp.float32)
        power = power + _dot_nt(_dot(row_hot, coupling_ref[link]), col_hot)
    return power


def _scan(v, cut, pw_ref, seg, backward, carry=None, levels=None):
    rows, width = v.shape
    scen = rows // seg
    t = lax.broadcasted_iota(jnp.int32, (rows, width), 0) % seg
    flags = 1.0 - cut
    if levels is None:
        levels = seg.bit_length() - 1
    step = functools.partial(_mm, nt=not backward)
    if carry is not None:
        pushed = step(carry, pw_ref[0])
        pushed = jnp.broadcast_to(pushed[:, None, :], (scen, seg, width)).reshape(rows, width)
        first = t == (seg - 1 if backward else 0)
        v = v + jnp.where(first, flags * pushed, 0.0)
    for level in range(levels):
        stride = 2**level
        if backward:
            prior_v = pltpu.roll(v, rows - stride, 0)
            prior_f = pltpu.roll(flags, rows - stride, 0)
            valid = t < seg - stride
        else:
            prior_v = pltpu.roll(v, stride, 0)
            prior_f = pltpu.roll(flags, stride, 0)
            valid = t >= stride
        prior_v = jnp.where(valid, prior_v, 0.0)
        prior_f = jnp.where(valid, prior_f, 1.0)
        v = v + flags * step(prior_v, pw_ref[level])
        flags = flags * prior_f
    return v


def _carry(g_ref, len_ref, pw_ref, scen, backward, seg):
    width = pw_ref.shape[1]
    g = g_ref[...][:, :width]
    rows = g.shape[0]
    devices = rows // scen
    local_levels = pw_ref.shape[0] - max((devices - 1).bit_length(), 1)
    r = lax.broadcasted_iota(jnp.int32, (rows, width), 0)
    flags = jnp.broadcast_to(_seg_flags(len_ref, devices, seg, not backward), (rows, width))
    step = functools.partial(_mm, nt=not backward)
    for level in range((devices - 1).bit_length()):
        stride = scen * 2**level
        if backward:
            prior_g = pltpu.roll(g, rows - stride, 0)
            prior_f = pltpu.roll(flags, rows - stride, 0)
            valid = r < rows - stride
        else:
            prior_g = pltpu.roll(g, stride, 0)
            prior_f = pltpu.roll(flags, stride, 0)
            valid = r >= stride
        prior_g = jnp.where(valid, prior_g, 0.0)
        prior_f = jnp.where(valid, prior_f, 1.0)
        g = g + flags * step(prior_g, pw_ref[local_levels + level])
        flags = flags * prior_f
    me = lax.axis_index("tm")
    target = me + 1 if backward else me - 1
    pick = lax.broadcasted_iota(jnp.int32, (scen, rows), 1)
    want = lax.broadcasted_iota(jnp.int32, (scen, rows), 0) + target * scen
    return _dot((pick == want).astype(jnp.float32), g)


def _ends(v, seg, backward, out_rows):
    rows, width = v.shape
    scen = rows // seg
    pick = lax.broadcasted_iota(jnp.int32, (scen, rows), 1)
    want = lax.broadcasted_iota(jnp.int32, (scen, rows), 0) * seg + (0 if backward else seg - 1)
    ends = _dot((pick == want).astype(jnp.float32), v)
    return jnp.broadcast_to(ends[None], (out_rows,) + ends.shape)


def _cut_rows(len_ref, shape, seg, start):
    rows, width = shape
    scen, episodes = len_ref.shape
    r = lax.broadcasted_iota(jnp.int32, (rows, 1), 0)
    which = r // seg
    pos = lax.axis_index("tm") * seg + r % seg
    hit = jnp.zeros((rows, 1), jnp.bool_)
    for s in range(scen):
        edge = 0
        for k in range(episodes):
            first = edge
            edge = edge + len_ref[s, k]
            hit = hit | ((which == s) & (pos == first if start else pos + 1 == edge))
    return jnp.broadcast_to(hit.astype(jnp.float32), shape)


def _seg_flags(len_ref, devices, seg, start):
    scen, episodes = len_ref.shape
    rows = devices * scen
    r = lax.broadcasted_iota(jnp.int32, (rows, 1), 0)
    which = r % scen
    lo = r // scen * seg
    hit = jnp.zeros((rows, 1), jnp.bool_)
    for s in range(scen):
        edge = 0
        for k in range(episodes):
            first = edge
            edge = edge + len_ref[s, k]
            if start:
                inside = (first >= lo) & (first < lo + seg)
            else:
                inside = (edge > lo) & (edge <= lo + seg)
            hit = hit | ((which == s) & inside)
    return 1.0 - hit.astype(jnp.float32)


def _vmem(count):
    return [pl.BlockSpec(memory_space=pltpu.VMEM)] * count


def _call(kernel, outs, *args, smem=()):
    specs = _vmem(len(args))
    for index in smem:
        specs[index] = pl.BlockSpec(memory_space=pltpu.SMEM)
    return pl.pallas_call(
        kernel,
        out_shape=outs,
        in_specs=specs,
        out_specs=tuple(_vmem(len(outs))),
    )(*args)


def k_first(seg, decay_ref, coupling_ref, links_ref, cw_ref, ref_ref, len_ref, pwb_ref, w1_ref,
            e1_ref):
    local_levels = seg.bit_length() - 1
    power = _build(decay_ref, coupling_ref, links_ref)
    pwb_ref[0] = power
    for level in range(1, pwb_ref.shape[0]):
        if level == local_levels:
            cut = _cut_rows(len_ref, cw_ref.shape, seg, False)
            w1 = cw_ref[...] * ref_ref[...]
            w1_ref[...] = w1
            e1_ref[...] = _ends(_scan(w1, cut, pwb_ref, seg, True), seg, True, e1_ref.shape[0])
        power = _dot(power, power)
        pwb_ref[level] = power


def k_states_in(seg, w1_ref, len_ref, c1_ref, xi_ref, gain_ref, imap_ref, pwb_ref,
                pwf_ref, d2_ref, e2_ref):
    shape = w1_ref.shape
    cut_e = _cut_rows(len_ref, shape, seg, False)
    cut_s = _cut_rows(len_ref, shape, seg, True)
    c1 = _carry(c1_ref, len_ref, pwb_ref, w1_ref.shape[0] // seg, True, seg)
    vt = _scan(w1_ref[...], cut_e, pwb_ref, seg, True, c1)
    controls = _mm(vt, gain_ref[...], nt=True)
    forcing = -_mm(controls, imap_ref[...], nt=True)
    rows, width = shape
    scen = rows // seg
    image = _dot_nt(xi_ref[...], pwf_ref[0])
    init = jnp.broadcast_to(image[:, None, :], (scen, seg, width)).reshape(rows, width)
    d2 = forcing + cut_s * init
    d2_ref[...] = d2
    e2_ref[...] = _ends(_scan(d2, cut_s, pwf_ref, seg, False), seg, False, e2_ref.shape[0])


def k_adjoint_in(seg, scale, d2_ref, len_ref, c2_ref, cw_ref, ref_ref, pwf_ref, pwb_ref,
                 x_ref, w3_ref, e3_ref):
    shape = d2_ref.shape
    rows, width = shape
    scen = rows // seg
    cut_s = _cut_rows(len_ref, shape, seg, True)
    cut_e = _cut_rows(len_ref, shape, seg, False)
    c2 = _carry(c2_ref, len_ref, pwf_ref, scen, False, seg)
    states = _scan(d2_ref[...], cut_s, pwf_ref, seg, False, c2)
    x_ref[...] = states
    offset = states - ref_ref[...]
    cw = cw_ref[...]
    w3 = cw * offset
    w3_ref[...] = w3
    per_row = jnp.sum(w3 * offset, axis=1, keepdims=True)
    copies = e3_ref.shape[0]
    pick = lax.broadcasted_iota(jnp.int32, (scen, rows), 1) // seg
    want = lax.broadcasted_iota(jnp.int32, (scen, rows), 0)
    sel = (pick == want).astype(jnp.float32)
    per_scen = _dot(sel, jnp.broadcast_to(per_row, (rows, 128))) * scale
    e3_ref[:, :, width:] = jnp.broadcast_to(per_scen[None], (copies, scen, 128))
    e3_ref[:, :, :width] = _ends(_scan(w3, cut_e, pwb_ref, seg, True), seg, True, copies)


def k_value_adjoint_in(seg, w3_ref, len_ref, c3_ref, imap_ref, gain_ref, pwb_ref,
                       pwf_ref, s4_ref, e4_ref):
    shape = w3_ref.shape
    cut_e = _cut_rows(len_ref, shape, seg, False)
    cut_s = _cut_rows(len_ref, shape, seg, True)
    c3 = _carry(c3_ref, len_ref, pwb_ref, w3_ref.shape[0] // seg, True, seg)
    adjoint = _scan(w3_ref[...], cut_e, pwb_ref, seg, True, c3)
    pulled = _mm(adjoint, imap_ref[...])
    source = -_mm(pulled, gain_ref[...])
    s4_ref[...] = source
    e4_ref[...] = _ends(_scan(source, cut_s, pwf_ref, seg, False), seg, False, e4_ref.shape[0])


def k_last(seg, s4_ref, len_ref, c4_ref, x_ref, ref_ref, pwf_ref, g_ref):
    shape = s4_ref.shape
    cut_s = _cut_rows(len_ref, shape, seg, True)
    c4 = _carry(c4_ref, len_ref, pwf_ref, s4_ref.shape[0] // seg, False, seg)
    va = _scan(s4_ref[...], cut_s, pwf_ref, seg, False, c4)
    ref = ref_ref[...]
    offset = x_ref[...] - ref
    g_ref[...] = 0.5 * offset * offset + ref * va


def per_device(ref_traj, cost_weights, x_init, decay, coupling, links, input_map, ff_gain, lengths):
    scen_count, seg_steps, width = ref_traj.shape
    rows = scen_count * seg_steps
    devices = lax.axis_size("tm")
    device = lax.axis_index("tm")
    total = seg_steps * devices
    local_levels = seg_steps.bit_length() - 1
    device_levels = (devices - 1).bit_length()
    power_count = local_levels + max(device_levels, 1)
    cw = cost_weights.reshape(rows, width)
    ref = ref_traj.reshape(rows, width)
    f32 = jnp.float32
    full = jax.ShapeDtypeStruct((rows, width), f32)
    ends = jax.ShapeDtypeStruct((devices, scen_count, width), f32)
    seg = seg_steps

    def gather(copies):
        every = lax.all_to_all(copies, "tm", 0, 0, tiled=True)
        return every.reshape(devices * scen_count, copies.shape[2])

    powers = jax.ShapeDtypeStruct((power_count, width, width), f32)
    pwb, w1, e1 = _call(
        functools.partial(k_first, seg), (powers, full, ends),
        decay.reshape(1, width), coupling, links.T, cw, ref, lengths, smem=(2, 5))
    pwf = pwb
    d2, e2 = _call(
        functools.partial(k_states_in, seg), (full, ends),
        w1, lengths, gather(e1), x_init, ff_gain, input_map, pwb, pwf, smem=(1,))
    packed = jax.ShapeDtypeStruct((devices, scen_count, width + 128), f32)
    states, w3, e3 = _call(
        functools.partial(k_adjoint_in, seg, 0.5 / total), (full, full, packed),
        d2, lengths, gather(e2), cw, ref, pwf, pwb, smem=(1,))
    g3 = gather(e3)
    cost = jnp.sum(g3[:, width].reshape(devices, scen_count), axis=0)
    s4, e4 = _call(
        functools.partial(k_value_adjoint_in, seg), (full, ends),
        w3, lengths, g3, input_map, ff_gain, pwb, pwf, smem=(1,))
    (grad,) = _call(
        functools.partial(k_last, seg), (full,), s4, lengths, gather(e4), states, ref, pwf,
        smem=(1,))
    shape3 = (scen_count, seg_steps, width)
    return (states.reshape(shape3), grad.reshape(shape3), cost)


def solution(mesh):
    placed = (
        P("groups", "tm", None),
        P("groups", "tm", None),
        P("groups", None),
        P(),
        P(),
        P(),
        P(),
        P(),
        P("groups", None),
    )
    return jax.shard_map(
        per_device,
        mesh=mesh,
        in_specs=placed,
        out_specs=(P("groups", "tm", None), P("groups", "tm", None), P("groups")),
        check_vma=False,
    )
```

```python
import functools

import jax
import jax.numpy as jnp
from jax import lax
from jax.experimental import pallas as pl
from jax.experimental.pallas import tpu as pltpu
from jax.sharding import PartitionSpec as P

HIGH = lax.Precision.HIGHEST


def build_dynamics(decay, coupling, links):
    size = decay.shape[0]
    width = coupling.shape[1]
    lanes = jnp.arange(size, dtype=jnp.int32)
    offsets = jnp.arange(width, dtype=jnp.int32)
    row_hot = (lanes[None, :, None] == links[:, 0:1, None] * width + offsets[None, None, :]).astype(
        jnp.float32
    )
    col_hot = (lanes[None, :, None] == links[:, 1:2, None] * width + offsets[None, None, :]).astype(
        jnp.float32
    )
    placed = jnp.einsum(
        "lia,lab,ljb->ij", row_hot, coupling, col_hot, precision=lax.Precision.HIGHEST
    )
    return jnp.diag(decay) + placed


def row_times(values, matrix):
    width = values.shape[-1]
    flat = jnp.dot(values.reshape(-1, width), matrix, precision=lax.Precision.HIGHEST)
    return flat.reshape(values.shape)


def _dot(a, b):
    return jnp.dot(a, b, precision=HIGH, preferred_element_type=jnp.float32)


def _dot_nt(a, b):
    return lax.dot_general(
        a, b, (((1,), (1,)), ((), ())), precision=HIGH, preferred_element_type=jnp.float32)


def _split(x):
    hi = x.astype(jnp.bfloat16)
    lo = (x - hi.astype(jnp.float32)).astype(jnp.bfloat16)
    return hi, lo


def _mm(a, b, nt=False):
    dims = (((1,), (1 if nt else 0,)), ((), ()))
    a_hi, a_lo = _split(a)
    b_hi, b_lo = _split(b)
    part = functools.partial(lax.dot_general, dimension_numbers=dims,
                             preferred_element_type=jnp.float32)
    rows = a.shape[0]
    both = part(jnp.concatenate([a_hi, a_lo], axis=0), b_hi)
    return both[:rows] + both[rows:] + part(a_hi, b_lo)


def _build(decay_ref, coupling_ref, links_ref):
    size = decay_ref.shape[1]
    width = coupling_ref.shape[1]
    r = lax.broadcasted_iota(jnp.int32, (size, size), 0)
    c = lax.broadcasted_iota(jnp.int32, (size, size), 1)
    power = jnp.where(r == c, jnp.broadcast_to(decay_ref[...], (size, size)), 0.0)
    lane = lax.broadcasted_iota(jnp.int32, (size, width), 0)
    off = lax.broadcasted_iota(jnp.int32, (size, width), 1)
    for link in range(coupling_ref.shape[0]):
        row_hot = (lane == links_ref[0, link] * width + off).astype(jnp.float32)
        col_hot = (lane == links_ref[1, link] * width + off).astype(jnp.float32)
        power = power + _dot_nt(_dot(row_hot, coupling_ref[link]), col_hot)
    return power


def _scan(v, cut, pw_ref, seg, backward, carry=None, levels=None):
    rows, width = v.shape
    scen = rows // seg
    t = lax.broadcasted_iota(jnp.int32, (rows, width), 0) % seg
    flags = 1.0 - cut
    if levels is None:
        levels = seg.bit_length() - 1
    step = functools.partial(_mm, nt=not backward)
    if carry is not None:
        pushed = step(carry, pw_ref[0])
        pushed = jnp.broadcast_to(pushed[:, None, :], (scen, seg, width)).reshape(rows, width)
        first = t == (seg - 1 if backward else 0)
        v = v + jnp.where(first, flags * pushed, 0.0)
    for level in range(levels):
        stride = 2**level
        if backward:
            prior_v = pltpu.roll(v, rows - stride, 0)
            prior_f = pltpu.roll(flags, rows - stride, 0)
            valid = t < seg - stride
        else:
            prior_v = pltpu.roll(v, stride, 0)
            prior_f = pltpu.roll(flags, stride, 0)
            valid = t >= stride
        prior_v = jnp.where(valid, prior_v, 0.0)
        prior_f = jnp.where(valid, prior_f, 1.0)
        v = v + flags * step(prior_v, pw_ref[level])
        flags = flags * prior_f
    return v


def _carry(g_ref, len_ref, pw_ref, scen, backward, seg):
    width = pw_ref.shape[1]
    g = g_ref[...][:, :width]
    rows = g.shape[0]
    devices = rows // scen
    local_levels = pw_ref.shape[0] - max((devices - 1).bit_length(), 1)
    r = lax.broadcasted_iota(jnp.int32, (rows, width), 0)
    flags = jnp.broadcast_to(_seg_flags(len_ref, devices, seg, not backward), (rows, width))
    step = functools.partial(_mm, nt=not backward)
    for level in range((devices - 1).bit_length()):
        stride = scen * 2**level
        if backward:
            prior_g = pltpu.roll(g, rows - stride, 0)
            prior_f = pltpu.roll(flags, rows - stride, 0)
            valid = r < rows - stride
        else:
            prior_g = pltpu.roll(g, stride, 0)
            prior_f = pltpu.roll(flags, stride, 0)
            valid = r >= stride
        prior_g = jnp.where(valid, prior_g, 0.0)
        prior_f = jnp.where(valid, prior_f, 1.0)
        g = g + flags * step(prior_g, pw_ref[local_levels + level])
        flags = flags * prior_f
    me = lax.axis_index("tm")
    target = me + 1 if backward else me - 1
    pick = lax.broadcasted_iota(jnp.int32, (scen, rows), 1)
    want = lax.broadcasted_iota(jnp.int32, (scen, rows), 0) + target * scen
    return _dot((pick == want).astype(jnp.float32), g)


def _ends(v, seg, backward, out_rows):
    rows, width = v.shape
    scen = rows // seg
    pick = lax.broadcasted_iota(jnp.int32, (scen, rows), 1)
    want = lax.broadcasted_iota(jnp.int32, (scen, rows), 0) * seg + (0 if backward else seg - 1)
    ends = _dot((pick == want).astype(jnp.float32), v)
    return jnp.broadcast_to(ends[None], (out_rows,) + ends.shape)


def _cut_rows(len_ref, shape, seg, start):
    rows, width = shape
    scen, episodes = len_ref.shape
    r = lax.broadcasted_iota(jnp.int32, (rows, 1), 0)
    which = r // seg
    pos = lax.axis_index("tm") * seg + r % seg
    hit = jnp.zeros((rows, 1), jnp.bool_)
    for s in range(scen):
        edge = 0
        for k in range(episodes):
            first = edge
            edge = edge + len_ref[s, k]
            hit = hit | ((which == s) & (pos == first if start else pos + 1 == edge))
    return jnp.broadcast_to(hit.astype(jnp.float32), shape)


def _seg_flags(len_ref, devices, seg, start):
    scen, episodes = len_ref.shape
    rows = devices * scen
    r = lax.broadcasted_iota(jnp.int32, (rows, 1), 0)
    which = r % scen
    lo = r // scen * seg
    hit = jnp.zeros((rows, 1), jnp.bool_)
    for s in range(scen):
        edge = 0
        for k in range(episodes):
            first = edge
            edge = edge + len_ref[s, k]
            if start:
                inside = (first >= lo) & (first < lo + seg)
            else:
                inside = (edge > lo) & (edge <= lo + seg)
            hit = hit | ((which == s) & inside)
    return 1.0 - hit.astype(jnp.float32)


def _vmem(count):
    return [pl.BlockSpec(memory_space=pltpu.VMEM)] * count


def _call(kernel, outs, *args, smem=()):
    specs = _vmem(len(args))
    for index in smem:
        specs[index] = pl.BlockSpec(memory_space=pltpu.SMEM)
    return pl.pallas_call(
        kernel,
        out_shape=outs,
        in_specs=specs,
        out_specs=tuple(_vmem(len(outs))),
    )(*args)


def k_first(seg, decay_ref, coupling_ref, links_ref, cw_ref, ref_ref, len_ref, pwb_ref, w1_ref,
            e1_ref):
    local_levels = seg.bit_length() - 1
    power = _build(decay_ref, coupling_ref, links_ref)
    pwb_ref[0] = power
    for level in range(1, pwb_ref.shape[0]):
        if level == local_levels:
            cut = _cut_rows(len_ref, cw_ref.shape, seg, False)
            w1 = cw_ref[...] * ref_ref[...]
            w1_ref[...] = w1
            e1_ref[...] = _ends(_scan(w1, cut, pwb_ref, seg, True), seg, True, e1_ref.shape[0])
        power = _dot(power, power)
        pwb_ref[level] = power


def k_states_in(seg, w1_ref, len_ref, c1_ref, xi_ref, gain_ref, imap_ref, pwb_ref, d2_ref, e2_ref):
    pwf_ref = pwb_ref
    shape = w1_ref.shape
    cut_e = _cut_rows(len_ref, shape, seg, False)
    cut_s = _cut_rows(len_ref, shape, seg, True)
    c1 = _carry(c1_ref, len_ref, pwb_ref, w1_ref.shape[0] // seg, True, seg)
    vt = _scan(w1_ref[...], cut_e, pwb_ref, seg, True, c1)
    controls = _mm(vt, gain_ref[...], nt=True)
    forcing = -_mm(controls, imap_ref[...], nt=True)
    rows, width = shape
    scen = rows // seg
    image = _dot_nt(xi_ref[...], pwf_ref[0])
    init = jnp.broadcast_to(image[:, None, :], (scen, seg, width)).reshape(rows, width)
    d2 = forcing + cut_s * init
    d2_ref[...] = d2
    e2_ref[...] = _ends(_scan(d2, cut_s, pwf_ref, seg, False), seg, False, e2_ref.shape[0])


def k_adjoint_in(seg, scale, d2_ref, len_ref, c2_ref, cw_ref, ref_ref, pwf_ref, x_ref, w3_ref,
                 e3_ref):
    pwb_ref = pwf_ref
    shape = d2_ref.shape
    rows, width = shape
    scen = rows // seg
    cut_s = _cut_rows(len_ref, shape, seg, True)
    cut_e = _cut_rows(len_ref, shape, seg, False)
    c2 = _carry(c2_ref, len_ref, pwf_ref, scen, False, seg)
    states = _scan(d2_ref[...], cut_s, pwf_ref, seg, False, c2)
    x_ref[...] = states
    offset = states - ref_ref[...]
    cw = cw_ref[...]
    w3 = cw * offset
    w3_ref[...] = w3
    per_row = jnp.sum(w3 * offset, axis=1, keepdims=True)
    copies = e3_ref.shape[0]
    pick = lax.broadcasted_iota(jnp.int32, (scen, rows), 1) // seg
    want = lax.broadcasted_iota(jnp.int32, (scen, rows), 0)
    sel = (pick == want).astype(jnp.float32)
    per_scen = _dot(sel, jnp.broadcast_to(per_row, (rows, 128))) * scale
    e3_ref[:, :, width:] = jnp.broadcast_to(per_scen[None], (copies, scen, 128))
    e3_ref[:, :, :width] = _ends(_scan(w3, cut_e, pwb_ref, seg, True), seg, True, copies)


def k_value_adjoint_in(seg, w3_ref, len_ref, c3_ref, imap_ref, gain_ref, pwb_ref, s4_ref, e4_ref):
    pwf_ref = pwb_ref
    shape = w3_ref.shape
    cut_e = _cut_rows(len_ref, shape, seg, False)
    cut_s = _cut_rows(len_ref, shape, seg, True)
    c3 = _carry(c3_ref, len_ref, pwb_ref, w3_ref.shape[0] // seg, True, seg)
    adjoint = _scan(w3_ref[...], cut_e, pwb_ref, seg, True, c3)
    pulled = _mm(adjoint, imap_ref[...])
    source = -_mm(pulled, gain_ref[...])
    s4_ref[...] = source
    e4_ref[...] = _ends(_scan(source, cut_s, pwf_ref, seg, False), seg, False, e4_ref.shape[0])


def k_last(seg, s4_ref, len_ref, c4_ref, x_ref, ref_ref, pwf_ref, g_ref):
    shape = s4_ref.shape
    cut_s = _cut_rows(len_ref, shape, seg, True)
    c4 = _carry(c4_ref, len_ref, pwf_ref, s4_ref.shape[0] // seg, False, seg)
    va = _scan(s4_ref[...], cut_s, pwf_ref, seg, False, c4)
    ref = ref_ref[...]
    offset = x_ref[...] - ref
    g_ref[...] = 0.5 * offset * offset + ref * va


def per_device(ref_traj, cost_weights, x_init, decay, coupling, links, input_map, ff_gain, lengths):
    scen_count, seg_steps, width = ref_traj.shape
    rows = scen_count * seg_steps
    devices = lax.axis_size("tm")
    device = lax.axis_index("tm")
    total = seg_steps * devices
    local_levels = seg_steps.bit_length() - 1
    device_levels = (devices - 1).bit_length()
    power_count = local_levels + max(device_levels, 1)
    cw = cost_weights.reshape(rows, width)
    ref = ref_traj.reshape(rows, width)
    f32 = jnp.float32
    full = jax.ShapeDtypeStruct((rows, width), f32)
    ends = jax.ShapeDtypeStruct((devices, scen_count, width), f32)
    seg = seg_steps

    def gather(copies):
        every = lax.all_to_all(copies, "tm", 0, 0, tiled=True)
        return every.reshape(devices * scen_count, copies.shape[2])

    powers = jax.ShapeDtypeStruct((power_count, width, width), f32)
    pwb, w1, e1 = _call(
        functools.partial(k_first, seg), (powers, full, ends),
        decay.reshape(1, width), coupling, links.T, cw, ref, lengths, smem=(2, 5))
    pwf = pwb
    d2, e2 = _call(
        functools.partial(k_states_in, seg), (full, ends),
        w1, lengths, gather(e1), x_init, ff_gain, input_map, pwb, smem=(1,))
    packed = jax.ShapeDtypeStruct((devices, scen_count, width + 128), f32)
    states, w3, e3 = _call(
        functools.partial(k_adjoint_in, seg, 0.5 / total), (full, full, packed),
        d2, lengths, gather(e2), cw, ref, pwf, smem=(1,))
    g3 = gather(e3)
    cost = jnp.sum(g3[:, width].reshape(devices, scen_count), axis=0)
    s4, e4 = _call(
        functools.partial(k_value_adjoint_in, seg), (full, ends),
        w3, lengths, g3, input_map, ff_gain, pwb, smem=(1,))
    (grad,) = _call(
        functools.partial(k_last, seg), (full,), s4, lengths, gather(e4), states, ref, pwf,
        smem=(1,))
    shape3 = (scen_count, seg_steps, width)
    return (states.reshape(shape3), grad.reshape(shape3), cost)


def solution(mesh):
    placed = (
        P("groups", "tm", None),
        P("groups", "tm", None),
        P("groups", None),
        P(),
        P(),
        P(),
        P(),
        P(),
        P("groups", None),
    )
    return jax.shard_map(
        per_device,
        mesh=mesh,
        in_specs=placed,
        out_specs=(P("groups", "tm", None), P("groups", "tm", None), P("groups")),
        check_vma=False,
    )
```

```python
import functools

import jax
import jax.numpy as jnp
from jax import lax
from jax.experimental import pallas as pl
from jax.experimental.pallas import tpu as pltpu
from jax.sharding import PartitionSpec as P

HIGH = lax.Precision.HIGHEST


def build_dynamics(decay, coupling, links):
    size = decay.shape[0]
    width = coupling.shape[1]
    lanes = jnp.arange(size, dtype=jnp.int32)
    offsets = jnp.arange(width, dtype=jnp.int32)
    row_hot = (lanes[None, :, None] == links[:, 0:1, None] * width + offsets[None, None, :]).astype(
        jnp.float32
    )
    col_hot = (lanes[None, :, None] == links[:, 1:2, None] * width + offsets[None, None, :]).astype(
        jnp.float32
    )
    placed = jnp.einsum(
        "lia,lab,ljb->ij", row_hot, coupling, col_hot, precision=lax.Precision.HIGHEST
    )
    return jnp.diag(decay) + placed


def row_times(values, matrix):
    width = values.shape[-1]
    flat = jnp.dot(values.reshape(-1, width), matrix, precision=lax.Precision.HIGHEST)
    return flat.reshape(values.shape)


def _dot(a, b):
    return jnp.dot(a, b, precision=HIGH, preferred_element_type=jnp.float32)


def _dot_nt(a, b):
    return lax.dot_general(
        a, b, (((1,), (1,)), ((), ())), precision=HIGH, preferred_element_type=jnp.float32)


def _split(x):
    hi = x.astype(jnp.bfloat16)
    lo = (x - hi.astype(jnp.float32)).astype(jnp.bfloat16)
    return hi, lo


class _Pair:
    def __init__(self, hi, lo):
        self.hi, self.lo = hi, lo
        self.shape = hi.shape

    def __getitem__(self, index):
        return (self.hi[index], self.lo[index])


def _mm(a, b, nt=False):
    dims = (((1,), (1 if nt else 0,)), ((), ()))
    a_hi, a_lo = _split(a)
    b_hi, b_lo = b if isinstance(b, tuple) else _split(b)
    part = functools.partial(lax.dot_general, dimension_numbers=dims,
                             preferred_element_type=jnp.float32)
    rows = a.shape[0]
    both = part(jnp.concatenate([a_hi, a_lo], axis=0), b_hi)
    return both[:rows] + both[rows:] + part(a_hi, b_lo)


def _build(decay_ref, coupling_ref, links_ref):
    size = decay_ref.shape[1]
    width = coupling_ref.shape[1]
    r = lax.broadcasted_iota(jnp.int32, (size, size), 0)
    c = lax.broadcasted_iota(jnp.int32, (size, size), 1)
    power = jnp.where(r == c, jnp.broadcast_to(decay_ref[...], (size, size)), 0.0)
    lane = lax.broadcasted_iota(jnp.int32, (size, width), 0)
    off = lax.broadcasted_iota(jnp.int32, (size, width), 1)
    for link in range(coupling_ref.shape[0]):
        row_hot = (lane == links_ref[0, link] * width + off).astype(jnp.float32)
        col_hot = (lane == links_ref[1, link] * width + off).astype(jnp.float32)
        power = power + _dot_nt(_dot(row_hot, coupling_ref[link]), col_hot)
    return power


def _scan(v, cut, pw_ref, seg, backward, carry=None, levels=None):
    rows, width = v.shape
    scen = rows // seg
    t = lax.broadcasted_iota(jnp.int32, (rows, width), 0) % seg
    flags = 1.0 - cut
    if levels is None:
        levels = seg.bit_length() - 1
    step = functools.partial(_mm, nt=not backward)
    if carry is not None:
        pushed = step(carry, pw_ref[0])
        pushed = jnp.broadcast_to(pushed[:, None, :], (scen, seg, width)).reshape(rows, width)
        first = t == (seg - 1 if backward else 0)
        v = v + jnp.where(first, flags * pushed, 0.0)
    for level in range(levels):
        stride = 2**level
        if backward:
            prior_v = pltpu.roll(v, rows - stride, 0)
            prior_f = pltpu.roll(flags, rows - stride, 0)
            valid = t < seg - stride
        else:
            prior_v = pltpu.roll(v, stride, 0)
            prior_f = pltpu.roll(flags, stride, 0)
            valid = t >= stride
        prior_v = jnp.where(valid, prior_v, 0.0)
        prior_f = jnp.where(valid, prior_f, 1.0)
        v = v + flags * step(prior_v, pw_ref[level])
        flags = flags * prior_f
    return v


def _carry(g_ref, len_ref, pw_ref, scen, backward, seg):
    width = pw_ref.shape[1]
    g = g_ref[...][:, :width]
    rows = g.shape[0]
    devices = rows // scen
    local_levels = pw_ref.shape[0] - max((devices - 1).bit_length(), 1)
    r = lax.broadcasted_iota(jnp.int32, (rows, width), 0)
    flags = jnp.broadcast_to(_seg_flags(len_ref, devices, seg, not backward), (rows, width))
    step = functools.partial(_mm, nt=not backward)
    for level in range((devices - 1).bit_length()):
        stride = scen * 2**level
        if backward:
            prior_g = pltpu.roll(g, rows - stride, 0)
            prior_f = pltpu.roll(flags, rows - stride, 0)
            valid = r < rows - stride
        else:
            prior_g = pltpu.roll(g, stride, 0)
            prior_f = pltpu.roll(flags, stride, 0)
            valid = r >= stride
        prior_g = jnp.where(valid, prior_g, 0.0)
        prior_f = jnp.where(valid, prior_f, 1.0)
        g = g + flags * step(prior_g, pw_ref[local_levels + level])
        flags = flags * prior_f
    me = lax.axis_index("tm")
    target = me + 1 if backward else me - 1
    pick = lax.broadcasted_iota(jnp.int32, (scen, rows), 1)
    want = lax.broadcasted_iota(jnp.int32, (scen, rows), 0) + target * scen
    return _dot((pick == want).astype(jnp.float32), g)


def _ends(v, seg, backward, out_rows):
    rows, width = v.shape
    scen = rows // seg
    pick = lax.broadcasted_iota(jnp.int32, (scen, rows), 1)
    want = lax.broadcasted_iota(jnp.int32, (scen, rows), 0) * seg + (0 if backward else seg - 1)
    ends = _dot((pick == want).astype(jnp.float32), v)
    return jnp.broadcast_to(ends[None], (out_rows,) + ends.shape)


def _cut_rows(len_ref, shape, seg, start):
    rows, width = shape
    scen, episodes = len_ref.shape
    r = lax.broadcasted_iota(jnp.int32, (rows, 1), 0)
    which = r // seg
    pos = lax.axis_index("tm") * seg + r % seg
    hit = jnp.zeros((rows, 1), jnp.bool_)
    for s in range(scen):
        edge = 0
        for k in range(episodes):
            first = edge
            edge = edge + len_ref[s, k]
            hit = hit | ((which == s) & (pos == first if start else pos + 1 == edge))
    return jnp.broadcast_to(hit.astype(jnp.float32), shape)


def _seg_flags(len_ref, devices, seg, start):
    scen, episodes = len_ref.shape
    rows = devices * scen
    r = lax.broadcasted_iota(jnp.int32, (rows, 1), 0)
    which = r % scen
    lo = r // scen * seg
    hit = jnp.zeros((rows, 1), jnp.bool_)
    for s in range(scen):
        edge = 0
        for k in range(episodes):
            first = edge
            edge = edge + len_ref[s, k]
            if start:
                inside = (first >= lo) & (first < lo + seg)
            else:
                inside = (edge > lo) & (edge <= lo + seg)
            hit = hit | ((which == s) & inside)
    return 1.0 - hit.astype(jnp.float32)


def _vmem(count):
    return [pl.BlockSpec(memory_space=pltpu.VMEM)] * count


def _call(kernel, outs, *args, smem=()):
    specs = _vmem(len(args))
    for index in smem:
        specs[index] = pl.BlockSpec(memory_space=pltpu.SMEM)
    return pl.pallas_call(
        kernel,
        out_shape=outs,
        in_specs=specs,
        out_specs=tuple(_vmem(len(outs))),
    )(*args)


def k_first(seg, decay_ref, coupling_ref, links_ref, cw_ref, ref_ref, len_ref, phi_ref, plo_ref,
            w1_ref, e1_ref):
    pwb_ref = _Pair(phi_ref, plo_ref)
    local_levels = seg.bit_length() - 1
    power = _build(decay_ref, coupling_ref, links_ref)
    phi_ref[0], plo_ref[0] = _split(power)
    for level in range(1, pwb_ref.shape[0]):
        if level == local_levels:
            cut = _cut_rows(len_ref, cw_ref.shape, seg, False)
            w1 = cw_ref[...] * ref_ref[...]
            w1_ref[...] = w1
            e1_ref[...] = _ends(_scan(w1, cut, pwb_ref, seg, True), seg, True, e1_ref.shape[0])
        power = _dot(power, power)
        phi_ref[level], plo_ref[level] = _split(power)


def k_states_in(seg, w1_ref, len_ref, c1_ref, xi_ref, gain_ref, imap_ref, phi_ref, plo_ref, d2_ref,
                e2_ref):
    pwb_ref = pwf_ref = _Pair(phi_ref, plo_ref)
    shape = w1_ref.shape
    cut_e = _cut_rows(len_ref, shape, seg, False)
    cut_s = _cut_rows(len_ref, shape, seg, True)
    c1 = _carry(c1_ref, len_ref, pwb_ref, w1_ref.shape[0] // seg, True, seg)
    vt = _scan(w1_ref[...], cut_e, pwb_ref, seg, True, c1)
    controls = _mm(vt, gain_ref[...], nt=True)
    forcing = -_mm(controls, imap_ref[...], nt=True)
    rows, width = shape
    scen = rows // seg
    image = _mm(xi_ref[...], pwf_ref[0], nt=True)
    init = jnp.broadcast_to(image[:, None, :], (scen, seg, width)).reshape(rows, width)
    d2 = forcing + cut_s * init
    d2_ref[...] = d2
    e2_ref[...] = _ends(_scan(d2, cut_s, pwf_ref, seg, False), seg, False, e2_ref.shape[0])


def k_adjoint_in(seg, scale, d2_ref, len_ref, c2_ref, cw_ref, ref_ref, phi_ref, plo_ref, x_ref,
                 w3_ref, e3_ref):
    pwb_ref = pwf_ref = _Pair(phi_ref, plo_ref)
    shape = d2_ref.shape
    rows, width = shape
    scen = rows // seg
    cut_s = _cut_rows(len_ref, shape, seg, True)
    cut_e = _cut_rows(len_ref, shape, seg, False)
    c2 = _carry(c2_ref, len_ref, pwf_ref, scen, False, seg)
    states = _scan(d2_ref[...], cut_s, pwf_ref, seg, False, c2)
    x_ref[...] = states
    offset = states - ref_ref[...]
    cw = cw_ref[...]
    w3 = cw * offset
    w3_ref[...] = w3
    per_row = jnp.sum(w3 * offset, axis=1, keepdims=True)
    copies = e3_ref.shape[0]
    pick = lax.broadcasted_iota(jnp.int32, (scen, rows), 1) // seg
    want = lax.broadcasted_iota(jnp.int32, (scen, rows), 0)
    sel = (pick == want).astype(jnp.float32)
    per_scen = _dot(sel, jnp.broadcast_to(per_row, (rows, 128))) * scale
    e3_ref[:, :, width:] = jnp.broadcast_to(per_scen[None], (copies, scen, 128))
    e3_ref[:, :, :width] = _ends(_scan(w3, cut_e, pwb_ref, seg, True), seg, True, copies)


def k_value_adjoint_in(seg, w3_ref, len_ref, c3_ref, imap_ref, gain_ref, phi_ref, plo_ref, s4_ref,
                       e4_ref):
    pwb_ref = pwf_ref = _Pair(phi_ref, plo_ref)
    shape = w3_ref.shape
    cut_e = _cut_rows(len_ref, shape, seg, False)
    cut_s = _cut_rows(len_ref, shape, seg, True)
    c3 = _carry(c3_ref, len_ref, pwb_ref, w3_ref.shape[0] // seg, True, seg)
    adjoint = _scan(w3_ref[...], cut_e, pwb_ref, seg, True, c3)
    pulled = _mm(adjoint, imap_ref[...])
    source = -_mm(pulled, gain_ref[...])
    s4_ref[...] = source
    e4_ref[...] = _ends(_scan(source, cut_s, pwf_ref, seg, False), seg, False, e4_ref.shape[0])


def k_last(seg, s4_ref, len_ref, c4_ref, x_ref, ref_ref, phi_ref, plo_ref, g_ref):
    pwf_ref = _Pair(phi_ref, plo_ref)
    shape = s4_ref.shape
    cut_s = _cut_rows(len_ref, shape, seg, True)
    c4 = _carry(c4_ref, len_ref, pwf_ref, s4_ref.shape[0] // seg, False, seg)
    va = _scan(s4_ref[...], cut_s, pwf_ref, seg, False, c4)
    ref = ref_ref[...]
    offset = x_ref[...] - ref
    g_ref[...] = 0.5 * offset * offset + ref * va


def per_device(ref_traj, cost_weights, x_init, decay, coupling, links, input_map, ff_gain, lengths):
    scen_count, seg_steps, width = ref_traj.shape
    rows = scen_count * seg_steps
    devices = lax.axis_size("tm")
    device = lax.axis_index("tm")
    total = seg_steps * devices
    local_levels = seg_steps.bit_length() - 1
    device_levels = (devices - 1).bit_length()
    power_count = local_levels + max(device_levels, 1)
    cw = cost_weights.reshape(rows, width)
    ref = ref_traj.reshape(rows, width)
    f32 = jnp.float32
    full = jax.ShapeDtypeStruct((rows, width), f32)
    ends = jax.ShapeDtypeStruct((devices, scen_count, width), f32)
    seg = seg_steps

    def gather(copies):
        every = lax.all_to_all(copies, "tm", 0, 0, tiled=True)
        return every.reshape(devices * scen_count, copies.shape[2])

    powers = jax.ShapeDtypeStruct((power_count, width, width), jnp.bfloat16)
    phi, plo, w1, e1 = _call(
        functools.partial(k_first, seg), (powers, powers, full, ends),
        decay.reshape(1, width), coupling, links.T, cw, ref, lengths, smem=(2, 5))
    d2, e2 = _call(
        functools.partial(k_states_in, seg), (full, ends),
        w1, lengths, gather(e1), x_init, ff_gain, input_map, phi, plo, smem=(1,))
    packed = jax.ShapeDtypeStruct((devices, scen_count, width + 128), f32)
    states, w3, e3 = _call(
        functools.partial(k_adjoint_in, seg, 0.5 / total), (full, full, packed),
        d2, lengths, gather(e2), cw, ref, phi, plo, smem=(1,))
    g3 = gather(e3)
    cost = jnp.sum(g3[:, width].reshape(devices, scen_count), axis=0)
    s4, e4 = _call(
        functools.partial(k_value_adjoint_in, seg), (full, ends),
        w3, lengths, g3, input_map, ff_gain, phi, plo, smem=(1,))
    (grad,) = _call(
        functools.partial(k_last, seg), (full,), s4, lengths, gather(e4), states, ref, phi, plo,
        smem=(1,))
    shape3 = (scen_count, seg_steps, width)
    return (states.reshape(shape3), grad.reshape(shape3), cost)


def solution(mesh):
    placed = (
        P("groups", "tm", None),
        P("groups", "tm", None),
        P("groups", None),
        P(),
        P(),
        P(),
        P(),
        P(),
        P("groups", None),
    )
    return jax.shard_map(
        per_device,
        mesh=mesh,
        in_specs=placed,
        out_specs=(P("groups", "tm", None), P("groups", "tm", None), P("groups")),
        check_vma=False,
    )
```

```python
import functools

import jax
import jax.numpy as jnp
from jax import lax
from jax.experimental import pallas as pl
from jax.experimental.pallas import tpu as pltpu
from jax.sharding import PartitionSpec as P

HIGH = lax.Precision.HIGHEST


def build_dynamics(decay, coupling, links):
    size = decay.shape[0]
    width = coupling.shape[1]
    lanes = jnp.arange(size, dtype=jnp.int32)
    offsets = jnp.arange(width, dtype=jnp.int32)
    row_hot = (lanes[None, :, None] == links[:, 0:1, None] * width + offsets[None, None, :]).astype(
        jnp.float32
    )
    col_hot = (lanes[None, :, None] == links[:, 1:2, None] * width + offsets[None, None, :]).astype(
        jnp.float32
    )
    placed = jnp.einsum(
        "lia,lab,ljb->ij", row_hot, coupling, col_hot, precision=lax.Precision.HIGHEST
    )
    return jnp.diag(decay) + placed


def row_times(values, matrix):
    width = values.shape[-1]
    flat = jnp.dot(values.reshape(-1, width), matrix, precision=lax.Precision.HIGHEST)
    return flat.reshape(values.shape)


def _dot(a, b):
    return jnp.dot(a, b, precision=HIGH, preferred_element_type=jnp.float32)


def _dot_nt(a, b):
    return lax.dot_general(
        a, b, (((1,), (1,)), ((), ())), precision=HIGH, preferred_element_type=jnp.float32)


def _split(x):
    hi = x.astype(jnp.bfloat16)
    lo = (x - hi.astype(jnp.float32)).astype(jnp.bfloat16)
    return hi, lo


class _Pair:
    def __init__(self, hi, lo):
        self.hi, self.lo = hi, lo
        self.shape = hi.shape

    def __getitem__(self, index):
        return (self.hi[index], self.lo[index])


def _mm(a, b, nt=False):
    dims = (((1,), (1 if nt else 0,)), ((), ()))
    a_hi, a_lo = _split(a)
    b_hi, b_lo = b if isinstance(b, tuple) else _split(b)
    part = functools.partial(lax.dot_general, dimension_numbers=dims,
                             preferred_element_type=jnp.float32)
    rows = a.shape[0]
    both = part(jnp.concatenate([a_hi, a_lo], axis=0), b_hi)
    return both[:rows] + both[rows:] + part(a_hi, b_lo)


def _build(decay_ref, coupling_ref, links_ref):
    size = decay_ref.shape[1]
    width = coupling_ref.shape[1]
    r = lax.broadcasted_iota(jnp.int32, (size, size), 0)
    c = lax.broadcasted_iota(jnp.int32, (size, size), 1)
    power = jnp.where(r == c, jnp.broadcast_to(decay_ref[...], (size, size)), 0.0)
    lane = lax.broadcasted_iota(jnp.int32, (size, width), 0)
    off = lax.broadcasted_iota(jnp.int32, (size, width), 1)
    for link in range(coupling_ref.shape[0]):
        row_hot = (lane == links_ref[0, link] * width + off).astype(jnp.float32)
        col_hot = (lane == links_ref[1, link] * width + off).astype(jnp.float32)
        power = power + _dot_nt(_dot(row_hot, coupling_ref[link]), col_hot)
    return power


def _scan(v, cut, pw_ref, seg, backward, carry=None, levels=None):
    rows, width = v.shape
    scen = rows // seg
    t = lax.broadcasted_iota(jnp.int32, (rows, width), 0) % seg
    flags = 1.0 - cut
    if levels is None:
        levels = seg.bit_length() - 1
    step = functools.partial(_mm, nt=not backward)
    if carry is not None:
        pushed = step(carry, pw_ref[0])
        pushed = jnp.broadcast_to(pushed[:, None, :], (scen, seg, width)).reshape(rows, width)
        first = t == (seg - 1 if backward else 0)
        v = v + jnp.where(first, flags * pushed, 0.0)
    for level in range(levels):
        stride = 2**level
        if backward:
            prior_v = pltpu.roll(v, rows - stride, 0)
            prior_f = pltpu.roll(flags, rows - stride, 0)
            valid = t < seg - stride
        else:
            prior_v = pltpu.roll(v, stride, 0)
            prior_f = pltpu.roll(flags, stride, 0)
            valid = t >= stride
        prior_v = jnp.where(valid, prior_v, 0.0)
        prior_f = jnp.where(valid, prior_f, 1.0)
        v = v + flags * step(prior_v, pw_ref[level])
        flags = flags * prior_f
    return v


def _carry(g_ref, len_ref, pw_ref, scen, backward, seg):
    width = pw_ref.shape[1]
    g = g_ref[...][:, :width]
    rows = g.shape[0]
    devices = rows // scen
    r = lax.broadcasted_iota(jnp.int32, (rows, width), 0)
    flags = jnp.broadcast_to(_seg_flags(len_ref, devices, seg, not backward), (rows, width))
    step = functools.partial(_mm, nt=not backward)
    for level in range((devices - 1).bit_length()):
        stride = scen * 2**level
        if backward:
            prior_g = pltpu.roll(g, rows - stride, 0)
            prior_f = pltpu.roll(flags, rows - stride, 0)
            valid = r < rows - stride
        else:
            prior_g = pltpu.roll(g, stride, 0)
            prior_f = pltpu.roll(flags, stride, 0)
            valid = r >= stride
        prior_g = jnp.where(valid, prior_g, 0.0)
        prior_f = jnp.where(valid, prior_f, 1.0)
        g = g + flags * step(prior_g, pw_ref[level])
        flags = flags * prior_f
    me = lax.axis_index("tm")
    target = me + 1 if backward else me - 1
    pick = lax.broadcasted_iota(jnp.int32, (scen, rows), 1)
    want = lax.broadcasted_iota(jnp.int32, (scen, rows), 0) + target * scen
    return _dot((pick == want).astype(jnp.float32), g)


def _ends(v, seg, backward, out_rows):
    rows, width = v.shape
    scen = rows // seg
    pick = lax.broadcasted_iota(jnp.int32, (scen, rows), 1)
    want = lax.broadcasted_iota(jnp.int32, (scen, rows), 0) * seg + (0 if backward else seg - 1)
    ends = _dot((pick == want).astype(jnp.float32), v)
    return jnp.broadcast_to(ends[None], (out_rows,) + ends.shape)


def _cut_rows(len_ref, shape, seg, start):
    rows, width = shape
    scen, episodes = len_ref.shape
    r = lax.broadcasted_iota(jnp.int32, (rows, 1), 0)
    which = r // seg
    pos = lax.axis_index("tm") * seg + r % seg
    hit = jnp.zeros((rows, 1), jnp.bool_)
    for s in range(scen):
        edge = 0
        for k in range(episodes):
            first = edge
            edge = edge + len_ref[s, k]
            hit = hit | ((which == s) & (pos == first if start else pos + 1 == edge))
    return jnp.broadcast_to(hit.astype(jnp.float32), shape)


def _seg_flags(len_ref, devices, seg, start):
    scen, episodes = len_ref.shape
    rows = devices * scen
    r = lax.broadcasted_iota(jnp.int32, (rows, 1), 0)
    which = r % scen
    lo = r // scen * seg
    hit = jnp.zeros((rows, 1), jnp.bool_)
    for s in range(scen):
        edge = 0
        for k in range(episodes):
            first = edge
            edge = edge + len_ref[s, k]
            if start:
                inside = (first >= lo) & (first < lo + seg)
            else:
                inside = (edge > lo) & (edge <= lo + seg)
            hit = hit | ((which == s) & inside)
    return 1.0 - hit.astype(jnp.float32)


def _vmem(count):
    return [pl.BlockSpec(memory_space=pltpu.VMEM)] * count


def _call(kernel, outs, *args, smem=()):
    specs = _vmem(len(args))
    for index in smem:
        specs[index] = pl.BlockSpec(memory_space=pltpu.SMEM)
    return pl.pallas_call(
        kernel,
        out_shape=outs,
        in_specs=specs,
        out_specs=tuple(_vmem(len(outs))),
    )(*args)


def k_first(seg, decay_ref, coupling_ref, links_ref, cw_ref, ref_ref, len_ref, phi_ref, plo_ref,
            top_ref, w1_ref, e1_ref):
    pwb_ref = _Pair(phi_ref, plo_ref)
    power = _build(decay_ref, coupling_ref, links_ref)
    phi_ref[0], plo_ref[0] = _split(power)
    for level in range(1, pwb_ref.shape[0]):
        power = _dot(power, power)
        phi_ref[level], plo_ref[level] = _split(power)
    top_ref[...] = power
    cut = _cut_rows(len_ref, cw_ref.shape, seg, False)
    w1 = cw_ref[...] * ref_ref[...]
    w1_ref[...] = w1
    e1_ref[...] = _ends(_scan(w1, cut, pwb_ref, seg, True), seg, True, e1_ref.shape[0])


def k_device_powers(top_ref, dhi_ref, dlo_ref):
    power = top_ref[...]
    for level in range(dhi_ref.shape[0]):
        power = _dot(power, power)
        dhi_ref[level], dlo_ref[level] = _split(power)


def k_states_in(seg, w1_ref, len_ref, c1_ref, xi_ref, gain_ref, imap_ref, phi_ref, plo_ref, dhi_ref, dlo_ref, d2_ref,
                e2_ref):
    pwb_ref = pwf_ref = _Pair(phi_ref, plo_ref)
    shape = w1_ref.shape
    cut_e = _cut_rows(len_ref, shape, seg, False)
    cut_s = _cut_rows(len_ref, shape, seg, True)
    c1 = _carry(c1_ref, len_ref, _Pair(dhi_ref, dlo_ref), w1_ref.shape[0] // seg, True, seg)
    vt = _scan(w1_ref[...], cut_e, pwb_ref, seg, True, c1)
    controls = _mm(vt, gain_ref[...], nt=True)
    forcing = -_mm(controls, imap_ref[...], nt=True)
    rows, width = shape
    scen = rows // seg
    image = _mm(xi_ref[...], pwf_ref[0], nt=True)
    init = jnp.broadcast_to(image[:, None, :], (scen, seg, width)).reshape(rows, width)
    d2 = forcing + cut_s * init
    d2_ref[...] = d2
    e2_ref[...] = _ends(_scan(d2, cut_s, pwf_ref, seg, False), seg, False, e2_ref.shape[0])


def k_adjoint_in(seg, scale, d2_ref, len_ref, c2_ref, cw_ref, ref_ref, phi_ref, plo_ref, dhi_ref, dlo_ref, x_ref,
                 w3_ref, e3_ref):
    pwb_ref = pwf_ref = _Pair(phi_ref, plo_ref)
    shape = d2_ref.shape
    rows, width = shape
    scen = rows // seg
    cut_s = _cut_rows(len_ref, shape, seg, True)
    cut_e = _cut_rows(len_ref, shape, seg, False)
    c2 = _carry(c2_ref, len_ref, _Pair(dhi_ref, dlo_ref), scen, False, seg)
    states = _scan(d2_ref[...], cut_s, pwf_ref, seg, False, c2)
    x_ref[...] = states
    offset = states - ref_ref[...]
    cw = cw_ref[...]
    w3 = cw * offset
    w3_ref[...] = w3
    per_row = jnp.sum(w3 * offset, axis=1, keepdims=True)
    copies = e3_ref.shape[0]
    pick = lax.broadcasted_iota(jnp.int32, (scen, rows), 1) // seg
    want = lax.broadcasted_iota(jnp.int32, (scen, rows), 0)
    sel = (pick == want).astype(jnp.float32)
    per_scen = _dot(sel, jnp.broadcast_to(per_row, (rows, 128))) * scale
    e3_ref[:, :, width:] = jnp.broadcast_to(per_scen[None], (copies, scen, 128))
    e3_ref[:, :, :width] = _ends(_scan(w3, cut_e, pwb_ref, seg, True), seg, True, copies)


def k_value_adjoint_in(seg, w3_ref, len_ref, c3_ref, imap_ref, gain_ref, phi_ref, plo_ref, dhi_ref, dlo_ref, s4_ref,
                       e4_ref):
    pwb_ref = pwf_ref = _Pair(phi_ref, plo_ref)
    shape = w3_ref.shape
    cut_e = _cut_rows(len_ref, shape, seg, False)
    cut_s = _cut_rows(len_ref, shape, seg, True)
    c3 = _carry(c3_ref, len_ref, _Pair(dhi_ref, dlo_ref), w3_ref.shape[0] // seg, True, seg)
    adjoint = _scan(w3_ref[...], cut_e, pwb_ref, seg, True, c3)
    pulled = _mm(adjoint, imap_ref[...])
    source = -_mm(pulled, gain_ref[...])
    s4_ref[...] = source
    e4_ref[...] = _ends(_scan(source, cut_s, pwf_ref, seg, False), seg, False, e4_ref.shape[0])


def k_last(seg, s4_ref, len_ref, c4_ref, x_ref, ref_ref, phi_ref, plo_ref, dhi_ref, dlo_ref, g_ref):
    pwf_ref = _Pair(phi_ref, plo_ref)
    shape = s4_ref.shape
    cut_s = _cut_rows(len_ref, shape, seg, True)
    c4 = _carry(c4_ref, len_ref, _Pair(dhi_ref, dlo_ref), s4_ref.shape[0] // seg, False, seg)
    va = _scan(s4_ref[...], cut_s, pwf_ref, seg, False, c4)
    ref = ref_ref[...]
    offset = x_ref[...] - ref
    g_ref[...] = 0.5 * offset * offset + ref * va


def per_device(ref_traj, cost_weights, x_init, decay, coupling, links, input_map, ff_gain, lengths):
    scen_count, seg_steps, width = ref_traj.shape
    rows = scen_count * seg_steps
    devices = lax.axis_size("tm")
    device = lax.axis_index("tm")
    total = seg_steps * devices
    local_levels = seg_steps.bit_length() - 1
    device_levels = (devices - 1).bit_length()
    power_count = local_levels + max(device_levels, 1)
    cw = cost_weights.reshape(rows, width)
    ref = ref_traj.reshape(rows, width)
    f32 = jnp.float32
    full = jax.ShapeDtypeStruct((rows, width), f32)
    ends = jax.ShapeDtypeStruct((devices, scen_count, width), f32)
    seg = seg_steps

    def gather(copies):
        every = lax.all_to_all(copies, "tm", 0, 0, tiled=True)
        return every.reshape(devices * scen_count, copies.shape[2])

    powers = jax.ShapeDtypeStruct((local_levels, width, width), jnp.bfloat16)
    square = jax.ShapeDtypeStruct((width, width), f32)
    phi, plo, top, w1, e1 = _call(
        functools.partial(k_first, seg), (powers, powers, square, full, ends),
        decay.reshape(1, width), coupling, links.T, cw, ref, lengths, smem=(2, 5))
    dev = jax.ShapeDtypeStruct((max(device_levels, 1), width, width), jnp.bfloat16)
    dhi, dlo = _call(k_device_powers, (dev, dev), top)
    d2, e2 = _call(
        functools.partial(k_states_in, seg), (full, ends),
        w1, lengths, gather(e1), x_init, ff_gain, input_map, phi, plo, dhi, dlo, smem=(1,))
    packed = jax.ShapeDtypeStruct((devices, scen_count, width + 128), f32)
    states, w3, e3 = _call(
        functools.partial(k_adjoint_in, seg, 0.5 / total), (full, full, packed),
        d2, lengths, gather(e2), cw, ref, phi, plo, dhi, dlo, smem=(1,))
    g3 = gather(e3)
    cost = jnp.sum(g3[:, width].reshape(devices, scen_count), axis=0)
    s4, e4 = _call(
        functools.partial(k_value_adjoint_in, seg), (full, ends),
        w3, lengths, g3, input_map, ff_gain, phi, plo, dhi, dlo, smem=(1,))
    (grad,) = _call(
        functools.partial(k_last, seg), (full,), s4, lengths, gather(e4), states, ref, phi, plo, dhi, dlo,
        smem=(1,))
    shape3 = (scen_count, seg_steps, width)
    return (states.reshape(shape3), grad.reshape(shape3), cost)


def solution(mesh):
    placed = (
        P("groups", "tm", None),
        P("groups", "tm", None),
        P("groups", None),
        P(),
        P(),
        P(),
        P(),
        P(),
        P("groups", None),
    )
    return jax.shard_map(
        per_device,
        mesh=mesh,
        in_specs=placed,
        out_specs=(P("groups", "tm", None), P("groups", "tm", None), P("groups")),
        check_vma=False,
    )
```

```python
import functools

import jax
import jax.numpy as jnp
from jax import lax
from jax.experimental import pallas as pl
from jax.experimental.pallas import tpu as pltpu
from jax.sharding import PartitionSpec as P

HIGH = lax.Precision.HIGHEST


def build_dynamics(decay, coupling, links):
    size = decay.shape[0]
    width = coupling.shape[1]
    lanes = jnp.arange(size, dtype=jnp.int32)
    offsets = jnp.arange(width, dtype=jnp.int32)
    row_hot = (lanes[None, :, None] == links[:, 0:1, None] * width + offsets[None, None, :]).astype(
        jnp.float32
    )
    col_hot = (lanes[None, :, None] == links[:, 1:2, None] * width + offsets[None, None, :]).astype(
        jnp.float32
    )
    placed = jnp.einsum(
        "lia,lab,ljb->ij", row_hot, coupling, col_hot, precision=lax.Precision.HIGHEST
    )
    return jnp.diag(decay) + placed


def row_times(values, matrix):
    width = values.shape[-1]
    flat = jnp.dot(values.reshape(-1, width), matrix, precision=lax.Precision.HIGHEST)
    return flat.reshape(values.shape)


def _dot(a, b):
    return jnp.dot(a, b, precision=HIGH, preferred_element_type=jnp.float32)


def _dot_nt(a, b):
    return lax.dot_general(
        a, b, (((1,), (1,)), ((), ())), precision=HIGH, preferred_element_type=jnp.float32)


def _split(x):
    hi = x.astype(jnp.bfloat16)
    lo = (x - hi.astype(jnp.float32)).astype(jnp.bfloat16)
    return hi, lo


class _Pair:
    def __init__(self, hi, lo):
        self.hi, self.lo = hi, lo
        self.shape = hi.shape

    def __getitem__(self, index):
        return (self.hi[index], self.lo[index])


def _mm(a, b, nt=False):
    dims = (((1,), (1 if nt else 0,)), ((), ()))
    a_hi, a_lo = _split(a)
    b_hi, b_lo = b if isinstance(b, tuple) else _split(b)
    part = functools.partial(lax.dot_general, dimension_numbers=dims,
                             preferred_element_type=jnp.float32)
    rows = a.shape[0]
    both = part(jnp.concatenate([a_hi, a_lo], axis=0), b_hi)
    return both[:rows] + both[rows:] + part(a_hi, b_lo)


def _build(decay_ref, coupling_ref, links_ref):
    size = decay_ref.shape[1]
    width = coupling_ref.shape[1]
    r = lax.broadcasted_iota(jnp.int32, (size, size), 0)
    c = lax.broadcasted_iota(jnp.int32, (size, size), 1)
    power = jnp.where(r == c, jnp.broadcast_to(decay_ref[...], (size, size)), 0.0)
    lane = lax.broadcasted_iota(jnp.int32, (size, width), 0)
    off = lax.broadcasted_iota(jnp.int32, (size, width), 1)
    for link in range(coupling_ref.shape[0]):
        row_hot = (lane == links_ref[0, link] * width + off).astype(jnp.float32)
        col_hot = (lane == links_ref[1, link] * width + off).astype(jnp.float32)
        power = power + _dot_nt(_dot(row_hot, coupling_ref[link]), col_hot)
    return power


def _scan(v, cut, pw_ref, seg, backward, carry=None, levels=None):
    rows, width = v.shape
    scen = rows // seg
    t = lax.broadcasted_iota(jnp.int32, (rows, width), 0) % seg
    flags = 1.0 - cut
    if levels is None:
        levels = seg.bit_length() - 1
    step = functools.partial(_mm, nt=not backward)
    if carry is not None:
        pushed = step(carry, pw_ref[0])
        pushed = jnp.broadcast_to(pushed[:, None, :], (scen, seg, width)).reshape(rows, width)
        first = t == (seg - 1 if backward else 0)
        v = v + jnp.where(first, flags * pushed, 0.0)
    for level in range(levels):
        stride = 2**level
        if backward:
            prior_v = pltpu.roll(v, rows - stride, 0)
            prior_f = pltpu.roll(flags, rows - stride, 0)
            valid = t < seg - stride
        else:
            prior_v = pltpu.roll(v, stride, 0)
            prior_f = pltpu.roll(flags, stride, 0)
            valid = t >= stride
        prior_v = jnp.where(valid, prior_v, 0.0)
        prior_f = jnp.where(valid, prior_f, 1.0)
        v = v + flags * step(prior_v, pw_ref[level])
        flags = flags * prior_f
    return v


def _carry(g_ref, len_ref, pw_ref, scen, backward, seg):
    width = pw_ref.shape[1]
    g = g_ref[...][:, :width]
    rows = g.shape[0]
    devices = rows // scen
    r = lax.broadcasted_iota(jnp.int32, (rows, width), 0)
    flags = jnp.broadcast_to(_seg_flags(len_ref, devices, seg, not backward), (rows, width))
    step = functools.partial(_mm, nt=not backward)
    for level in range((devices - 1).bit_length()):
        stride = scen * 2**level
        if backward:
            prior_g = pltpu.roll(g, rows - stride, 0)
            prior_f = pltpu.roll(flags, rows - stride, 0)
            valid = r < rows - stride
        else:
            prior_g = pltpu.roll(g, stride, 0)
            prior_f = pltpu.roll(flags, stride, 0)
            valid = r >= stride
        prior_g = jnp.where(valid, prior_g, 0.0)
        prior_f = jnp.where(valid, prior_f, 1.0)
        g = g + flags * step(prior_g, pw_ref[level])
        flags = flags * prior_f
    me = lax.axis_index("tm")
    target = me + 1 if backward else me - 1
    pick = lax.broadcasted_iota(jnp.int32, (scen, rows), 1)
    want = lax.broadcasted_iota(jnp.int32, (scen, rows), 0) + target * scen
    return _dot((pick == want).astype(jnp.float32), g)


def _ends(v, seg, backward, out_rows):
    rows, width = v.shape
    scen = rows // seg
    pick = lax.broadcasted_iota(jnp.int32, (scen, rows), 1)
    want = lax.broadcasted_iota(jnp.int32, (scen, rows), 0) * seg + (0 if backward else seg - 1)
    ends = _dot((pick == want).astype(jnp.float32), v)
    return jnp.broadcast_to(ends[None], (out_rows,) + ends.shape)


def _cut_rows(len_ref, shape, seg, start):
    rows, width = shape
    scen, episodes = len_ref.shape
    r = lax.broadcasted_iota(jnp.int32, (rows, 1), 0)
    which = r // seg
    pos = lax.axis_index("tm") * seg + r % seg
    hit = jnp.zeros((rows, 1), jnp.bool_)
    for s in range(scen):
        edge = 0
        for k in range(episodes):
            first = edge
            edge = edge + len_ref[s, k]
            hit = hit | ((which == s) & (pos == first if start else pos + 1 == edge))
    return jnp.broadcast_to(hit.astype(jnp.float32), shape)


def _seg_flags(len_ref, devices, seg, start):
    scen, episodes = len_ref.shape
    rows = devices * scen
    r = lax.broadcasted_iota(jnp.int32, (rows, 1), 0)
    which = r % scen
    lo = r // scen * seg
    hit = jnp.zeros((rows, 1), jnp.bool_)
    for s in range(scen):
        edge = 0
        for k in range(episodes):
            first = edge
            edge = edge + len_ref[s, k]
            if start:
                inside = (first >= lo) & (first < lo + seg)
            else:
                inside = (edge > lo) & (edge <= lo + seg)
            hit = hit | ((which == s) & inside)
    return 1.0 - hit.astype(jnp.float32)


def _vmem(count):
    return [pl.BlockSpec(memory_space=pltpu.VMEM)] * count


def _call(kernel, outs, *args, smem=()):
    specs = _vmem(len(args))
    for index in smem:
        specs[index] = pl.BlockSpec(memory_space=pltpu.SMEM)
    return pl.pallas_call(
        kernel,
        out_shape=outs,
        in_specs=specs,
        out_specs=tuple(_vmem(len(outs))),
    )(*args)


def k_first(seg, decay_ref, coupling_ref, links_ref, cw_ref, ref_ref, len_ref, phi_ref, plo_ref,
            top_ref, w1_ref, e1_ref):
    power = _build(decay_ref, coupling_ref, links_ref)
    cut = _cut_rows(len_ref, cw_ref.shape, seg, False)
    v = cw_ref[...] * ref_ref[...]
    w1_ref[...] = v
    rows, width = v.shape
    t = lax.broadcasted_iota(jnp.int32, (rows, width), 0) % seg
    flags = 1.0 - cut
    for level in range(phi_ref.shape[0]):
        if level:
            power = _dot(power, power)
        pair = _split(power)
        phi_ref[level], plo_ref[level] = pair
        stride = 2**level
        prior_v = pltpu.roll(v, rows - stride, 0)
        prior_f = pltpu.roll(flags, rows - stride, 0)
        valid = t < seg - stride
        prior_v = jnp.where(valid, prior_v, 0.0)
        prior_f = jnp.where(valid, prior_f, 1.0)
        v = v + flags * _mm(prior_v, pair)
        flags = flags * prior_f
    top_ref[...] = power
    e1_ref[...] = _ends(v, seg, True, e1_ref.shape[0])


def k_device_powers(top_ref, dhi_ref, dlo_ref):
    power = top_ref[...]
    for level in range(dhi_ref.shape[0]):
        power = _dot(power, power)
        dhi_ref[level], dlo_ref[level] = _split(power)


def k_states_in(seg, w1_ref, len_ref, c1_ref, xi_ref, gain_ref, imap_ref, phi_ref, plo_ref, dhi_ref, dlo_ref, d2_ref,
                e2_ref):
    pwb_ref = pwf_ref = _Pair(phi_ref, plo_ref)
    shape = w1_ref.shape
    cut_e = _cut_rows(len_ref, shape, seg, False)
    cut_s = _cut_rows(len_ref, shape, seg, True)
    c1 = _carry(c1_ref, len_ref, _Pair(dhi_ref, dlo_ref), w1_ref.shape[0] // seg, True, seg)
    vt = _scan(w1_ref[...], cut_e, pwb_ref, seg, True, c1)
    controls = _mm(vt, gain_ref[...], nt=True)
    forcing = -_mm(controls, imap_ref[...], nt=True)
    rows, width = shape
    scen = rows // seg
    image = _mm(xi_ref[...], pwf_ref[0], nt=True)
    init = jnp.broadcast_to(image[:, None, :], (scen, seg, width)).reshape(rows, width)
    d2 = forcing + cut_s * init
    d2_ref[...] = d2
    e2_ref[...] = _ends(_scan(d2, cut_s, pwf_ref, seg, False), seg, False, e2_ref.shape[0])


def k_adjoint_in(seg, scale, d2_ref, len_ref, c2_ref, cw_ref, ref_ref, phi_ref, plo_ref, dhi_ref, dlo_ref, x_ref,
                 w3_ref, e3_ref):
    pwb_ref = pwf_ref = _Pair(phi_ref, plo_ref)
    shape = d2_ref.shape
    rows, width = shape
    scen = rows // seg
    cut_s = _cut_rows(len_ref, shape, seg, True)
    cut_e = _cut_rows(len_ref, shape, seg, False)
    c2 = _carry(c2_ref, len_ref, _Pair(dhi_ref, dlo_ref), scen, False, seg)
    states = _scan(d2_ref[...], cut_s, pwf_ref, seg, False, c2)
    x_ref[...] = states
    offset = states - ref_ref[...]
    cw = cw_ref[...]
    w3 = cw * offset
    w3_ref[...] = w3
    per_row = jnp.sum(w3 * offset, axis=1, keepdims=True)
    copies = e3_ref.shape[0]
    pick = lax.broadcasted_iota(jnp.int32, (scen, rows), 1) // seg
    want = lax.broadcasted_iota(jnp.int32, (scen, rows), 0)
    sel = (pick == want).astype(jnp.float32)
    per_scen = _dot(sel, jnp.broadcast_to(per_row, (rows, 128))) * scale
    e3_ref[:, :, width:] = jnp.broadcast_to(per_scen[None], (copies, scen, 128))
    e3_ref[:, :, :width] = _ends(_scan(w3, cut_e, pwb_ref, seg, True), seg, True, copies)


def k_value_adjoint_in(seg, w3_ref, len_ref, c3_ref, imap_ref, gain_ref, phi_ref, plo_ref, dhi_ref, dlo_ref, s4_ref,
                       e4_ref):
    pwb_ref = pwf_ref = _Pair(phi_ref, plo_ref)
    shape = w3_ref.shape
    cut_e = _cut_rows(len_ref, shape, seg, False)
    cut_s = _cut_rows(len_ref, shape, seg, True)
    c3 = _carry(c3_ref, len_ref, _Pair(dhi_ref, dlo_ref), w3_ref.shape[0] // seg, True, seg)
    adjoint = _scan(w3_ref[...], cut_e, pwb_ref, seg, True, c3)
    pulled = _mm(adjoint, imap_ref[...])
    source = -_mm(pulled, gain_ref[...])
    s4_ref[...] = source
    e4_ref[...] = _ends(_scan(source, cut_s, pwf_ref, seg, False), seg, False, e4_ref.shape[0])


def k_last(seg, s4_ref, len_ref, c4_ref, x_ref, ref_ref, phi_ref, plo_ref, dhi_ref, dlo_ref, g_ref):
    pwf_ref = _Pair(phi_ref, plo_ref)
    shape = s4_ref.shape
    cut_s = _cut_rows(len_ref, shape, seg, True)
    c4 = _carry(c4_ref, len_ref, _Pair(dhi_ref, dlo_ref), s4_ref.shape[0] // seg, False, seg)
    va = _scan(s4_ref[...], cut_s, pwf_ref, seg, False, c4)
    ref = ref_ref[...]
    offset = x_ref[...] - ref
    g_ref[...] = 0.5 * offset * offset + ref * va


def per_device(ref_traj, cost_weights, x_init, decay, coupling, links, input_map, ff_gain, lengths):
    scen_count, seg_steps, width = ref_traj.shape
    rows = scen_count * seg_steps
    devices = lax.axis_size("tm")
    device = lax.axis_index("tm")
    total = seg_steps * devices
    local_levels = seg_steps.bit_length() - 1
    device_levels = (devices - 1).bit_length()
    power_count = local_levels + max(device_levels, 1)
    cw = cost_weights.reshape(rows, width)
    ref = ref_traj.reshape(rows, width)
    f32 = jnp.float32
    full = jax.ShapeDtypeStruct((rows, width), f32)
    ends = jax.ShapeDtypeStruct((devices, scen_count, width), f32)
    seg = seg_steps

    def gather(copies):
        every = lax.all_to_all(copies, "tm", 0, 0, tiled=True)
        return every.reshape(devices * scen_count, copies.shape[2])

    powers = jax.ShapeDtypeStruct((local_levels, width, width), jnp.bfloat16)
    square = jax.ShapeDtypeStruct((width, width), f32)
    phi, plo, top, w1, e1 = _call(
        functools.partial(k_first, seg), (powers, powers, square, full, ends),
        decay.reshape(1, width), coupling, links.T, cw, ref, lengths, smem=(2, 5))
    dev = jax.ShapeDtypeStruct((max(device_levels, 1), width, width), jnp.bfloat16)
    dhi, dlo = _call(k_device_powers, (dev, dev), top)
    d2, e2 = _call(
        functools.partial(k_states_in, seg), (full, ends),
        w1, lengths, gather(e1), x_init, ff_gain, input_map, phi, plo, dhi, dlo, smem=(1,))
    packed = jax.ShapeDtypeStruct((devices, scen_count, width + 128), f32)
    states, w3, e3 = _call(
        functools.partial(k_adjoint_in, seg, 0.5 / total), (full, full, packed),
        d2, lengths, gather(e2), cw, ref, phi, plo, dhi, dlo, smem=(1,))
    g3 = gather(e3)
    cost = jnp.sum(g3[:, width].reshape(devices, scen_count), axis=0)
    s4, e4 = _call(
        functools.partial(k_value_adjoint_in, seg), (full, ends),
        w3, lengths, g3, input_map, ff_gain, phi, plo, dhi, dlo, smem=(1,))
    (grad,) = _call(
        functools.partial(k_last, seg), (full,), s4, lengths, gather(e4), states, ref, phi, plo, dhi, dlo,
        smem=(1,))
    shape3 = (scen_count, seg_steps, width)
    return (states.reshape(shape3), grad.reshape(shape3), cost)


def solution(mesh):
    placed = (
        P("groups", "tm", None),
        P("groups", "tm", None),
        P("groups", None),
        P(),
        P(),
        P(),
        P(),
        P(),
        P("groups", None),
    )
    return jax.shard_map(
        per_device,
        mesh=mesh,
        in_specs=placed,
        out_specs=(P("groups", "tm", None), P("groups", "tm", None), P("groups")),
        check_vma=False,
    )
```

```python
import functools

import jax
import jax.numpy as jnp
from jax import lax
from jax.experimental import pallas as pl
from jax.experimental.pallas import tpu as pltpu
from jax.sharding import PartitionSpec as P

HIGH = lax.Precision.HIGHEST


def build_dynamics(decay, coupling, links):
    size = decay.shape[0]
    width = coupling.shape[1]
    lanes = jnp.arange(size, dtype=jnp.int32)
    offsets = jnp.arange(width, dtype=jnp.int32)
    row_hot = (lanes[None, :, None] == links[:, 0:1, None] * width + offsets[None, None, :]).astype(
        jnp.float32
    )
    col_hot = (lanes[None, :, None] == links[:, 1:2, None] * width + offsets[None, None, :]).astype(
        jnp.float32
    )
    placed = jnp.einsum(
        "lia,lab,ljb->ij", row_hot, coupling, col_hot, precision=lax.Precision.HIGHEST
    )
    return jnp.diag(decay) + placed


def row_times(values, matrix):
    width = values.shape[-1]
    flat = jnp.dot(values.reshape(-1, width), matrix, precision=lax.Precision.HIGHEST)
    return flat.reshape(values.shape)


def _dot(a, b):
    return jnp.dot(a, b, precision=HIGH, preferred_element_type=jnp.float32)


def _dot_nt(a, b):
    return lax.dot_general(
        a, b, (((1,), (1,)), ((), ())), precision=HIGH, preferred_element_type=jnp.float32)


def _split(x):
    hi = x.astype(jnp.bfloat16)
    lo = (x - hi.astype(jnp.float32)).astype(jnp.bfloat16)
    return hi, lo


class _Pair:
    def __init__(self, hi, lo):
        self.hi, self.lo = hi, lo
        self.shape = hi.shape

    def __getitem__(self, index):
        return (self.hi[index], self.lo[index])


def _mm(a, b, nt=False):
    dims = (((1,), (1 if nt else 0,)), ((), ()))
    a_hi, a_lo = _split(a)
    b_hi, b_lo = b if isinstance(b, tuple) else _split(b)
    part = functools.partial(lax.dot_general, dimension_numbers=dims,
                             preferred_element_type=jnp.float32)
    rows = a.shape[0]
    both = part(jnp.concatenate([a_hi, a_lo], axis=0), b_hi)
    return both[:rows] + both[rows:] + part(a_hi, b_lo)


def _build(decay_ref, coupling_ref, links_ref):
    size = decay_ref.shape[1]
    width = coupling_ref.shape[1]
    r = lax.broadcasted_iota(jnp.int32, (size, size), 0)
    c = lax.broadcasted_iota(jnp.int32, (size, size), 1)
    power = jnp.where(r == c, jnp.broadcast_to(decay_ref[...], (size, size)), 0.0)
    lane = lax.broadcasted_iota(jnp.int32, (size, width), 0)
    off = lax.broadcasted_iota(jnp.int32, (size, width), 1)
    for link in range(coupling_ref.shape[0]):
        row_hot = (lane == links_ref[0, link] * width + off).astype(jnp.float32)
        col_hot = (lane == links_ref[1, link] * width + off).astype(jnp.float32)
        power = power + _dot_nt(_dot(row_hot, coupling_ref[link]), col_hot)
    return power


def _scan(v, cut, pw_ref, seg, backward, carry=None, levels=None):
    rows, width = v.shape
    scen = rows // seg
    t = lax.broadcasted_iota(jnp.int32, (rows, width), 0) % seg
    flags = 1.0 - cut
    if levels is None:
        levels = seg.bit_length() - 1
    step = functools.partial(_mm, nt=not backward)
    if carry is not None:
        pushed = step(carry, pw_ref[0])
        pushed = jnp.broadcast_to(pushed[:, None, :], (scen, seg, width)).reshape(rows, width)
        first = t == (seg - 1 if backward else 0)
        v = v + jnp.where(first, flags * pushed, 0.0)
    for level in range(levels):
        stride = 2**level
        if backward:
            prior_v = pltpu.roll(v, rows - stride, 0)
            prior_f = pltpu.roll(flags, rows - stride, 0)
            valid = t < seg - stride
        else:
            prior_v = pltpu.roll(v, stride, 0)
            prior_f = pltpu.roll(flags, stride, 0)
            valid = t >= stride
        prior_v = jnp.where(valid, prior_v, 0.0)
        prior_f = jnp.where(valid, prior_f, 1.0)
        v = v + flags * step(prior_v, pw_ref[level])
        flags = flags * prior_f
    return v


def _carry(g_ref, len_ref, pw_ref, scen, backward, seg):
    width = pw_ref.shape[1]
    g = g_ref[...][:, :width]
    rows = g.shape[0]
    devices = rows // scen
    r = lax.broadcasted_iota(jnp.int32, (rows, width), 0)
    flags = jnp.broadcast_to(_seg_flags(len_ref, devices, seg, not backward), (rows, width))
    step = functools.partial(_mm, nt=not backward)
    for level in range((devices - 1).bit_length()):
        stride = scen * 2**level
        if backward:
            prior_g = pltpu.roll(g, rows - stride, 0)
            prior_f = pltpu.roll(flags, rows - stride, 0)
            valid = r < rows - stride
        else:
            prior_g = pltpu.roll(g, stride, 0)
            prior_f = pltpu.roll(flags, stride, 0)
            valid = r >= stride
        prior_g = jnp.where(valid, prior_g, 0.0)
        prior_f = jnp.where(valid, prior_f, 1.0)
        g = g + flags * step(prior_g, pw_ref[level])
        flags = flags * prior_f
    me = lax.axis_index("tm")
    target = me + 1 if backward else me - 1
    pick = lax.broadcasted_iota(jnp.int32, (scen, rows), 1)
    want = lax.broadcasted_iota(jnp.int32, (scen, rows), 0) + target * scen
    return _dot((pick == want).astype(jnp.float32), g)


def _ends(v, seg, backward, out_rows):
    rows, width = v.shape
    scen = rows // seg
    ends = v.reshape(scen, seg, width)[:, 0 if backward else seg - 1, :]
    return jnp.broadcast_to(ends[None], (out_rows,) + ends.shape)


def _cut_rows(len_ref, shape, seg, start):
    rows, width = shape
    scen, episodes = len_ref.shape
    r = lax.broadcasted_iota(jnp.int32, (rows, 1), 0)
    which = r // seg
    pos = lax.axis_index("tm") * seg + r % seg
    hit = jnp.zeros((rows, 1), jnp.bool_)
    for s in range(scen):
        edge = 0
        for k in range(episodes):
            first = edge
            edge = edge + len_ref[s, k]
            hit = hit | ((which == s) & (pos == first if start else pos + 1 == edge))
    return jnp.broadcast_to(hit.astype(jnp.float32), shape)


def _seg_flags(len_ref, devices, seg, start):
    scen, episodes = len_ref.shape
    rows = devices * scen
    r = lax.broadcasted_iota(jnp.int32, (rows, 1), 0)
    which = r % scen
    lo = r // scen * seg
    hit = jnp.zeros((rows, 1), jnp.bool_)
    for s in range(scen):
        edge = 0
        for k in range(episodes):
            first = edge
            edge = edge + len_ref[s, k]
            if start:
                inside = (first >= lo) & (first < lo + seg)
            else:
                inside = (edge > lo) & (edge <= lo + seg)
            hit = hit | ((which == s) & inside)
    return 1.0 - hit.astype(jnp.float32)


def _vmem(count):
    return [pl.BlockSpec(memory_space=pltpu.VMEM)] * count


def _call(kernel, outs, *args, smem=()):
    specs = _vmem(len(args))
    for index in smem:
        specs[index] = pl.BlockSpec(memory_space=pltpu.SMEM)
    return pl.pallas_call(
        kernel,
        out_shape=outs,
        in_specs=specs,
        out_specs=tuple(_vmem(len(outs))),
    )(*args)


def k_first(seg, decay_ref, coupling_ref, links_ref, cw_ref, ref_ref, len_ref, phi_ref, plo_ref,
            top_ref, w1_ref, e1_ref):
    pwb_ref = _Pair(phi_ref, plo_ref)
    power = _build(decay_ref, coupling_ref, links_ref)
    phi_ref[0], plo_ref[0] = _split(power)
    for level in range(1, pwb_ref.shape[0]):
        power = _dot(power, power)
        phi_ref[level], plo_ref[level] = _split(power)
    top_ref[...] = power
    cut = _cut_rows(len_ref, cw_ref.shape, seg, False)
    w1 = cw_ref[...] * ref_ref[...]
    w1_ref[...] = w1
    e1_ref[...] = _ends(_scan(w1, cut, pwb_ref, seg, True), seg, True, e1_ref.shape[0])


def k_device_powers(top_ref, dhi_ref, dlo_ref):
    power = top_ref[...]
    for level in range(dhi_ref.shape[0]):
        power = _dot(power, power)
        dhi_ref[level], dlo_ref[level] = _split(power)


def k_states_in(seg, w1_ref, len_ref, c1_ref, xi_ref, gain_ref, imap_ref, phi_ref, plo_ref, dhi_ref, dlo_ref, d2_ref,
                e2_ref):
    pwb_ref = pwf_ref = _Pair(phi_ref, plo_ref)
    shape = w1_ref.shape
    cut_e = _cut_rows(len_ref, shape, seg, False)
    cut_s = _cut_rows(len_ref, shape, seg, True)
    c1 = _carry(c1_ref, len_ref, _Pair(dhi_ref, dlo_ref), w1_ref.shape[0] // seg, True, seg)
    vt = _scan(w1_ref[...], cut_e, pwb_ref, seg, True, c1)
    controls = _mm(vt, gain_ref[...], nt=True)
    forcing = -_mm(controls, imap_ref[...], nt=True)
    rows, width = shape
    scen = rows // seg
    image = _mm(xi_ref[...], pwf_ref[0], nt=True)
    init = jnp.broadcast_to(image[:, None, :], (scen, seg, width)).reshape(rows, width)
    d2 = forcing + cut_s * init
    d2_ref[...] = d2
    e2_ref[...] = _ends(_scan(d2, cut_s, pwf_ref, seg, False), seg, False, e2_ref.shape[0])


def k_adjoint_in(seg, scale, d2_ref, len_ref, c2_ref, cw_ref, ref_ref, phi_ref, plo_ref, dhi_ref, dlo_ref, x_ref,
                 w3_ref, e3_ref):
    pwb_ref = pwf_ref = _Pair(phi_ref, plo_ref)
    shape = d2_ref.shape
    rows, width = shape
    scen = rows // seg
    cut_s = _cut_rows(len_ref, shape, seg, True)
    cut_e = _cut_rows(len_ref, shape, seg, False)
    c2 = _carry(c2_ref, len_ref, _Pair(dhi_ref, dlo_ref), scen, False, seg)
    states = _scan(d2_ref[...], cut_s, pwf_ref, seg, False, c2)
    x_ref[...] = states
    offset = states - ref_ref[...]
    cw = cw_ref[...]
    w3 = cw * offset
    w3_ref[...] = w3
    per_row = jnp.sum(w3 * offset, axis=1, keepdims=True)
    copies = e3_ref.shape[0]
    pick = lax.broadcasted_iota(jnp.int32, (scen, rows), 1) // seg
    want = lax.broadcasted_iota(jnp.int32, (scen, rows), 0)
    sel = (pick == want).astype(jnp.float32)
    per_scen = _dot(sel, jnp.broadcast_to(per_row, (rows, 128))) * scale
    e3_ref[:, :, width:] = jnp.broadcast_to(per_scen[None], (copies, scen, 128))
    e3_ref[:, :, :width] = _ends(_scan(w3, cut_e, pwb_ref, seg, True), seg, True, copies)


def k_value_adjoint_in(seg, w3_ref, len_ref, c3_ref, imap_ref, gain_ref, phi_ref, plo_ref, dhi_ref, dlo_ref, s4_ref,
                       e4_ref):
    pwb_ref = pwf_ref = _Pair(phi_ref, plo_ref)
    shape = w3_ref.shape
    cut_e = _cut_rows(len_ref, shape, seg, False)
    cut_s = _cut_rows(len_ref, shape, seg, True)
    c3 = _carry(c3_ref, len_ref, _Pair(dhi_ref, dlo_ref), w3_ref.shape[0] // seg, True, seg)
    adjoint = _scan(w3_ref[...], cut_e, pwb_ref, seg, True, c3)
    pulled = _mm(adjoint, imap_ref[...])
    source = -_mm(pulled, gain_ref[...])
    s4_ref[...] = source
    e4_ref[...] = _ends(_scan(source, cut_s, pwf_ref, seg, False), seg, False, e4_ref.shape[0])


def k_last(seg, s4_ref, len_ref, c4_ref, x_ref, ref_ref, phi_ref, plo_ref, dhi_ref, dlo_ref, g_ref):
    pwf_ref = _Pair(phi_ref, plo_ref)
    shape = s4_ref.shape
    cut_s = _cut_rows(len_ref, shape, seg, True)
    c4 = _carry(c4_ref, len_ref, _Pair(dhi_ref, dlo_ref), s4_ref.shape[0] // seg, False, seg)
    va = _scan(s4_ref[...], cut_s, pwf_ref, seg, False, c4)
    ref = ref_ref[...]
    offset = x_ref[...] - ref
    g_ref[...] = 0.5 * offset * offset + ref * va


def per_device(ref_traj, cost_weights, x_init, decay, coupling, links, input_map, ff_gain, lengths):
    scen_count, seg_steps, width = ref_traj.shape
    rows = scen_count * seg_steps
    devices = lax.axis_size("tm")
    device = lax.axis_index("tm")
    total = seg_steps * devices
    local_levels = seg_steps.bit_length() - 1
    device_levels = (devices - 1).bit_length()
    power_count = local_levels + max(device_levels, 1)
    cw = cost_weights.reshape(rows, width)
    ref = ref_traj.reshape(rows, width)
    f32 = jnp.float32
    full = jax.ShapeDtypeStruct((rows, width), f32)
    ends = jax.ShapeDtypeStruct((devices, scen_count, width), f32)
    seg = seg_steps

    def gather(copies):
        every = lax.all_to_all(copies, "tm", 0, 0, tiled=True)
        return every.reshape(devices * scen_count, copies.shape[2])

    powers = jax.ShapeDtypeStruct((local_levels, width, width), jnp.bfloat16)
    square = jax.ShapeDtypeStruct((width, width), f32)
    phi, plo, top, w1, e1 = _call(
        functools.partial(k_first, seg), (powers, powers, square, full, ends),
        decay.reshape(1, width), coupling, links.T, cw, ref, lengths, smem=(2, 5))
    dev = jax.ShapeDtypeStruct((max(device_levels, 1), width, width), jnp.bfloat16)
    dhi, dlo = _call(k_device_powers, (dev, dev), top)
    d2, e2 = _call(
        functools.partial(k_states_in, seg), (full, ends),
        w1, lengths, gather(e1), x_init, ff_gain, input_map, phi, plo, dhi, dlo, smem=(1,))
    packed = jax.ShapeDtypeStruct((devices, scen_count, width + 128), f32)
    states, w3, e3 = _call(
        functools.partial(k_adjoint_in, seg, 0.5 / total), (full, full, packed),
        d2, lengths, gather(e2), cw, ref, phi, plo, dhi, dlo, smem=(1,))
    g3 = gather(e3)
    cost = jnp.sum(g3[:, width].reshape(devices, scen_count), axis=0)
    s4, e4 = _call(
        functools.partial(k_value_adjoint_in, seg), (full, ends),
        w3, lengths, g3, input_map, ff_gain, phi, plo, dhi, dlo, smem=(1,))
    (grad,) = _call(
        functools.partial(k_last, seg), (full,), s4, lengths, gather(e4), states, ref, phi, plo, dhi, dlo,
        smem=(1,))
    shape3 = (scen_count, seg_steps, width)
    return (states.reshape(shape3), grad.reshape(shape3), cost)


def solution(mesh):
    placed = (
        P("groups", "tm", None),
        P("groups", "tm", None),
        P("groups", None),
        P(),
        P(),
        P(),
        P(),
        P(),
        P("groups", None),
    )
    return jax.shard_map(
        per_device,
        mesh=mesh,
        in_specs=placed,
        out_specs=(P("groups", "tm", None), P("groups", "tm", None), P("groups")),
        check_vma=False,
    )
```

```python
import functools

import jax
import jax.numpy as jnp
from jax import lax
from jax.experimental import pallas as pl
from jax.experimental.pallas import tpu as pltpu
from jax.sharding import PartitionSpec as P

HIGH = lax.Precision.HIGHEST


def build_dynamics(decay, coupling, links):
    size = decay.shape[0]
    width = coupling.shape[1]
    lanes = jnp.arange(size, dtype=jnp.int32)
    offsets = jnp.arange(width, dtype=jnp.int32)
    row_hot = (lanes[None, :, None] == links[:, 0:1, None] * width + offsets[None, None, :]).astype(
        jnp.float32
    )
    col_hot = (lanes[None, :, None] == links[:, 1:2, None] * width + offsets[None, None, :]).astype(
        jnp.float32
    )
    placed = jnp.einsum(
        "lia,lab,ljb->ij", row_hot, coupling, col_hot, precision=lax.Precision.HIGHEST
    )
    return jnp.diag(decay) + placed


def row_times(values, matrix):
    width = values.shape[-1]
    flat = jnp.dot(values.reshape(-1, width), matrix, precision=lax.Precision.HIGHEST)
    return flat.reshape(values.shape)


def _dot(a, b):
    return jnp.dot(a, b, precision=HIGH, preferred_element_type=jnp.float32)


def _dot_nt(a, b):
    return lax.dot_general(
        a, b, (((1,), (1,)), ((), ())), precision=HIGH, preferred_element_type=jnp.float32)


def _split(x):
    hi = x.astype(jnp.bfloat16)
    lo = (x - hi.astype(jnp.float32)).astype(jnp.bfloat16)
    return hi, lo


class _Pair:
    def __init__(self, hi, lo):
        self.hi, self.lo = hi, lo
        self.shape = hi.shape

    def __getitem__(self, index):
        return (self.hi[index], self.lo[index])


def _mm(a, b, nt=False):
    dims = (((1,), (1 if nt else 0,)), ((), ()))
    a_hi, a_lo = _split(a)
    b_hi, b_lo = b if isinstance(b, tuple) else _split(b)
    part = functools.partial(lax.dot_general, dimension_numbers=dims,
                             preferred_element_type=jnp.float32)
    rows = a.shape[0]
    both = part(jnp.concatenate([a_hi, a_lo], axis=0), b_hi)
    return both[:rows] + both[rows:] + part(a_hi, b_lo)


def _build(decay_ref, coupling_ref, links_ref):
    size = decay_ref.shape[1]
    width = coupling_ref.shape[1]
    r = lax.broadcasted_iota(jnp.int32, (size, size), 0)
    c = lax.broadcasted_iota(jnp.int32, (size, size), 1)
    power = jnp.where(r == c, jnp.broadcast_to(decay_ref[...], (size, size)), 0.0)
    lane = lax.broadcasted_iota(jnp.int32, (size, width), 0)
    off = lax.broadcasted_iota(jnp.int32, (size, width), 1)
    for link in range(coupling_ref.shape[0]):
        row_hot = (lane == links_ref[0, link] * width + off).astype(jnp.float32)
        col_hot = (lane == links_ref[1, link] * width + off).astype(jnp.float32)
        power = power + _dot_nt(_dot(row_hot, coupling_ref[link]), col_hot)
    return power


def _scan(v, cut, pw_ref, seg, backward, carry=None, levels=None):
    rows, width = v.shape
    scen = rows // seg
    t = lax.broadcasted_iota(jnp.int32, (rows, width), 0) % seg
    flags = 1.0 - cut
    if levels is None:
        levels = seg.bit_length() - 1
    step = functools.partial(_mm, nt=not backward)
    if carry is not None:
        pushed = step(carry, pw_ref[0])
        pushed = jnp.broadcast_to(pushed[:, None, :], (scen, seg, width)).reshape(rows, width)
        first = t == (seg - 1 if backward else 0)
        v = v + jnp.where(first, flags * pushed, 0.0)
    for level in range(levels):
        stride = 2**level
        if backward:
            prior_v = pltpu.roll(v, rows - stride, 0)
            prior_f = pltpu.roll(flags, rows - stride, 0)
            valid = t < seg - stride
        else:
            prior_v = pltpu.roll(v, stride, 0)
            prior_f = pltpu.roll(flags, stride, 0)
            valid = t >= stride
        prior_v = jnp.where(valid, prior_v, 0.0)
        prior_f = jnp.where(valid, prior_f, 1.0)
        v = v + flags * step(prior_v, pw_ref[level])
        flags = flags * prior_f
    return v


def _carry(g_ref, len_ref, pw_ref, scen, backward, seg):
    width = pw_ref.shape[1]
    g = g_ref[...][:, :width]
    rows = g.shape[0]
    devices = rows // scen
    r = lax.broadcasted_iota(jnp.int32, (rows, width), 0)
    flags = jnp.broadcast_to(_seg_flags(len_ref, devices, seg, not backward), (rows, width))
    step = functools.partial(_mm, nt=not backward)
    for level in range((devices - 1).bit_length()):
        stride = scen * 2**level
        if backward:
            prior_g = pltpu.roll(g, rows - stride, 0)
            prior_f = pltpu.roll(flags, rows - stride, 0)
            valid = r < rows - stride
        else:
            prior_g = pltpu.roll(g, stride, 0)
            prior_f = pltpu.roll(flags, stride, 0)
            valid = r >= stride
        prior_g = jnp.where(valid, prior_g, 0.0)
        prior_f = jnp.where(valid, prior_f, 1.0)
        g = g + flags * step(prior_g, pw_ref[level])
        flags = flags * prior_f
    me = lax.axis_index("tm")
    target = me + 1 if backward else me - 1
    pick = lax.broadcasted_iota(jnp.int32, (scen, rows), 1)
    want = lax.broadcasted_iota(jnp.int32, (scen, rows), 0) + target * scen
    return _dot((pick == want).astype(jnp.float32), g)


def _ends(v, seg, backward, out_rows):
    rows, width = v.shape
    scen = rows // seg
    ends = v.reshape(scen, seg, width)[:, 0 if backward else seg - 1, :]
    return jnp.broadcast_to(ends[None], (out_rows,) + ends.shape)


def _cut_rows(len_ref, shape, seg, start):
    rows, width = shape
    scen, episodes = len_ref.shape
    r = lax.broadcasted_iota(jnp.int32, (rows, 1), 0)
    which = r // seg
    pos = lax.axis_index("tm") * seg + r % seg
    hit = jnp.zeros((rows, 1), jnp.bool_)
    for s in range(scen):
        edge = 0
        for k in range(episodes):
            first = edge
            edge = edge + len_ref[s, k]
            hit = hit | ((which == s) & (pos == first if start else pos + 1 == edge))
    return jnp.broadcast_to(hit.astype(jnp.float32), shape)


def _seg_flags(len_ref, devices, seg, start):
    scen, episodes = len_ref.shape
    rows = devices * scen
    r = lax.broadcasted_iota(jnp.int32, (rows, 1), 0)
    which = r % scen
    lo = r // scen * seg
    hit = jnp.zeros((rows, 1), jnp.bool_)
    for s in range(scen):
        edge = 0
        for k in range(episodes):
            first = edge
            edge = edge + len_ref[s, k]
            if start:
                inside = (first >= lo) & (first < lo + seg)
            else:
                inside = (edge > lo) & (edge <= lo + seg)
            hit = hit | ((which == s) & inside)
    return 1.0 - hit.astype(jnp.float32)


def _vmem(count):
    return [pl.BlockSpec(memory_space=pltpu.VMEM)] * count


def _call(kernel, outs, *args, smem=()):
    specs = _vmem(len(args))
    for index in smem:
        specs[index] = pl.BlockSpec(memory_space=pltpu.SMEM)
    return pl.pallas_call(
        kernel,
        out_shape=outs,
        in_specs=specs,
        out_specs=tuple(_vmem(len(outs))),
    )(*args)


def k_first(seg, decay_ref, coupling_ref, links_ref, cw_ref, ref_ref, len_ref, phi_ref, plo_ref,
            top_ref, w1_ref, e1_ref):
    pwb_ref = _Pair(phi_ref, plo_ref)
    power = _build(decay_ref, coupling_ref, links_ref)
    phi_ref[0], plo_ref[0] = _split(power)
    for level in range(1, pwb_ref.shape[0]):
        power = _dot(power, power)
        phi_ref[level], plo_ref[level] = _split(power)
    top_ref[...] = power
    cut = _cut_rows(len_ref, cw_ref.shape, seg, False)
    w1 = cw_ref[...] * ref_ref[...]
    w1_ref[...] = w1
    e1_ref[...] = _ends(_scan(w1, cut, pwb_ref, seg, True), seg, True, e1_ref.shape[0])


def k_device_powers(top_ref, dhi_ref, dlo_ref):
    power = top_ref[...]
    for level in range(dhi_ref.shape[0]):
        power = _dot(power, power)
        dhi_ref[level], dlo_ref[level] = _split(power)


def k_states_in(seg, w1_ref, len_ref, c1_ref, xi_ref, gain_ref, imap_ref, phi_ref, plo_ref, dhi_ref, dlo_ref, d2_ref,
                e2_ref):
    pwb_ref = pwf_ref = _Pair(phi_ref, plo_ref)
    shape = w1_ref.shape
    cut_e = _cut_rows(len_ref, shape, seg, False)
    cut_s = _cut_rows(len_ref, shape, seg, True)
    c1 = _carry(c1_ref, len_ref, _Pair(dhi_ref, dlo_ref), w1_ref.shape[0] // seg, True, seg)
    vt = _scan(w1_ref[...], cut_e, pwb_ref, seg, True, c1)
    controls = _mm(vt, gain_ref[...], nt=True)
    forcing = -_mm(controls, imap_ref[...], nt=True)
    rows, width = shape
    scen = rows // seg
    image = _mm(xi_ref[...], pwf_ref[0], nt=True)
    init = jnp.broadcast_to(image[:, None, :], (scen, seg, width)).reshape(rows, width)
    d2 = forcing + cut_s * init
    d2_ref[...] = d2
    e2_ref[...] = _ends(_scan(d2, cut_s, pwf_ref, seg, False), seg, False, e2_ref.shape[0])


def k_adjoint_in(seg, scale, d2_ref, len_ref, c2_ref, cw_ref, ref_ref, phi_ref, plo_ref, dhi_ref, dlo_ref, x_ref,
                 w3_ref, e3_ref):
    pwb_ref = pwf_ref = _Pair(phi_ref, plo_ref)
    shape = d2_ref.shape
    rows, width = shape
    scen = rows // seg
    cut_s = _cut_rows(len_ref, shape, seg, True)
    cut_e = _cut_rows(len_ref, shape, seg, False)
    c2 = _carry(c2_ref, len_ref, _Pair(dhi_ref, dlo_ref), scen, False, seg)
    states = _scan(d2_ref[...], cut_s, pwf_ref, seg, False, c2)
    x_ref[...] = states
    offset = states - ref_ref[...]
    cw = cw_ref[...]
    w3 = cw * offset
    w3_ref[...] = w3
    per_row = jnp.sum(w3 * offset, axis=1, keepdims=True)
    copies = e3_ref.shape[0]
    per_scen = jnp.sum(per_row.reshape(scen, seg, 1), axis=1) * scale
    per_scen = jnp.broadcast_to(per_scen, (scen, 128))
    e3_ref[:, :, width:] = jnp.broadcast_to(per_scen[None], (copies, scen, 128))
    e3_ref[:, :, :width] = _ends(_scan(w3, cut_e, pwb_ref, seg, True), seg, True, copies)


def k_value_adjoint_in(seg, w3_ref, len_ref, c3_ref, imap_ref, gain_ref, phi_ref, plo_ref, dhi_ref, dlo_ref, s4_ref,
                       e4_ref):
    pwb_ref = pwf_ref = _Pair(phi_ref, plo_ref)
    shape = w3_ref.shape
    cut_e = _cut_rows(len_ref, shape, seg, False)
    cut_s = _cut_rows(len_ref, shape, seg, True)
    c3 = _carry(c3_ref, len_ref, _Pair(dhi_ref, dlo_ref), w3_ref.shape[0] // seg, True, seg)
    adjoint = _scan(w3_ref[...], cut_e, pwb_ref, seg, True, c3)
    pulled = _mm(adjoint, imap_ref[...])
    source = -_mm(pulled, gain_ref[...])
    s4_ref[...] = source
    e4_ref[...] = _ends(_scan(source, cut_s, pwf_ref, seg, False), seg, False, e4_ref.shape[0])


def k_last(seg, s4_ref, len_ref, c4_ref, x_ref, ref_ref, phi_ref, plo_ref, dhi_ref, dlo_ref, g_ref):
    pwf_ref = _Pair(phi_ref, plo_ref)
    shape = s4_ref.shape
    cut_s = _cut_rows(len_ref, shape, seg, True)
    c4 = _carry(c4_ref, len_ref, _Pair(dhi_ref, dlo_ref), s4_ref.shape[0] // seg, False, seg)
    va = _scan(s4_ref[...], cut_s, pwf_ref, seg, False, c4)
    ref = ref_ref[...]
    offset = x_ref[...] - ref
    g_ref[...] = 0.5 * offset * offset + ref * va


def per_device(ref_traj, cost_weights, x_init, decay, coupling, links, input_map, ff_gain, lengths):
    scen_count, seg_steps, width = ref_traj.shape
    rows = scen_count * seg_steps
    devices = lax.axis_size("tm")
    device = lax.axis_index("tm")
    total = seg_steps * devices
    local_levels = seg_steps.bit_length() - 1
    device_levels = (devices - 1).bit_length()
    power_count = local_levels + max(device_levels, 1)
    cw = cost_weights.reshape(rows, width)
    ref = ref_traj.reshape(rows, width)
    f32 = jnp.float32
    full = jax.ShapeDtypeStruct((rows, width), f32)
    ends = jax.ShapeDtypeStruct((devices, scen_count, width), f32)
    seg = seg_steps

    def gather(copies):
        every = lax.all_to_all(copies, "tm", 0, 0, tiled=True)
        return every.reshape(devices * scen_count, copies.shape[2])

    powers = jax.ShapeDtypeStruct((local_levels, width, width), jnp.bfloat16)
    square = jax.ShapeDtypeStruct((width, width), f32)
    phi, plo, top, w1, e1 = _call(
        functools.partial(k_first, seg), (powers, powers, square, full, ends),
        decay.reshape(1, width), coupling, links.T, cw, ref, lengths, smem=(2, 5))
    dev = jax.ShapeDtypeStruct((max(device_levels, 1), width, width), jnp.bfloat16)
    dhi, dlo = _call(k_device_powers, (dev, dev), top)
    d2, e2 = _call(
        functools.partial(k_states_in, seg), (full, ends),
        w1, lengths, gather(e1), x_init, ff_gain, input_map, phi, plo, dhi, dlo, smem=(1,))
    packed = jax.ShapeDtypeStruct((devices, scen_count, width + 128), f32)
    states, w3, e3 = _call(
        functools.partial(k_adjoint_in, seg, 0.5 / total), (full, full, packed),
        d2, lengths, gather(e2), cw, ref, phi, plo, dhi, dlo, smem=(1,))
    g3 = gather(e3)
    cost = jnp.sum(g3[:, width].reshape(devices, scen_count), axis=0)
    s4, e4 = _call(
        functools.partial(k_value_adjoint_in, seg), (full, ends),
        w3, lengths, g3, input_map, ff_gain, phi, plo, dhi, dlo, smem=(1,))
    (grad,) = _call(
        functools.partial(k_last, seg), (full,), s4, lengths, gather(e4), states, ref, phi, plo, dhi, dlo,
        smem=(1,))
    shape3 = (scen_count, seg_steps, width)
    return (states.reshape(shape3), grad.reshape(shape3), cost)


def solution(mesh):
    placed = (
        P("groups", "tm", None),
        P("groups", "tm", None),
        P("groups", None),
        P(),
        P(),
        P(),
        P(),
        P(),
        P("groups", None),
    )
    return jax.shard_map(
        per_device,
        mesh=mesh,
        in_specs=placed,
        out_specs=(P("groups", "tm", None), P("groups", "tm", None), P("groups")),
        check_vma=False,
    )
```

```python
import functools

import jax
import jax.numpy as jnp
from jax import lax
from jax.experimental import pallas as pl
from jax.experimental.pallas import tpu as pltpu
from jax.sharding import PartitionSpec as P

HIGH = lax.Precision.HIGHEST


def build_dynamics(decay, coupling, links):
    size = decay.shape[0]
    width = coupling.shape[1]
    lanes = jnp.arange(size, dtype=jnp.int32)
    offsets = jnp.arange(width, dtype=jnp.int32)
    row_hot = (lanes[None, :, None] == links[:, 0:1, None] * width + offsets[None, None, :]).astype(
        jnp.float32
    )
    col_hot = (lanes[None, :, None] == links[:, 1:2, None] * width + offsets[None, None, :]).astype(
        jnp.float32
    )
    placed = jnp.einsum(
        "lia,lab,ljb->ij", row_hot, coupling, col_hot, precision=lax.Precision.HIGHEST
    )
    return jnp.diag(decay) + placed


def row_times(values, matrix):
    width = values.shape[-1]
    flat = jnp.dot(values.reshape(-1, width), matrix, precision=lax.Precision.HIGHEST)
    return flat.reshape(values.shape)


def _dot(a, b):
    return jnp.dot(a, b, precision=HIGH, preferred_element_type=jnp.float32)


def _dot_nt(a, b):
    return lax.dot_general(
        a, b, (((1,), (1,)), ((), ())), precision=HIGH, preferred_element_type=jnp.float32)


def _split(x):
    hi = x.astype(jnp.bfloat16)
    lo = (x - hi.astype(jnp.float32)).astype(jnp.bfloat16)
    return hi, lo


class _Pair:
    def __init__(self, hi, lo):
        self.hi, self.lo = hi, lo
        self.shape = hi.shape

    def __getitem__(self, index):
        return (self.hi[index], self.lo[index])


def _mm(a, b, nt=False):
    dims = (((1,), (1 if nt else 0,)), ((), ()))
    a_hi, a_lo = _split(a)
    b_hi, b_lo = b if isinstance(b, tuple) else _split(b)
    part = functools.partial(lax.dot_general, dimension_numbers=dims,
                             preferred_element_type=jnp.float32)
    rows = a.shape[0]
    both = part(jnp.concatenate([a_hi, a_lo], axis=0), b_hi)
    return both[:rows] + both[rows:] + part(a_hi, b_lo)


def _build(decay_ref, coupling_ref, links_ref):
    size = decay_ref.shape[1]
    width = coupling_ref.shape[1]
    r = lax.broadcasted_iota(jnp.int32, (size, size), 0)
    c = lax.broadcasted_iota(jnp.int32, (size, size), 1)
    power = jnp.where(r == c, jnp.broadcast_to(decay_ref[...], (size, size)), 0.0)
    lane = lax.broadcasted_iota(jnp.int32, (size, width), 0)
    off = lax.broadcasted_iota(jnp.int32, (size, width), 1)
    for link in range(coupling_ref.shape[0]):
        row_hot = (lane == links_ref[0, link] * width + off).astype(jnp.float32)
        col_hot = (lane == links_ref[1, link] * width + off).astype(jnp.float32)
        power = power + _dot_nt(_dot(row_hot, coupling_ref[link]), col_hot)
    return power


def _scan(v, cut, pw_ref, seg, backward, carry=None, levels=None):
    rows, width = v.shape
    scen = rows // seg
    t = lax.broadcasted_iota(jnp.int32, (rows, width), 0) % seg
    flags = 1.0 - cut
    if levels is None:
        levels = seg.bit_length() - 1
    step = functools.partial(_mm, nt=not backward)
    if carry is not None:
        pushed = step(carry, pw_ref[0])
        pushed = jnp.broadcast_to(pushed[:, None, :], (scen, seg, width)).reshape(rows, width)
        first = t == (seg - 1 if backward else 0)
        v = v + jnp.where(first, flags * pushed, 0.0)
    for level in range(levels):
        stride = 2**level
        if backward:
            prior_v = pltpu.roll(v, rows - stride, 0)
            prior_f = pltpu.roll(flags, rows - stride, 0)
            valid = t < seg - stride
        else:
            prior_v = pltpu.roll(v, stride, 0)
            prior_f = pltpu.roll(flags, stride, 0)
            valid = t >= stride
        prior_v = jnp.where(valid, prior_v, 0.0)
        prior_f = jnp.where(valid, prior_f, 1.0)
        v = v + flags * step(prior_v, pw_ref[level])
        flags = flags * prior_f
    return v


def _carry(g_ref, len_ref, pw_ref, scen, backward, seg):
    width = pw_ref.shape[1]
    g = g_ref[...][:, :width]
    rows = g.shape[0]
    devices = rows // scen
    r = lax.broadcasted_iota(jnp.int32, (rows, width), 0)
    flags = jnp.broadcast_to(_seg_flags(len_ref, devices, seg, not backward), (rows, width))
    step = functools.partial(_mm, nt=not backward)
    for level in range((devices - 1).bit_length()):
        stride = scen * 2**level
        if backward:
            prior_g = pltpu.roll(g, rows - stride, 0)
            prior_f = pltpu.roll(flags, rows - stride, 0)
            valid = r < rows - stride
        else:
            prior_g = pltpu.roll(g, stride, 0)
            prior_f = pltpu.roll(flags, stride, 0)
            valid = r >= stride
        prior_g = jnp.where(valid, prior_g, 0.0)
        prior_f = jnp.where(valid, prior_f, 1.0)
        g = g + flags * step(prior_g, pw_ref[level])
        flags = flags * prior_f
    me = lax.axis_index("tm")
    target = me + 1 if backward else me - 1
    if devices & (devices - 1):
        pick = lax.broadcasted_iota(jnp.int32, (scen, rows), 1)
        want = lax.broadcasted_iota(jnp.int32, (scen, rows), 0) + target * scen
        return _dot((pick == want).astype(jnp.float32), g)
    picked = jnp.where(r // scen == target, g, 0.0)
    for level in range((devices - 1).bit_length()):
        picked = picked + pltpu.roll(picked, scen * 2**level, 0)
    return picked[:scen]


def _ends(v, seg, backward, out_rows):
    rows, width = v.shape
    scen = rows // seg
    ends = v.reshape(scen, seg, width)[:, 0 if backward else seg - 1, :]
    return jnp.broadcast_to(ends[None], (out_rows,) + ends.shape)


def _cut_rows(len_ref, shape, seg, start):
    rows, width = shape
    scen, episodes = len_ref.shape
    r = lax.broadcasted_iota(jnp.int32, (rows, 1), 0)
    which = r // seg
    pos = lax.axis_index("tm") * seg + r % seg
    hit = jnp.zeros((rows, 1), jnp.bool_)
    for s in range(scen):
        edge = 0
        for k in range(episodes):
            first = edge
            edge = edge + len_ref[s, k]
            hit = hit | ((which == s) & (pos == first if start else pos + 1 == edge))
    return jnp.broadcast_to(hit.astype(jnp.float32), shape)


def _seg_flags(len_ref, devices, seg, start):
    scen, episodes = len_ref.shape
    rows = devices * scen
    r = lax.broadcasted_iota(jnp.int32, (rows, 1), 0)
    which = r % scen
    lo = r // scen * seg
    hit = jnp.zeros((rows, 1), jnp.bool_)
    for s in range(scen):
        edge = 0
        for k in range(episodes):
            first = edge
            edge = edge + len_ref[s, k]
            if start:
                inside = (first >= lo) & (first < lo + seg)
            else:
                inside = (edge > lo) & (edge <= lo + seg)
            hit = hit | ((which == s) & inside)
    return 1.0 - hit.astype(jnp.float32)


def _vmem(count):
    return [pl.BlockSpec(memory_space=pltpu.VMEM)] * count


def _call(kernel, outs, *args, smem=()):
    specs = _vmem(len(args))
    for index in smem:
        specs[index] = pl.BlockSpec(memory_space=pltpu.SMEM)
    return pl.pallas_call(
        kernel,
        out_shape=outs,
        in_specs=specs,
        out_specs=tuple(_vmem(len(outs))),
    )(*args)


def k_first(seg, decay_ref, coupling_ref, links_ref, cw_ref, ref_ref, len_ref, phi_ref, plo_ref,
            top_ref, w1_ref, e1_ref):
    pwb_ref = _Pair(phi_ref, plo_ref)
    power = _build(decay_ref, coupling_ref, links_ref)
    phi_ref[0], plo_ref[0] = _split(power)
    for level in range(1, pwb_ref.shape[0]):
        power = _dot(power, power)
        phi_ref[level], plo_ref[level] = _split(power)
    top_ref[...] = power
    cut = _cut_rows(len_ref, cw_ref.shape, seg, False)
    w1 = cw_ref[...] * ref_ref[...]
    w1_ref[...] = w1
    e1_ref[...] = _ends(_scan(w1, cut, pwb_ref, seg, True), seg, True, e1_ref.shape[0])


def k_device_powers(top_ref, dhi_ref, dlo_ref):
    power = top_ref[...]
    for level in range(dhi_ref.shape[0]):
        power = _dot(power, power)
        dhi_ref[level], dlo_ref[level] = _split(power)


def k_states_in(seg, w1_ref, len_ref, c1_ref, xi_ref, gain_ref, imap_ref, phi_ref, plo_ref, dhi_ref, dlo_ref, d2_ref,
                e2_ref):
    pwb_ref = pwf_ref = _Pair(phi_ref, plo_ref)
    shape = w1_ref.shape
    cut_e = _cut_rows(len_ref, shape, seg, False)
    cut_s = _cut_rows(len_ref, shape, seg, True)
    c1 = _carry(c1_ref, len_ref, _Pair(dhi_ref, dlo_ref), w1_ref.shape[0] // seg, True, seg)
    vt = _scan(w1_ref[...], cut_e, pwb_ref, seg, True, c1)
    controls = _mm(vt, gain_ref[...], nt=True)
    forcing = -_mm(controls, imap_ref[...], nt=True)
    rows, width = shape
    scen = rows // seg
    image = _mm(xi_ref[...], pwf_ref[0], nt=True)
    init = jnp.broadcast_to(image[:, None, :], (scen, seg, width)).reshape(rows, width)
    d2 = forcing + cut_s * init
    d2_ref[...] = d2
    e2_ref[...] = _ends(_scan(d2, cut_s, pwf_ref, seg, False), seg, False, e2_ref.shape[0])


def k_adjoint_in(seg, scale, d2_ref, len_ref, c2_ref, cw_ref, ref_ref, phi_ref, plo_ref, dhi_ref, dlo_ref, x_ref,
                 w3_ref, e3_ref):
    pwb_ref = pwf_ref = _Pair(phi_ref, plo_ref)
    shape = d2_ref.shape
    rows, width = shape
    scen = rows // seg
    cut_s = _cut_rows(len_ref, shape, seg, True)
    cut_e = _cut_rows(len_ref, shape, seg, False)
    c2 = _carry(c2_ref, len_ref, _Pair(dhi_ref, dlo_ref), scen, False, seg)
    states = _scan(d2_ref[...], cut_s, pwf_ref, seg, False, c2)
    x_ref[...] = states
    offset = states - ref_ref[...]
    cw = cw_ref[...]
    w3 = cw * offset
    w3_ref[...] = w3
    per_row = jnp.sum(w3 * offset, axis=1, keepdims=True)
    copies = e3_ref.shape[0]
    per_scen = jnp.sum(per_row.reshape(scen, seg, 1), axis=1) * scale
    per_scen = jnp.broadcast_to(per_scen, (scen, 128))
    e3_ref[:, :, width:] = jnp.broadcast_to(per_scen[None], (copies, scen, 128))
    e3_ref[:, :, :width] = _ends(_scan(w3, cut_e, pwb_ref, seg, True), seg, True, copies)


def k_value_adjoint_in(seg, w3_ref, len_ref, c3_ref, imap_ref, gain_ref, phi_ref, plo_ref, dhi_ref, dlo_ref, s4_ref,
                       e4_ref):
    pwb_ref = pwf_ref = _Pair(phi_ref, plo_ref)
    shape = w3_ref.shape
    cut_e = _cut_rows(len_ref, shape, seg, False)
    cut_s = _cut_rows(len_ref, shape, seg, True)
    c3 = _carry(c3_ref, len_ref, _Pair(dhi_ref, dlo_ref), w3_ref.shape[0] // seg, True, seg)
    adjoint = _scan(w3_ref[...], cut_e, pwb_ref, seg, True, c3)
    pulled = _mm(adjoint, imap_ref[...])
    source = -_mm(pulled, gain_ref[...])
    s4_ref[...] = source
    e4_ref[...] = _ends(_scan(source, cut_s, pwf_ref, seg, False), seg, False, e4_ref.shape[0])


def k_last(seg, s4_ref, len_ref, c4_ref, x_ref, ref_ref, phi_ref, plo_ref, dhi_ref, dlo_ref, g_ref):
    pwf_ref = _Pair(phi_ref, plo_ref)
    shape = s4_ref.shape
    cut_s = _cut_rows(len_ref, shape, seg, True)
    c4 = _carry(c4_ref, len_ref, _Pair(dhi_ref, dlo_ref), s4_ref.shape[0] // seg, False, seg)
    va = _scan(s4_ref[...], cut_s, pwf_ref, seg, False, c4)
    ref = ref_ref[...]
    offset = x_ref[...] - ref
    g_ref[...] = 0.5 * offset * offset + ref * va


def per_device(ref_traj, cost_weights, x_init, decay, coupling, links, input_map, ff_gain, lengths):
    scen_count, seg_steps, width = ref_traj.shape
    rows = scen_count * seg_steps
    devices = lax.axis_size("tm")
    device = lax.axis_index("tm")
    total = seg_steps * devices
    local_levels = seg_steps.bit_length() - 1
    device_levels = (devices - 1).bit_length()
    power_count = local_levels + max(device_levels, 1)
    cw = cost_weights.reshape(rows, width)
    ref = ref_traj.reshape(rows, width)
    f32 = jnp.float32
    full = jax.ShapeDtypeStruct((rows, width), f32)
    ends = jax.ShapeDtypeStruct((devices, scen_count, width), f32)
    seg = seg_steps

    def gather(copies):
        every = lax.all_to_all(copies, "tm", 0, 0, tiled=True)
        return every.reshape(devices * scen_count, copies.shape[2])

    powers = jax.ShapeDtypeStruct((local_levels, width, width), jnp.bfloat16)
    square = jax.ShapeDtypeStruct((width, width), f32)
    phi, plo, top, w1, e1 = _call(
        functools.partial(k_first, seg), (powers, powers, square, full, ends),
        decay.reshape(1, width), coupling, links.T, cw, ref, lengths, smem=(2, 5))
    dev = jax.ShapeDtypeStruct((max(device_levels, 1), width, width), jnp.bfloat16)
    dhi, dlo = _call(k_device_powers, (dev, dev), top)
    d2, e2 = _call(
        functools.partial(k_states_in, seg), (full, ends),
        w1, lengths, gather(e1), x_init, ff_gain, input_map, phi, plo, dhi, dlo, smem=(1,))
    packed = jax.ShapeDtypeStruct((devices, scen_count, width + 128), f32)
    states, w3, e3 = _call(
        functools.partial(k_adjoint_in, seg, 0.5 / total), (full, full, packed),
        d2, lengths, gather(e2), cw, ref, phi, plo, dhi, dlo, smem=(1,))
    g3 = gather(e3)
    cost = jnp.sum(g3[:, width].reshape(devices, scen_count), axis=0)
    s4, e4 = _call(
        functools.partial(k_value_adjoint_in, seg), (full, ends),
        w3, lengths, g3, input_map, ff_gain, phi, plo, dhi, dlo, smem=(1,))
    (grad,) = _call(
        functools.partial(k_last, seg), (full,), s4, lengths, gather(e4), states, ref, phi, plo, dhi, dlo,
        smem=(1,))
    shape3 = (scen_count, seg_steps, width)
    return (states.reshape(shape3), grad.reshape(shape3), cost)


def solution(mesh):
    placed = (
        P("groups", "tm", None),
        P("groups", "tm", None),
        P("groups", None),
        P(),
        P(),
        P(),
        P(),
        P(),
        P("groups", None),
    )
    return jax.shard_map(
        per_device,
        mesh=mesh,
        in_specs=placed,
        out_specs=(P("groups", "tm", None), P("groups", "tm", None), P("groups")),
        check_vma=False,
    )
```

```python
import functools

import jax
import jax.numpy as jnp
from jax import lax
from jax.experimental import pallas as pl
from jax.experimental.pallas import tpu as pltpu
from jax.sharding import PartitionSpec as P

HIGH = lax.Precision.HIGHEST


def build_dynamics(decay, coupling, links):
    size = decay.shape[0]
    width = coupling.shape[1]
    lanes = jnp.arange(size, dtype=jnp.int32)
    offsets = jnp.arange(width, dtype=jnp.int32)
    row_hot = (lanes[None, :, None] == links[:, 0:1, None] * width + offsets[None, None, :]).astype(
        jnp.float32
    )
    col_hot = (lanes[None, :, None] == links[:, 1:2, None] * width + offsets[None, None, :]).astype(
        jnp.float32
    )
    placed = jnp.einsum(
        "lia,lab,ljb->ij", row_hot, coupling, col_hot, precision=lax.Precision.HIGHEST
    )
    return jnp.diag(decay) + placed


def row_times(values, matrix):
    width = values.shape[-1]
    flat = jnp.dot(values.reshape(-1, width), matrix, precision=lax.Precision.HIGHEST)
    return flat.reshape(values.shape)


def _dot(a, b):
    return jnp.dot(a, b, precision=HIGH, preferred_element_type=jnp.float32)


def _dot_nt(a, b):
    return lax.dot_general(
        a, b, (((1,), (1,)), ((), ())), precision=HIGH, preferred_element_type=jnp.float32)


def _split(x):
    hi = x.astype(jnp.bfloat16)
    lo = (x - hi.astype(jnp.float32)).astype(jnp.bfloat16)
    return hi, lo


class _Pair:
    def __init__(self, hi, lo):
        self.hi, self.lo = hi, lo
        self.shape = hi.shape

    def __getitem__(self, index):
        return (self.hi[index], self.lo[index])


def _mm(a, b, nt=False):
    dims = (((1,), (1 if nt else 0,)), ((), ()))
    a_hi, a_lo = _split(a)
    b_hi, b_lo = b if isinstance(b, tuple) else _split(b)
    part = functools.partial(lax.dot_general, dimension_numbers=dims,
                             preferred_element_type=jnp.float32)
    rows = a.shape[0]
    both = part(jnp.concatenate([a_hi, a_lo], axis=0), b_hi)
    return both[:rows] + both[rows:] + part(a_hi, b_lo)


def _build(decay_ref, coupling_ref, links_ref):
    size = decay_ref.shape[1]
    width = coupling_ref.shape[1]
    r = lax.broadcasted_iota(jnp.int32, (size, size), 0)
    c = lax.broadcasted_iota(jnp.int32, (size, size), 1)
    power = jnp.where(r == c, jnp.broadcast_to(decay_ref[...], (size, size)), 0.0)
    lane = lax.broadcasted_iota(jnp.int32, (size, width), 0)
    off = lax.broadcasted_iota(jnp.int32, (size, width), 1)
    for link in range(coupling_ref.shape[0]):
        row_hot = (lane == links_ref[0, link] * width + off).astype(jnp.float32)
        col_hot = (lane == links_ref[1, link] * width + off).astype(jnp.float32)
        power = power + _dot_nt(_dot(row_hot, coupling_ref[link]), col_hot)
    return power


def _scan(v, cut, pw_ref, seg, backward, carry=None, levels=None):
    rows, width = v.shape
    scen = rows // seg
    t = lax.broadcasted_iota(jnp.int32, (rows, width), 0) % seg
    flags = 1.0 - cut
    if levels is None:
        levels = seg.bit_length() - 1
    step = functools.partial(_mm, nt=not backward)
    if carry is not None:
        pushed = step(carry, pw_ref[0])
        pushed = jnp.broadcast_to(pushed[:, None, :], (scen, seg, width)).reshape(rows, width)
        first = t == (seg - 1 if backward else 0)
        v = v + jnp.where(first, flags * pushed, 0.0)
    for level in range(levels):
        stride = 2**level
        if backward:
            prior_v = pltpu.roll(v, rows - stride, 0)
            prior_f = pltpu.roll(flags, rows - stride, 0)
            valid = t < seg - stride
        else:
            prior_v = pltpu.roll(v, stride, 0)
            prior_f = pltpu.roll(flags, stride, 0)
            valid = t >= stride
        prior_v = jnp.where(valid, prior_v, 0.0)
        prior_f = jnp.where(valid, prior_f, 1.0)
        v = v + flags * step(prior_v, pw_ref[level])
        flags = flags * prior_f
    return v


def _block(scen):
    return -(-scen // 8) * 8


def _carry(g_ref, len_ref, pw_ref, real, backward, seg):
    width = pw_ref.shape[1]
    g = g_ref[...][:, :width]
    rows = g.shape[0]
    scen = _block(real)
    devices = rows // scen
    r = lax.broadcasted_iota(jnp.int32, (rows, width), 0)
    flags = jnp.broadcast_to(_seg_flags(len_ref, devices, seg, not backward), (rows, width))
    step = functools.partial(_mm, nt=not backward)
    for level in range((devices - 1).bit_length()):
        stride = scen * 2**level
        if backward:
            prior_g = pltpu.roll(g, rows - stride, 0)
            prior_f = pltpu.roll(flags, rows - stride, 0)
            valid = r < rows - stride
        else:
            prior_g = pltpu.roll(g, stride, 0)
            prior_f = pltpu.roll(flags, stride, 0)
            valid = r >= stride
        prior_g = jnp.where(valid, prior_g, 0.0)
        prior_f = jnp.where(valid, prior_f, 1.0)
        g = g + flags * step(prior_g, pw_ref[level])
        flags = flags * prior_f
    me = lax.axis_index("tm")
    target = me + 1 if backward else me - 1
    if devices & (devices - 1):
        pick = lax.broadcasted_iota(jnp.int32, (scen, rows), 1)
        want = lax.broadcasted_iota(jnp.int32, (scen, rows), 0) + target * scen
        return _dot((pick == want).astype(jnp.float32), g)[:real]
    picked = jnp.where(r // scen == target, g, 0.0)
    for level in range((devices - 1).bit_length()):
        picked = picked + pltpu.roll(picked, scen * 2**level, 0)
    return picked[:real]


def _ends(v, seg, backward, out_rows):
    rows, width = v.shape
    scen = rows // seg
    ends = _pad(v.reshape(scen, seg, width)[:, 0 if backward else seg - 1, :])
    return jnp.broadcast_to(ends[None], (out_rows,) + ends.shape)


def _pad(rows_in):
    extra = _block(rows_in.shape[0]) - rows_in.shape[0]
    if not extra:
        return rows_in
    return jnp.concatenate([rows_in, jnp.zeros((extra, rows_in.shape[1]), rows_in.dtype)], axis=0)


def _cut_rows(len_ref, shape, seg, start):
    rows, width = shape
    scen, episodes = len_ref.shape
    r = lax.broadcasted_iota(jnp.int32, (rows, 1), 0)
    which = r // seg
    pos = lax.axis_index("tm") * seg + r % seg
    hit = jnp.zeros((rows, 1), jnp.bool_)
    for s in range(scen):
        edge = 0
        for k in range(episodes):
            first = edge
            edge = edge + len_ref[s, k]
            hit = hit | ((which == s) & (pos == first if start else pos + 1 == edge))
    return jnp.broadcast_to(hit.astype(jnp.float32), shape)


def _seg_flags(len_ref, devices, seg, start):
    scen, episodes = len_ref.shape
    block = _block(scen)
    rows = devices * block
    r = lax.broadcasted_iota(jnp.int32, (rows, 1), 0)
    which = r % block
    lo = r // block * seg
    hit = jnp.zeros((rows, 1), jnp.bool_)
    for s in range(scen):
        edge = 0
        for k in range(episodes):
            first = edge
            edge = edge + len_ref[s, k]
            if start:
                inside = (first >= lo) & (first < lo + seg)
            else:
                inside = (edge > lo) & (edge <= lo + seg)
            hit = hit | ((which == s) & inside)
    return 1.0 - hit.astype(jnp.float32)


def _vmem(count):
    return [pl.BlockSpec(memory_space=pltpu.VMEM)] * count


def _call(kernel, outs, *args, smem=()):
    specs = _vmem(len(args))
    for index in smem:
        specs[index] = pl.BlockSpec(memory_space=pltpu.SMEM)
    return pl.pallas_call(
        kernel,
        out_shape=outs,
        in_specs=specs,
        out_specs=tuple(_vmem(len(outs))),
    )(*args)


def k_first(seg, decay_ref, coupling_ref, links_ref, cw_ref, ref_ref, len_ref, phi_ref, plo_ref,
            top_ref, w1_ref, e1_ref):
    pwb_ref = _Pair(phi_ref, plo_ref)
    power = _build(decay_ref, coupling_ref, links_ref)
    phi_ref[0], plo_ref[0] = _split(power)
    for level in range(1, pwb_ref.shape[0]):
        power = _dot(power, power)
        phi_ref[level], plo_ref[level] = _split(power)
    top_ref[...] = power
    cut = _cut_rows(len_ref, cw_ref.shape, seg, False)
    w1 = cw_ref[...] * ref_ref[...]
    w1_ref[...] = w1
    e1_ref[...] = _ends(_scan(w1, cut, pwb_ref, seg, True), seg, True, e1_ref.shape[0])


def k_device_powers(top_ref, dhi_ref, dlo_ref):
    power = top_ref[...]
    for level in range(dhi_ref.shape[0]):
        power = _dot(power, power)
        dhi_ref[level], dlo_ref[level] = _split(power)


def k_states_in(seg, w1_ref, len_ref, c1_ref, xi_ref, gain_ref, imap_ref, phi_ref, plo_ref, dhi_ref, dlo_ref, d2_ref,
                e2_ref):
    pwb_ref = pwf_ref = _Pair(phi_ref, plo_ref)
    shape = w1_ref.shape
    cut_e = _cut_rows(len_ref, shape, seg, False)
    cut_s = _cut_rows(len_ref, shape, seg, True)
    c1 = _carry(c1_ref, len_ref, _Pair(dhi_ref, dlo_ref), w1_ref.shape[0] // seg, True, seg)
    vt = _scan(w1_ref[...], cut_e, pwb_ref, seg, True, c1)
    controls = _mm(vt, gain_ref[...], nt=True)
    forcing = -_mm(controls, imap_ref[...], nt=True)
    rows, width = shape
    scen = rows // seg
    image = _mm(xi_ref[...], pwf_ref[0], nt=True)
    init = jnp.broadcast_to(image[:, None, :], (scen, seg, width)).reshape(rows, width)
    d2 = forcing + cut_s * init
    d2_ref[...] = d2
    e2_ref[...] = _ends(_scan(d2, cut_s, pwf_ref, seg, False), seg, False, e2_ref.shape[0])


def k_adjoint_in(seg, scale, d2_ref, len_ref, c2_ref, cw_ref, ref_ref, phi_ref, plo_ref, dhi_ref, dlo_ref, x_ref,
                 w3_ref, e3_ref):
    pwb_ref = pwf_ref = _Pair(phi_ref, plo_ref)
    shape = d2_ref.shape
    rows, width = shape
    scen = rows // seg
    cut_s = _cut_rows(len_ref, shape, seg, True)
    cut_e = _cut_rows(len_ref, shape, seg, False)
    c2 = _carry(c2_ref, len_ref, _Pair(dhi_ref, dlo_ref), scen, False, seg)
    states = _scan(d2_ref[...], cut_s, pwf_ref, seg, False, c2)
    x_ref[...] = states
    offset = states - ref_ref[...]
    cw = cw_ref[...]
    w3 = cw * offset
    w3_ref[...] = w3
    per_row = jnp.sum(w3 * offset, axis=1, keepdims=True)
    copies = e3_ref.shape[0]
    per_scen = jnp.sum(per_row.reshape(scen, seg, 1), axis=1) * scale
    per_scen = _pad(jnp.broadcast_to(per_scen, (scen, 128)))
    e3_ref[:, :, width:] = jnp.broadcast_to(per_scen[None], (copies,) + per_scen.shape)
    e3_ref[:, :, :width] = _ends(_scan(w3, cut_e, pwb_ref, seg, True), seg, True, copies)


def k_value_adjoint_in(seg, w3_ref, len_ref, c3_ref, imap_ref, gain_ref, phi_ref, plo_ref, dhi_ref, dlo_ref, s4_ref,
                       e4_ref):
    pwb_ref = pwf_ref = _Pair(phi_ref, plo_ref)
    shape = w3_ref.shape
    cut_e = _cut_rows(len_ref, shape, seg, False)
    cut_s = _cut_rows(len_ref, shape, seg, True)
    c3 = _carry(c3_ref, len_ref, _Pair(dhi_ref, dlo_ref), w3_ref.shape[0] // seg, True, seg)
    adjoint = _scan(w3_ref[...], cut_e, pwb_ref, seg, True, c3)
    pulled = _mm(adjoint, imap_ref[...])
    source = -_mm(pulled, gain_ref[...])
    s4_ref[...] = source
    e4_ref[...] = _ends(_scan(source, cut_s, pwf_ref, seg, False), seg, False, e4_ref.shape[0])


def k_last(seg, s4_ref, len_ref, c4_ref, x_ref, ref_ref, phi_ref, plo_ref, dhi_ref, dlo_ref, g_ref):
    pwf_ref = _Pair(phi_ref, plo_ref)
    shape = s4_ref.shape
    cut_s = _cut_rows(len_ref, shape, seg, True)
    c4 = _carry(c4_ref, len_ref, _Pair(dhi_ref, dlo_ref), s4_ref.shape[0] // seg, False, seg)
    va = _scan(s4_ref[...], cut_s, pwf_ref, seg, False, c4)
    ref = ref_ref[...]
    offset = x_ref[...] - ref
    g_ref[...] = 0.5 * offset * offset + ref * va


def per_device(ref_traj, cost_weights, x_init, decay, coupling, links, input_map, ff_gain, lengths):
    scen_count, seg_steps, width = ref_traj.shape
    rows = scen_count * seg_steps
    devices = lax.axis_size("tm")
    device = lax.axis_index("tm")
    total = seg_steps * devices
    local_levels = seg_steps.bit_length() - 1
    device_levels = (devices - 1).bit_length()
    power_count = local_levels + max(device_levels, 1)
    cw = cost_weights.reshape(rows, width)
    ref = ref_traj.reshape(rows, width)
    f32 = jnp.float32
    full = jax.ShapeDtypeStruct((rows, width), f32)
    block = _block(scen_count)
    ends = jax.ShapeDtypeStruct((devices, block, width), f32)
    seg = seg_steps

    def gather(copies):
        every = lax.all_to_all(copies, "tm", 0, 0, tiled=True)
        return every.reshape(devices * block, copies.shape[2])

    powers = jax.ShapeDtypeStruct((local_levels, width, width), jnp.bfloat16)
    square = jax.ShapeDtypeStruct((width, width), f32)
    phi, plo, top, w1, e1 = _call(
        functools.partial(k_first, seg), (powers, powers, square, full, ends),
        decay.reshape(1, width), coupling, links.T, cw, ref, lengths, smem=(2, 5))
    dev = jax.ShapeDtypeStruct((max(device_levels, 1), width, width), jnp.bfloat16)
    dhi, dlo = _call(k_device_powers, (dev, dev), top)
    d2, e2 = _call(
        functools.partial(k_states_in, seg), (full, ends),
        w1, lengths, gather(e1), x_init, ff_gain, input_map, phi, plo, dhi, dlo, smem=(1,))
    packed = jax.ShapeDtypeStruct((devices, block, width + 128), f32)
    states, w3, e3 = _call(
        functools.partial(k_adjoint_in, seg, 0.5 / total), (full, full, packed),
        d2, lengths, gather(e2), cw, ref, phi, plo, dhi, dlo, smem=(1,))
    g3 = gather(e3)
    cost = jnp.sum(g3[:, width].reshape(devices, block)[:, :scen_count], axis=0)
    s4, e4 = _call(
        functools.partial(k_value_adjoint_in, seg), (full, ends),
        w3, lengths, g3, input_map, ff_gain, phi, plo, dhi, dlo, smem=(1,))
    (grad,) = _call(
        functools.partial(k_last, seg), (full,), s4, lengths, gather(e4), states, ref, phi, plo, dhi, dlo,
        smem=(1,))
    shape3 = (scen_count, seg_steps, width)
    return (states.reshape(shape3), grad.reshape(shape3), cost)


def solution(mesh):
    placed = (
        P("groups", "tm", None),
        P("groups", "tm", None),
        P("groups", None),
        P(),
        P(),
        P(),
        P(),
        P(),
        P("groups", None),
    )
    return jax.shard_map(
        per_device,
        mesh=mesh,
        in_specs=placed,
        out_specs=(P("groups", "tm", None), P("groups", "tm", None), P("groups")),
        check_vma=False,
    )
```
